32 devices in a mesh: groups: 2 (over y), patch: 4 (over z), chan: 2 (over x), col: 2 (over core).
Axes of the slice: x: 2, y: 2, z: 4, core: 2. Of those that a mesh axis runs over, the one named last changes fastest.
Arguments:
- features: bfloat16 [1280, 48, 256], P('chan', ('groups', 'patch'), 'col'), parts along dimension 1, may hold values from -16 to 16
- cache_codes: bfloat16 [1280, 16, 256], P('chan', ('groups', 'patch'), 'col'), parts along dimension 1, may hold values from -127 to 127
- cache_scale: float32 [16, 256], P(('groups', 'patch'), 'col'), parts along dimension 0, may hold values from 0.001 to 0.01
- step_index: int32 [2], P('groups'), parts along dimension 0, may hold values from 0 to 999
- gn1_gain: float32 [1280], P('chan'), may hold values from 0.1 to 1.9
- gn1_shift: float32 [1280], P('chan'), may hold values from -3 to 3
- conv1_weight: bfloat16 [3, 3, 1280, 1280], P(None, None, 'patch', 'chan'), may hold values from -0.0546875 to 0.0546875
- conv1_bias: float32 [1280], P('chan'), may hold values from -3 to 3
- temb_weight: bfloat16 [1280, 1280], P(None, 'chan'), may hold values from -0.15625 to 0.15625
- gn2_gain: float32 [1280], P('chan'), may hold values from 0.1 to 1.9
- gn2_shift: float32 [1280], P('chan'), may hold values from -3 to 3
- conv2_weight: bfloat16 [3, 3, 1280, 1280], P(None, None, 'patch', 'chan'), may hold values from -0.0546875 to 0.0546875
- conv2_bias: float32 [1280], P('chan'), may hold values from -3 to 3
Outputs:
- block_out: bfloat16 [1280, 48, 256], P('chan', ('groups', 'patch'), 'col'), parts along dimension 1
The draws below stay inside these ranges and needn't reach their ends.
There are 2 independent parts, one for each index of `groups`. The reference program is written for one: setup_inputs(seed, part) draws one part's arguments, and reference() takes and returns one part's arrays. A program takes and returns all parts, laid end to end along the dimension named above; an argument that names none is the same for every part. Nothing has to cross between parts.
All inputs are finite; a program needn't handle non-finite values.
Results may differ from the reference program's by a relative error of at most 0.009.
Values may be sent and summed in bfloat16 or wider, within the bound.
No kernel may reach another device: no remote copies, remote signals or barrier semaphores. Data moves between devices by JAX's collectives and lax.ppermute only.
A program may use at most 128 MiB of HBM per device.

```python
import math
import jax
import jax.numpy as jnp
from jax import lax

C = 1280
GROUPS = 32
TEMB = 1280
ROWS_DEV = 6
ROWS = 24
COLS = 256
N_PATCH = 4
N_CHAN = 2


def draw_features(key, part):
    subkeys = jax.random.split(key, 4)
    noise_val = jnp.clip(jax.random.normal(subkeys[0], (C, ROWS, COLS), jnp.float32), -3.0, 3.0)
    chan_scale = jnp.exp(jax.random.uniform(subkeys[1], (C, 1, 1), jnp.float32, 0.0, math.log(4.0)))
    ramp = jnp.arange(ROWS).astype(jnp.float32) / max(ROWS - 1, 1)
    row_rough = jnp.exp(jax.random.uniform(subkeys[2], (ROWS,), jnp.float32, 0.0, math.log(2.0)))
    row_scale = (jnp.exp(math.log(3.0) * ramp) * row_rough).reshape(1, ROWS, 1)
    col_scale = jnp.exp(jax.random.uniform(subkeys[3], (1, 1, COLS), jnp.float32, 0.0, math.log(2.0)))
    values = 0.1 * noise_val * chan_scale * row_scale * col_scale
    return values.astype(jnp.bfloat16)


def block_levels(rng, shape, cuts, smallest, top_value):
    level, own = 1.0, jax.random.fold_in(rng, 6)
    for dim, shards_of in cuts:
        heights = jnp.exp(jax.random.uniform(jax.random.fold_in(own, dim), (shards_of,), jnp.float32, smallest / len(cuts), top_value / len(cuts)))
        level = level * jnp.repeat(heights, shape[dim] // shards_of).reshape([-1 if axis == dim else 1 for axis in range(len(shape))])
    return level


def noise(stream_key, dims, spread, most, pieces=(), dtype=jnp.bfloat16):
    level = block_levels(stream_key, dims, pieces, -0.22, 0.18) if pieces else 1.0
    drawn = jax.random.normal(stream_key, dims, jnp.float32) * spread * level
    return jnp.minimum(jnp.maximum(drawn, -most), most).astype(dtype)


def setup_inputs(seed: int = 0, part: int = 0) -> dict:
    arg_keys = jax.random.split(jax.random.key(seed), 14)
    own_keys = jax.random.split(jax.random.fold_in(arg_keys[13], part), 14)
    return {
        "features": draw_features(jax.random.fold_in(jax.random.fold_in(arg_keys[13], part), 71), part),
        "cache_codes": jnp.clip(jax.random.uniform(own_keys[1], (C, 2 * N_PATCH, COLS), jnp.float32, -127.0, 127.0) * block_levels(own_keys[1], (C, 2 * N_PATCH, COLS), ((0, 2), (1, 4), (2, 2)), -0.4, 0.0), -127.0, 127.0).astype(jnp.bfloat16),
        "cache_scale": jnp.clip(jnp.exp(math.log(0.01) - 2.30258502 * jax.random.uniform(own_keys[2], (2 * N_PATCH, COLS), jnp.float32) ** block_levels(own_keys[2], (2 * N_PATCH, COLS), ((0, 4), (1, 2)), -0.2, 0.2)), 0.001, 0.01),
        "step_index": jax.random.randint(own_keys[3], (1,), 0, 1000).astype(jnp.int32),
        "gn1_gain": jnp.clip(1.0 + 0.18 * jax.random.normal(arg_keys[4], (C,), jnp.float32), 0.1, 1.9),
        "gn1_shift": noise(arg_keys[5], (C,), 0.5, 3.0, ((0, 2),), jnp.float32),
        "conv1_weight": noise(arg_keys[6], (3, 3, C, C), (9 * C) ** -0.5, 0.0546875, ((2, 4), (3, 2))),
        "conv1_bias": noise(arg_keys[7], (C,), 0.5, 3.0, ((0, 2),), jnp.float32),
        "temb_weight": noise(arg_keys[8], (TEMB, C), TEMB ** -0.5, 0.15625, ((1, 2),)),
        "gn2_gain": jnp.clip(1.0 + 0.18 * jax.random.normal(arg_keys[9], (C,), jnp.float32), 0.1, 1.9),
        "gn2_shift": noise(arg_keys[10], (C,), 0.5, 3.0, ((0, 2),), jnp.float32),
        "conv2_weight": noise(arg_keys[11], (3, 3, C, C), (9 * C) ** -0.5, 0.0546875, ((2, 4), (3, 2))),
        "conv2_bias": noise(arg_keys[12], (C,), 0.5, 3.0, ((0, 2),), jnp.float32),
    }


norm_epsilon = 1e-05

def group_moments(values):
    grouped = values.reshape(GROUPS, -1)
    total_cells = grouped.shape[1]
    group_mean = lax.optimization_barrier(jnp.sum(grouped, axis=1)) / total_cells
    group_var = lax.optimization_barrier(jnp.sum(grouped * grouped, axis=1)) / total_cells - group_mean * group_mean
    return (group_mean, lax.rsqrt(group_var + norm_epsilon))

def activate(values, group_mean, inv_std, gain_vec, shift_vec):
    width = C // GROUPS
    shape_tail = (C,) + (1,) * (values.ndim - 1)
    mean_chan = jnp.repeat(group_mean, width).reshape(shape_tail)
    inv_chan = jnp.repeat(inv_std, width).reshape(shape_tail)
    normed = (values - mean_chan) * inv_chan * gain_vec.reshape(shape_tail) + shift_vec.reshape(shape_tail)
    return jax.nn.silu(normed)

def conv_blocks(blocks, weights):
    block_count, _, height_pad, width_pad = blocks.shape
    height = height_pad - 2
    width = width_pad - 2
    in_block = C // N_CHAN
    total = jnp.zeros((block_count, C, height, width), jnp.float32)
    for chan_block in range(N_CHAN):
        partial_value = jnp.zeros((block_count, C, height, width), jnp.float32)
        for row_off in range(3):
            for col_off in range(3):
                piece = blocks[:, chan_block * in_block:(chan_block + 1) * in_block, row_off:row_off + height, col_off:col_off + width].astype(jnp.float32)
                kernel = weights[row_off, col_off, :, chan_block * in_block:(chan_block + 1) * in_block].astype(jnp.float32)
                partial_value = partial_value + jnp.einsum('oc,bchw->bohw', kernel, piece)
        rounded = lax.optimization_barrier(partial_value.astype(jnp.bfloat16))
        total = total + rounded.astype(jnp.float32)
    return total

def time_bias(step_index, temb_weight):
    half_width = TEMB // 2
    freqs = jnp.exp(-math.log(10000.0) * jnp.arange(half_width).astype(jnp.float32) / half_width)
    angles = step_index[0].astype(jnp.float32) * freqs
    embed = jnp.concatenate([jnp.cos(angles), jnp.sin(angles)])
    gated = jax.nn.silu(embed).astype(jnp.bfloat16)
    return jnp.dot(gated[None, :], temb_weight, preferred_element_type=jnp.float32)[0]

def reference(features, cache_codes, cache_scale, step_index, gn1_gain, gn1_shift, conv1_weight, conv1_bias, temb_weight, gn2_gain, gn2_shift, conv2_weight, conv2_bias):
    feat32 = features.astype(jnp.float32)
    mean_one, inv_one = group_moments(feat32)
    own_act = activate(feat32, mean_one, inv_one, gn1_gain, gn1_shift)
    stale = cache_codes.astype(jnp.float32) * cache_scale[None, :, :]
    rim_act = activate(stale, mean_one, inv_one, gn1_gain, gn1_shift)
    patch_ids = jnp.arange(N_PATCH)
    upper_keep = (patch_ids > 0).astype(jnp.float32)
    lower_keep = (patch_ids < N_PATCH - 1).astype(jnp.float32)
    upper_rim = rim_act[:, 0::2, :] * upper_keep[None, :, None]
    lower_rim = rim_act[:, 1::2, :] * lower_keep[None, :, None]
    own_rows = own_act.reshape(C, N_PATCH, ROWS_DEV, COLS)
    stacked = jnp.concatenate([upper_rim[:, :, None, :], own_rows, lower_rim[:, :, None, :]], axis=2)
    blocks_one = jnp.transpose(stacked, (1, 0, 2, 3)).astype(jnp.bfloat16)
    blocks_one = jnp.pad(blocks_one, ((0, 0), (0, 0), (0, 0), (1, 1)))
    sum_one = conv_blocks(blocks_one, conv1_weight)
    sum_one = jnp.transpose(sum_one, (1, 0, 2, 3)).reshape(C, ROWS, COLS)
    temb_bias = time_bias(step_index, temb_weight)
    hidden = (sum_one + conv1_bias[:, None, None] + temb_bias[:, None, None]).astype(jnp.bfloat16)
    hidden32 = hidden.astype(jnp.float32)
    mean_two, inv_two = group_moments(hidden32)
    act_two = activate(hidden32, mean_two, inv_two, gn2_gain, gn2_shift).astype(jnp.bfloat16)
    blocks_two = jnp.pad(act_two, ((0, 0), (1, 1), (1, 1)))[None]
    sum_two = conv_blocks(blocks_two, conv2_weight)[0]
    return (sum_two + conv2_bias[:, None, None] + feat32).astype(jnp.bfloat16)
```

```python
import math

import jax
import jax.numpy as jnp
from jax import lax
from jax.sharding import PartitionSpec as P

GROUPS = 32


norm_epsilon = 1e-05


def extended(value, sides, width):
    for axis, dim in sides:
        count, length = (lax.axis_size(axis), value.shape[dim])
        up = [(i, (i + 1) % count) for i in range(count - 1)]
        down = [(j, i) for i, j in up]
        last = lax.slice_in_dim(value, length - width, length, axis=dim)
        leading = lax.slice_in_dim(value, 0, width, axis=dim)
        before = lax.ppermute(last, axis, up)
        after = lax.ppermute(leading, axis, down)
        value = jnp.concatenate([before, value, after], axis=dim)
    return value


def group_moments(values, group_count, cell_total):
    grouped = values.reshape(group_count, -1)
    local_sums = (jnp.sum(grouped, axis=1), jnp.sum(grouped * grouped, axis=1))
    totals = lax.psum((local_sums[0], local_sums[1]), ("patch", "col"))
    group_mean = totals[0] / cell_total
    group_var = totals[1] / cell_total - group_mean * group_mean
    return (group_mean, lax.rsqrt(group_var + norm_epsilon))


def activate(values, group_mean, inv_std, gain_vec, shift_vec):
    channels = values.shape[0]
    width = channels // group_mean.shape[0]
    shape_tail = (channels,) + (1,) * (values.ndim - 1)
    mean_chan = jnp.repeat(group_mean, width).reshape(shape_tail)
    inv_chan = jnp.repeat(inv_std, width).reshape(shape_tail)
    normed = (values - mean_chan) * inv_chan * gain_vec.reshape(shape_tail) + shift_vec.reshape(
        shape_tail
    )
    return jax.nn.silu(normed)


def swap(value, axis):
    return lax.ppermute(value, axis, [(0, 1), (1, 0)])


def fetch_weights(weights):
    taps = weights.shape[0] * weights.shape[1]
    out_block, in_block = weights.shape[2], weights.shape[3]
    flat = weights.reshape(taps, out_block, in_block)
    share_y = lax.axis_size("groups") == 2
    n_y = 2 if share_y else 1
    n_c = lax.axis_size("col")
    y_id = lax.axis_index("groups") if share_y else 0
    c_id = lax.axis_index("col")
    piece = out_block // (n_y * n_c)
    own = y_id * n_c + c_id
    mine = lax.dynamic_slice_in_dim(flat, own * piece, piece, axis=1)
    got = lax.all_gather(mine, "patch", axis=0, tiled=False)
    slots, ids = [got], [own]
    if share_y:
        slots.append(swap(got, "groups"))
        ids.append((1 - y_id) * n_c + c_id)
    if n_c == 2:
        for i in range(len(slots)):
            slots.append(swap(slots[i], "col"))
            ids.append(ids[i] - c_id + (1 - c_id))
    return slots, ids


def conv_slots(padded, slots):
    in_chans, height_pad, width_pad = padded.shape
    height = height_pad - 2
    width = width_pad - 2
    windows = [
        [padded[:, a : a + height, b : b + width] for b in range(3)] for a in range(3)
    ]
    outs = []
    for got in slots:
        total = None
        for a in range(3):
            for b in range(3):
                term = jnp.einsum(
                    "poc,chw->pohw",
                    got[:, a * 3 + b],
                    windows[a][b],
                    preferred_element_type=jnp.float32,
                )
                total = term if total is None else total + term
        outs.append(total.astype(jnp.bfloat16))
    return jnp.stack(outs)


def reduce_chan(parts, ids):
    n_slots, blocks, piece, height, width = parts.shape
    n_k = lax.axis_size("chan")
    k = lax.axis_index("chan")
    per = blocks // n_k
    if n_k == 2:
        mine = lax.dynamic_slice_in_dim(parts, k * per, per, axis=1)
        other = lax.dynamic_slice_in_dim(parts, (1 - k) * per, per, axis=1)
        total = mine.astype(jnp.float32) + swap(other, "chan").astype(jnp.float32)
    else:
        split = parts.reshape(n_slots, n_k, per, piece, height, width)
        split = jnp.moveaxis(split, 1, 0)
        got = lax.all_to_all(split, "chan", 0, 0, tiled=False)
        total = jnp.sum(got.astype(jnp.float32), axis=0)
    where = jnp.zeros((n_slots,), jnp.int32)
    for slot, ident in enumerate(ids):
        where = where.at[ident].set(slot)
    ordered = jnp.take(total, where, axis=0)
    ordered = jnp.moveaxis(ordered, 0, 1)
    return ordered.reshape(per * n_slots * piece, height, width)


def time_bias(step_index, temb_weight):
    half_width = temb_weight.shape[0] // 2
    freqs = jnp.exp(-math.log(10000.0) * jnp.arange(half_width).astype(jnp.float32) / half_width)
    angles = step_index[0].astype(jnp.float32) * freqs
    embed = jnp.concatenate([jnp.cos(angles), jnp.sin(angles)])
    gated = jax.nn.silu(embed).astype(jnp.bfloat16)
    return jnp.dot(gated[None, :], temb_weight, preferred_element_type=jnp.float32)[0]


def on_device(
    features,
    cache_codes,
    cache_scale,
    step_index,
    gn1_gain,
    gn1_shift,
    conv1_weight,
    conv1_bias,
    temb_weight,
    gn2_gain,
    gn2_shift,
    conv2_weight,
    conv2_bias,
):
    channels, rows_here, cols_here = features.shape
    patches = lax.axis_size("patch")
    group_count = GROUPS // lax.axis_size("chan")
    cell_total = channels // group_count * rows_here * patches * cols_here * lax.axis_size("col")
    slots_one, ids_one = fetch_weights(conv1_weight)
    slots_two, ids_two = fetch_weights(conv2_weight)
    feat32 = features.astype(jnp.float32)
    mean_one, inv_one = group_moments(feat32, group_count, cell_total)
    own_act = activate(feat32, mean_one, inv_one, gn1_gain, gn1_shift)
    stale = cache_codes.astype(jnp.float32) * cache_scale[None, :, :]
    rim_act = activate(stale, mean_one, inv_one, gn1_gain, gn1_shift)
    where_patch = lax.axis_index("patch")
    upper_rim = rim_act[:, 0:1, :] * (where_patch > 0).astype(jnp.float32)
    lower_rim = rim_act[:, 1:2, :] * (where_patch < patches - 1).astype(jnp.float32)
    block_one = jnp.concatenate([upper_rim, own_act, lower_rim], axis=1).astype(jnp.bfloat16)
    padded_one = extended(block_one, (("col", 2),), 1)
    sum_one = reduce_chan(conv_slots(padded_one, slots_one), ids_one)
    temb_bias = time_bias(step_index, temb_weight)
    hidden = (sum_one + conv1_bias[:, None, None] + temb_bias[:, None, None]).astype(jnp.bfloat16)
    hidden32 = hidden.astype(jnp.float32)
    mean_two, inv_two = group_moments(hidden32, group_count, cell_total)
    act_two = activate(hidden32, mean_two, inv_two, gn2_gain, gn2_shift).astype(jnp.bfloat16)
    padded_two = extended(act_two, (("patch", 1), ("col", 2)), 1)
    sum_two = reduce_chan(conv_slots(padded_two, slots_two), ids_two)
    return (sum_two + conv2_bias[:, None, None] + feat32).astype(jnp.bfloat16)


def solution(mesh):
    return jax.shard_map(
        on_device,
        mesh=mesh,
        in_specs=(
            P("chan", ("groups", "patch"), "col"),
            P("chan", ("groups", "patch"), "col"),
            P(("groups", "patch"), "col"),
            P("groups"),
            P("chan"),
            P("chan"),
            P(None, None, "patch", "chan"),
            P("chan"),
            P(None, "chan"),
            P("chan"),
            P("chan"),
            P(None, None, "patch", "chan"),
            P("chan"),
        ),
        out_specs=P("chan", ("groups", "patch"), "col"),
        check_vma=False,
    )
```

```python
import math

import jax
import jax.numpy as jnp
from jax import lax
from jax.sharding import PartitionSpec as P

GROUPS = 32


norm_epsilon = 1e-05


def extended(value, sides, width):
    for axis, dim in sides:
        count, length = (lax.axis_size(axis), value.shape[dim])
        up = [(i, (i + 1) % count) for i in range(count - 1)]
        down = [(j, i) for i, j in up]
        last = lax.slice_in_dim(value, length - width, length, axis=dim)
        leading = lax.slice_in_dim(value, 0, width, axis=dim)
        before = lax.ppermute(last, axis, up)
        after = lax.ppermute(leading, axis, down)
        value = jnp.concatenate([before, value, after], axis=dim)
    return value


def group_moments(values, group_count, cell_total):
    grouped = values.reshape(group_count, -1)
    local_sums = (jnp.sum(grouped, axis=1), jnp.sum(grouped * grouped, axis=1))
    totals = lax.psum((local_sums[0], local_sums[1]), ("patch", "col"))
    group_mean = totals[0] / cell_total
    group_var = totals[1] / cell_total - group_mean * group_mean
    return (group_mean, lax.rsqrt(group_var + norm_epsilon))


def activate(values, group_mean, inv_std, gain_vec, shift_vec):
    channels = values.shape[0]
    width = channels // group_mean.shape[0]
    shape_tail = (channels,) + (1,) * (values.ndim - 1)
    mean_chan = jnp.repeat(group_mean, width).reshape(shape_tail)
    inv_chan = jnp.repeat(inv_std, width).reshape(shape_tail)
    normed = (values - mean_chan) * inv_chan * gain_vec.reshape(shape_tail) + shift_vec.reshape(
        shape_tail
    )
    return jax.nn.silu(normed)


def swap(value, axis):
    return lax.ppermute(value, axis, [(0, 1), (1, 0)])


def fetch_weights(weights):
    taps = weights.shape[0] * weights.shape[1]
    out_block, in_block = weights.shape[2], weights.shape[3]
    flat = weights.reshape(taps, out_block, in_block)
    share_y = lax.axis_size("groups") == 2
    n_y = 2 if share_y else 1
    n_c = lax.axis_size("col")
    y_id = lax.axis_index("groups") if share_y else 0
    c_id = lax.axis_index("col")
    piece = out_block // (n_y * n_c)
    own = y_id * n_c + c_id
    mine = lax.dynamic_slice_in_dim(flat, own * piece, piece, axis=1)
    got = lax.all_gather(mine, "patch", axis=0, tiled=False)
    slots, ids = [got], [own]
    if share_y:
        slots.append(swap(got, "groups"))
        ids.append((1 - y_id) * n_c + c_id)
    if n_c == 2:
        for i in range(len(slots)):
            slots.append(swap(slots[i], "col"))
            ids.append(ids[i] - c_id + (1 - c_id))
    return slots, ids


def conv_slots(padded, slots):
    in_chans, height_pad, width_pad = padded.shape
    height = height_pad - 2
    width = width_pad - 2
    windows = [
        [padded[:, a : a + height, b : b + width] for b in range(3)] for a in range(3)
    ]
    outs = []
    for got in slots:
        total = None
        for a in range(3):
            for b in range(3):
                term = jnp.einsum(
                    "poc,chw->pohw",
                    got[:, a * 3 + b],
                    windows[a][b],
                    preferred_element_type=jnp.float32,
                )
                total = term if total is None else total + term
        outs.append(total.astype(jnp.bfloat16))
    return jnp.stack(outs)


def reduce_chan(parts, ids):
    n_slots, blocks, piece, height, width = parts.shape
    n_k = lax.axis_size("chan")
    k = lax.axis_index("chan")
    per = blocks // n_k
    if n_k == 2:
        mine = lax.dynamic_slice_in_dim(parts, k * per, per, axis=1)
        other = lax.dynamic_slice_in_dim(parts, (1 - k) * per, per, axis=1)
        total = mine.astype(jnp.float32) + swap(other, "chan").astype(jnp.float32)
    else:
        split = parts.reshape(n_slots, n_k, per, piece, height, width)
        split = jnp.moveaxis(split, 1, 0)
        got = lax.all_to_all(split, "chan", 0, 0, tiled=False)
        total = jnp.sum(got.astype(jnp.float32), axis=0)
    where = jnp.zeros((n_slots,), jnp.int32)
    for slot, ident in enumerate(ids):
        where = where.at[ident].set(slot)
    ordered = jnp.take(total, where, axis=0)
    ordered = jnp.moveaxis(ordered, 0, 1)
    return ordered.reshape(per * n_slots * piece, height, width)


def line_weights(weights):
    taps = weights.shape[0] * weights.shape[1]
    out_block, in_block = weights.shape[2], weights.shape[3]
    flat = weights.reshape(taps, out_block, in_block)
    n_p, n_c = lax.axis_size("patch"), lax.axis_size("col")
    p, c, y = lax.axis_index("patch"), lax.axis_index("col"), lax.axis_index("groups")
    half = out_block // 2
    own_half = lax.dynamic_slice_in_dim(flat, y * half, half, axis=1)
    own_other = lax.dynamic_slice_in_dim(flat, (1 - y) * half, half, axis=1)
    per_core = n_p // n_c
    pieces = []
    for r in range(per_core):
        source = c * per_core + r
        mine = p == source
        held = jnp.where(mine, own_half, jnp.zeros_like(own_half))
        for t in range(1, n_p):
            up = [((s + t - 1) * n_c + cc, (s + t) * n_c + cc)
                  for cc in range(n_c) for s in [cc * per_core + r] if s + t < n_p]
            down = [((s - t + 1) * n_c + cc, (s - t) * n_c + cc)
                    for cc in range(n_c) for s in [cc * per_core + r] if s - t >= 0]
            got = held
            for pairs in (up, down):
                if pairs:
                    got = got + lax.ppermute(held, ("patch", "col"), pairs)
            held = got
        trade = [((g * n_p + z) * n_c + cc, ((1 - g) * n_p + z) * n_c + cc)
                 for g in range(2) for z in range(n_p) for cc in range(n_c)
                 if z != cc * per_core + r]
        other = lax.ppermute(held, ("groups", "patch", "col"), trade)
        other = jnp.where(mine, own_other, other)
        first = jnp.where(y == 0, held, other)
        second = jnp.where(y == 0, other, held)
        pieces += [first, second]
    return jnp.concatenate(pieces, axis=1)


def full_width(block):
    other = swap(block, "col")
    c = lax.axis_index("col")
    left = jnp.where(c == 0, block, other)
    right = jnp.where(c == 0, other, block)
    return jnp.pad(jnp.concatenate([left, right], axis=2), ((0, 0), (0, 0), (1, 1)))


def conv_full(padded, weight):
    height = padded.shape[1] - 2
    width = padded.shape[2] - 2
    total = None
    for a in range(3):
        for b in range(3):
            term = jnp.einsum(
                "oc,chw->ohw",
                weight[a * 3 + b],
                padded[:, a : a + height, b : b + width],
                preferred_element_type=jnp.float32,
            )
            total = term if total is None else total + term
    return total.astype(jnp.bfloat16)


def reduce_cores(part):
    k, c = lax.axis_index("chan"), lax.axis_index("col")
    width = part.shape[2] // 2
    piece = lambda j: lax.dynamic_slice_in_dim(part, j * width, width, axis=2)
    send_a = piece(jnp.where(k == c, 1 - c, c))
    got_a = lax.ppermute(send_a, ("chan", "col"), [(0, 1), (3, 2), (1, 3), (2, 0)])
    got_b = lax.ppermute(piece(1 - c), ("chan", "col"), [(1, 2), (2, 1)])
    first = jnp.where(k == c, piece(c), got_b)
    return first.astype(jnp.float32) + got_a.astype(jnp.float32)


def fast_path():
    return (
        lax.axis_size("chan") == 2
        and lax.axis_size("col") == 2
        and lax.axis_size("groups") == 2
        and lax.axis_size("patch") % 2 == 0
    )


def time_bias(step_index, temb_weight):
    half_width = temb_weight.shape[0] // 2
    freqs = jnp.exp(-math.log(10000.0) * jnp.arange(half_width).astype(jnp.float32) / half_width)
    angles = step_index[0].astype(jnp.float32) * freqs
    embed = jnp.concatenate([jnp.cos(angles), jnp.sin(angles)])
    gated = jax.nn.silu(embed).astype(jnp.bfloat16)
    return jnp.dot(gated[None, :], temb_weight, preferred_element_type=jnp.float32)[0]


def on_device(
    features,
    cache_codes,
    cache_scale,
    step_index,
    gn1_gain,
    gn1_shift,
    conv1_weight,
    conv1_bias,
    temb_weight,
    gn2_gain,
    gn2_shift,
    conv2_weight,
    conv2_bias,
):
    channels, rows_here, cols_here = features.shape
    patches = lax.axis_size("patch")
    group_count = GROUPS // lax.axis_size("chan")
    cell_total = channels // group_count * rows_here * patches * cols_here * lax.axis_size("col")
    fast = fast_path()
    if fast:
        weight_one = line_weights(conv1_weight)
        weight_two = line_weights(conv2_weight)
    else:
        slots_one, ids_one = fetch_weights(conv1_weight)
        slots_two, ids_two = fetch_weights(conv2_weight)
    feat32 = features.astype(jnp.float32)
    mean_one, inv_one = group_moments(feat32, group_count, cell_total)
    own_act = activate(feat32, mean_one, inv_one, gn1_gain, gn1_shift)
    stale = cache_codes.astype(jnp.float32) * cache_scale[None, :, :]
    rim_act = activate(stale, mean_one, inv_one, gn1_gain, gn1_shift)
    where_patch = lax.axis_index("patch")
    upper_rim = rim_act[:, 0:1, :] * (where_patch > 0).astype(jnp.float32)
    lower_rim = rim_act[:, 1:2, :] * (where_patch < patches - 1).astype(jnp.float32)
    block_one = jnp.concatenate([upper_rim, own_act, lower_rim], axis=1).astype(jnp.bfloat16)
    if fast:
        sum_one = reduce_cores(conv_full(full_width(block_one), weight_one))
    else:
        padded_one = extended(block_one, (("col", 2),), 1)
        sum_one = reduce_chan(conv_slots(padded_one, slots_one), ids_one)
    temb_bias = time_bias(step_index, temb_weight)
    hidden = (sum_one + conv1_bias[:, None, None] + temb_bias[:, None, None]).astype(jnp.bfloat16)
    hidden32 = hidden.astype(jnp.float32)
    mean_two, inv_two = group_moments(hidden32, group_count, cell_total)
    act_two = activate(hidden32, mean_two, inv_two, gn2_gain, gn2_shift).astype(jnp.bfloat16)
    if fast:
        rows_two = extended(act_two, (("patch", 1),), 1)
        sum_two = reduce_cores(conv_full(full_width(rows_two), weight_two))
    else:
        padded_two = extended(act_two, (("patch", 1), ("col", 2)), 1)
        sum_two = reduce_chan(conv_slots(padded_two, slots_two), ids_two)
    return (sum_two + conv2_bias[:, None, None] + feat32).astype(jnp.bfloat16)


def solution(mesh):
    return jax.shard_map(
        on_device,
        mesh=mesh,
        in_specs=(
            P("chan", ("groups", "patch"), "col"),
            P("chan", ("groups", "patch"), "col"),
            P(("groups", "patch"), "col"),
            P("groups"),
            P("chan"),
            P("chan"),
            P(None, None, "patch", "chan"),
            P("chan"),
            P(None, "chan"),
            P("chan"),
            P("chan"),
            P(None, None, "patch", "chan"),
            P("chan"),
        ),
        out_specs=P("chan", ("groups", "patch"), "col"),
        check_vma=False,
    )
```

```python
import math

import jax
import jax.numpy as jnp
from jax import lax
from jax.sharding import PartitionSpec as P

GROUPS = 32


norm_epsilon = 1e-05


def extended(value, sides, width):
    for axis, dim in sides:
        count, length = (lax.axis_size(axis), value.shape[dim])
        up = [(i, (i + 1) % count) for i in range(count - 1)]
        down = [(j, i) for i, j in up]
        last = lax.slice_in_dim(value, length - width, length, axis=dim)
        leading = lax.slice_in_dim(value, 0, width, axis=dim)
        before = lax.ppermute(last, axis, up)
        after = lax.ppermute(leading, axis, down)
        value = jnp.concatenate([before, value, after], axis=dim)
    return value


def group_moments(values, group_count, cell_total):
    grouped = values.reshape(group_count, -1)
    local_sums = (jnp.sum(grouped, axis=1), jnp.sum(grouped * grouped, axis=1))
    totals = lax.psum((local_sums[0], local_sums[1]), ("patch", "col"))
    group_mean = totals[0] / cell_total
    group_var = totals[1] / cell_total - group_mean * group_mean
    return (group_mean, lax.rsqrt(group_var + norm_epsilon))


def activate(values, group_mean, inv_std, gain_vec, shift_vec):
    channels = values.shape[0]
    width = channels // group_mean.shape[0]
    shape_tail = (channels,) + (1,) * (values.ndim - 1)
    mean_chan = jnp.repeat(group_mean, width).reshape(shape_tail)
    inv_chan = jnp.repeat(inv_std, width).reshape(shape_tail)
    normed = (values - mean_chan) * inv_chan * gain_vec.reshape(shape_tail) + shift_vec.reshape(
        shape_tail
    )
    return jax.nn.silu(normed)


def swap(value, axis):
    return lax.ppermute(value, axis, [(0, 1), (1, 0)])


def fetch_weights(weights):
    taps = weights.shape[0] * weights.shape[1]
    out_block, in_block = weights.shape[2], weights.shape[3]
    flat = weights.reshape(taps, out_block, in_block)
    share_y = lax.axis_size("groups") == 2
    n_y = 2 if share_y else 1
    n_c = lax.axis_size("col")
    y_id = lax.axis_index("groups") if share_y else 0
    c_id = lax.axis_index("col")
    piece = out_block // (n_y * n_c)
    own = y_id * n_c + c_id
    mine = lax.dynamic_slice_in_dim(flat, own * piece, piece, axis=1)
    got = lax.all_gather(mine, "patch", axis=0, tiled=False)
    slots, ids = [got], [own]
    if share_y:
        slots.append(swap(got, "groups"))
        ids.append((1 - y_id) * n_c + c_id)
    if n_c == 2:
        for i in range(len(slots)):
            slots.append(swap(slots[i], "col"))
            ids.append(ids[i] - c_id + (1 - c_id))
    return slots, ids


def conv_slots(padded, slots):
    in_chans, height_pad, width_pad = padded.shape
    height = height_pad - 2
    width = width_pad - 2
    windows = [
        [padded[:, a : a + height, b : b + width] for b in range(3)] for a in range(3)
    ]
    outs = []
    for got in slots:
        total = None
        for a in range(3):
            for b in range(3):
                term = jnp.einsum(
                    "poc,chw->pohw",
                    got[:, a * 3 + b],
                    windows[a][b],
                    preferred_element_type=jnp.float32,
                )
                total = term if total is None else total + term
        outs.append(total.astype(jnp.bfloat16))
    return jnp.stack(outs)


def reduce_chan(parts, ids):
    n_slots, blocks, piece, height, width = parts.shape
    n_k = lax.axis_size("chan")
    k = lax.axis_index("chan")
    per = blocks // n_k
    if n_k == 2:
        mine = lax.dynamic_slice_in_dim(parts, k * per, per, axis=1)
        other = lax.dynamic_slice_in_dim(parts, (1 - k) * per, per, axis=1)
        total = mine.astype(jnp.float32) + swap(other, "chan").astype(jnp.float32)
    else:
        split = parts.reshape(n_slots, n_k, per, piece, height, width)
        split = jnp.moveaxis(split, 1, 0)
        got = lax.all_to_all(split, "chan", 0, 0, tiled=False)
        total = jnp.sum(got.astype(jnp.float32), axis=0)
    where = jnp.zeros((n_slots,), jnp.int32)
    for slot, ident in enumerate(ids):
        where = where.at[ident].set(slot)
    ordered = jnp.take(total, where, axis=0)
    ordered = jnp.moveaxis(ordered, 0, 1)
    return ordered.reshape(per * n_slots * piece, height, width)


def line_weights(weights, after=None):
    taps = weights.shape[0] * weights.shape[1]
    out_block, in_block = weights.shape[2], weights.shape[3]
    flat = weights.reshape(taps, out_block, in_block)
    if after is not None:
        flat, _ = lax.optimization_barrier((flat, after))
    n_p, n_c = lax.axis_size("patch"), lax.axis_size("col")
    p, c, y = lax.axis_index("patch"), lax.axis_index("col"), lax.axis_index("groups")
    half = out_block // 2
    own_half = lax.dynamic_slice_in_dim(flat, y * half, half, axis=1)
    own_other = lax.dynamic_slice_in_dim(flat, (1 - y) * half, half, axis=1)
    per_core = n_p // n_c
    roles = range(per_core)
    home = lambda r, cc: cc * per_core + r
    zero = jnp.zeros_like(own_half)
    held = [jnp.where(p == home(r, c), own_half, zero) for r in roles]
    other = [jnp.where(p == home(r, c), own_other, zero) for r in roles]
    lines = []

    def pick(values, tests):
        out = values[-1]
        for value, test in zip(values[:-1], tests[:-1]):
            out = jnp.where(test, value, out)
        return out

    for t in range(1, n_p):
        new_held = list(held)
        for d in (1, -1):
            pairs, senders = [], set()
            for r in roles:
                for cc in range(n_c):
                    z_to = home(r, cc) + d * t
                    if 0 <= z_to < n_p:
                        pairs.append(((z_to - d) * n_c + cc, z_to * n_c + cc))
            if not pairs:
                continue
            assert len({a for a, _ in pairs}) == len(pairs)
            assert len({b for _, b in pairs}) == len(pairs)
            payload = pick(held, [p == home(r, c) + d * (t - 1) for r in roles])
            got = lax.ppermute(payload, ("patch", "col"), pairs)
            for r in roles:
                new_held[r] = jnp.where(p == home(r, c) + d * t, got, new_held[r])
        held = new_held
        if t == n_p - 1:
            lines = list(held)
        trade = []
        for g in range(2):
            for z in range(n_p):
                for cc in range(n_c):
                    if any(abs(z - home(r, cc)) == t for r in roles):
                        trade.append(((g * n_p + z) * n_c + cc, ((1 - g) * n_p + z) * n_c + cc))
        if not trade:
            continue
        final = [abs(p - home(r, c)) == t for r in roles]
        got = lax.ppermute(pick(held, final), ("groups", "patch", "col"), trade)
        other = [jnp.where(final[r], got, other[r]) for r in roles]
    pieces = []
    for r in roles:
        pieces += [jnp.where(y == 0, held[r], other[r]), jnp.where(y == 0, other[r], held[r])]
    return jnp.concatenate(pieces, axis=1), lines


def full_width(block):
    other = swap(block, "col")
    c = lax.axis_index("col")
    left = jnp.where(c == 0, block, other)
    right = jnp.where(c == 0, other, block)
    return jnp.pad(jnp.concatenate([left, right], axis=2), ((0, 0), (0, 0), (1, 1)))


def conv_full(padded, weight):
    kernel = weight.reshape(3, 3, weight.shape[1], weight.shape[2])
    total = lax.conv_general_dilated(
        padded[None],
        kernel,
        window_strides=(1, 1),
        padding="VALID",
        dimension_numbers=("NCHW", "HWOI", "NCHW"),
        preferred_element_type=jnp.float32,
    )[0]
    return total.astype(jnp.bfloat16)


def reduce_cores(part):
    k, c = lax.axis_index("chan"), lax.axis_index("col")
    width = part.shape[2] // 2
    piece = lambda j: lax.dynamic_slice_in_dim(part, j * width, width, axis=2)
    send_a = piece(jnp.where(k == c, 1 - c, c))
    got_a = lax.ppermute(send_a, ("chan", "col"), [(0, 1), (3, 2), (1, 3), (2, 0)])
    got_b = lax.ppermute(piece(1 - c), ("chan", "col"), [(1, 2), (2, 1)])
    first = jnp.where(k == c, piece(c), got_b)
    return first.astype(jnp.float32) + got_a.astype(jnp.float32)


def fast_path():
    return (
        lax.axis_size("chan") == 2
        and lax.axis_size("col") == 2
        and lax.axis_size("groups") == 2
        and lax.axis_size("patch") % 2 == 0
    )


def time_bias(step_index, temb_weight):
    half_width = temb_weight.shape[0] // 2
    freqs = jnp.exp(-math.log(10000.0) * jnp.arange(half_width).astype(jnp.float32) / half_width)
    angles = step_index[0].astype(jnp.float32) * freqs
    embed = jnp.concatenate([jnp.cos(angles), jnp.sin(angles)])
    gated = jax.nn.silu(embed).astype(jnp.bfloat16)
    return jnp.dot(gated[None, :], temb_weight, preferred_element_type=jnp.float32)[0]


def on_device(
    features,
    cache_codes,
    cache_scale,
    step_index,
    gn1_gain,
    gn1_shift,
    conv1_weight,
    conv1_bias,
    temb_weight,
    gn2_gain,
    gn2_shift,
    conv2_weight,
    conv2_bias,
):
    channels, rows_here, cols_here = features.shape
    patches = lax.axis_size("patch")
    group_count = GROUPS // lax.axis_size("chan")
    cell_total = channels // group_count * rows_here * patches * cols_here * lax.axis_size("col")
    fast = fast_path()
    feat32 = features.astype(jnp.float32)
    mean_one, inv_one = group_moments(feat32, group_count, cell_total)
    if fast:
        weight_one, lines_one = line_weights(conv1_weight, after=mean_one)
        weight_two, _ = line_weights(conv2_weight, after=lines_one)
    else:
        slots_one, ids_one = fetch_weights(conv1_weight)
        slots_two, ids_two = fetch_weights(conv2_weight)
    own_act = activate(feat32, mean_one, inv_one, gn1_gain, gn1_shift)
    stale = cache_codes.astype(jnp.float32) * cache_scale[None, :, :]
    rim_act = activate(stale, mean_one, inv_one, gn1_gain, gn1_shift)
    where_patch = lax.axis_index("patch")
    upper_rim = rim_act[:, 0:1, :] * (where_patch > 0).astype(jnp.float32)
    lower_rim = rim_act[:, 1:2, :] * (where_patch < patches - 1).astype(jnp.float32)
    block_one = jnp.concatenate([upper_rim, own_act, lower_rim], axis=1).astype(jnp.bfloat16)
    if fast:
        sum_one = reduce_cores(conv_full(full_width(block_one), weight_one))
    else:
        padded_one = extended(block_one, (("col", 2),), 1)
        sum_one = reduce_chan(conv_slots(padded_one, slots_one), ids_one)
    temb_bias = time_bias(step_index, temb_weight)
    hidden = (sum_one + conv1_bias[:, None, None] + temb_bias[:, None, None]).astype(jnp.bfloat16)
    hidden32 = hidden.astype(jnp.float32)
    mean_two, inv_two = group_moments(hidden32, group_count, cell_total)
    act_two = activate(hidden32, mean_two, inv_two, gn2_gain, gn2_shift).astype(jnp.bfloat16)
    if fast:
        rows_two = extended(act_two, (("patch", 1),), 1)
        sum_two = reduce_cores(conv_full(full_width(rows_two), weight_two))
    else:
        padded_two = extended(act_two, (("patch", 1), ("col", 2)), 1)
        sum_two = reduce_chan(conv_slots(padded_two, slots_two), ids_two)
    return (sum_two + conv2_bias[:, None, None] + feat32).astype(jnp.bfloat16)


def solution(mesh):
    return jax.shard_map(
        on_device,
        mesh=mesh,
        in_specs=(
            P("chan", ("groups", "patch"), "col"),
            P("chan", ("groups", "patch"), "col"),
            P(("groups", "patch"), "col"),
            P("groups"),
            P("chan"),
            P("chan"),
            P(None, None, "patch", "chan"),
            P("chan"),
            P(None, "chan"),
            P("chan"),
            P("chan"),
            P(None, None, "patch", "chan"),
            P("chan"),
        ),
        out_specs=P("chan", ("groups", "patch"), "col"),
        check_vma=False,
    )
```

```python
import math

import jax
import jax.numpy as jnp
from jax import lax
from jax.sharding import PartitionSpec as P

GROUPS = 32


norm_epsilon = 1e-05


def extended(value, sides, width):
    for axis, dim in sides:
        count, length = (lax.axis_size(axis), value.shape[dim])
        up = [(i, (i + 1) % count) for i in range(count - 1)]
        down = [(j, i) for i, j in up]
        last = lax.slice_in_dim(value, length - width, length, axis=dim)
        leading = lax.slice_in_dim(value, 0, width, axis=dim)
        before = lax.ppermute(last, axis, up)
        after = lax.ppermute(leading, axis, down)
        value = jnp.concatenate([before, value, after], axis=dim)
    return value


def group_moments(values, group_count, cell_total):
    grouped = values.reshape(group_count, -1)
    local_sums = (jnp.sum(grouped, axis=1), jnp.sum(grouped * grouped, axis=1))
    totals = lax.psum((local_sums[0], local_sums[1]), ("patch", "col"))
    group_mean = totals[0] / cell_total
    group_var = totals[1] / cell_total - group_mean * group_mean
    return (group_mean, lax.rsqrt(group_var + norm_epsilon))


def activate(values, group_mean, inv_std, gain_vec, shift_vec):
    channels = values.shape[0]
    width = channels // group_mean.shape[0]
    shape_tail = (channels,) + (1,) * (values.ndim - 1)
    mean_chan = jnp.repeat(group_mean, width).reshape(shape_tail)
    inv_chan = jnp.repeat(inv_std, width).reshape(shape_tail)
    normed = (values - mean_chan) * inv_chan * gain_vec.reshape(shape_tail) + shift_vec.reshape(
        shape_tail
    )
    return jax.nn.silu(normed)


def swap(value, axis):
    return lax.ppermute(value, axis, [(0, 1), (1, 0)])


def fetch_weights(weights):
    taps = weights.shape[0] * weights.shape[1]
    out_block, in_block = weights.shape[2], weights.shape[3]
    flat = weights.reshape(taps, out_block, in_block)
    share_y = lax.axis_size("groups") == 2
    n_y = 2 if share_y else 1
    n_c = lax.axis_size("col")
    y_id = lax.axis_index("groups") if share_y else 0
    c_id = lax.axis_index("col")
    piece = out_block // (n_y * n_c)
    own = y_id * n_c + c_id
    mine = lax.dynamic_slice_in_dim(flat, own * piece, piece, axis=1)
    got = lax.all_gather(mine, "patch", axis=0, tiled=False)
    slots, ids = [got], [own]
    if share_y:
        slots.append(swap(got, "groups"))
        ids.append((1 - y_id) * n_c + c_id)
    if n_c == 2:
        for i in range(len(slots)):
            slots.append(swap(slots[i], "col"))
            ids.append(ids[i] - c_id + (1 - c_id))
    return slots, ids


def conv_slots(padded, slots):
    in_chans, height_pad, width_pad = padded.shape
    height = height_pad - 2
    width = width_pad - 2
    windows = [
        [padded[:, a : a + height, b : b + width] for b in range(3)] for a in range(3)
    ]
    outs = []
    for got in slots:
        total = None
        for a in range(3):
            for b in range(3):
                term = jnp.einsum(
                    "poc,chw->pohw",
                    got[:, a * 3 + b],
                    windows[a][b],
                    preferred_element_type=jnp.float32,
                )
                total = term if total is None else total + term
        outs.append(total.astype(jnp.bfloat16))
    return jnp.stack(outs)


def reduce_chan(parts, ids):
    n_slots, blocks, piece, height, width = parts.shape
    n_k = lax.axis_size("chan")
    k = lax.axis_index("chan")
    per = blocks // n_k
    if n_k == 2:
        mine = lax.dynamic_slice_in_dim(parts, k * per, per, axis=1)
        other = lax.dynamic_slice_in_dim(parts, (1 - k) * per, per, axis=1)
        total = mine.astype(jnp.float32) + swap(other, "chan").astype(jnp.float32)
    else:
        split = parts.reshape(n_slots, n_k, per, piece, height, width)
        split = jnp.moveaxis(split, 1, 0)
        got = lax.all_to_all(split, "chan", 0, 0, tiled=False)
        total = jnp.sum(got.astype(jnp.float32), axis=0)
    where = jnp.zeros((n_slots,), jnp.int32)
    for slot, ident in enumerate(ids):
        where = where.at[ident].set(slot)
    ordered = jnp.take(total, where, axis=0)
    ordered = jnp.moveaxis(ordered, 0, 1)
    return ordered.reshape(per * n_slots * piece, height, width)


def line_weights(weights, after=None):
    taps = weights.shape[0] * weights.shape[1]
    out_block, in_block = weights.shape[2], weights.shape[3]
    flat = weights.reshape(taps, out_block, in_block)
    if after is not None:
        flat, _ = lax.optimization_barrier((flat, after))
    n_p, n_c = lax.axis_size("patch"), lax.axis_size("col")
    p, c, y = lax.axis_index("patch"), lax.axis_index("col"), lax.axis_index("groups")
    half = out_block // 2
    own_half = lax.dynamic_slice_in_dim(flat, y * half, half, axis=1)
    own_other = lax.dynamic_slice_in_dim(flat, (1 - y) * half, half, axis=1)
    per_core = n_p // n_c
    needs = lambda z, cc, s: cc * per_core <= s < (cc + 1) * per_core
    bufs = {"own": own_half, "own_o": own_other}
    last = {1: own_half, -1: own_half}
    lines = []
    for t in range(1, n_p):
        for d in (1, -1):
            pairs = [((z - d) * n_c + cc, z * n_c + cc)
                     for z in range(n_p) for cc in range(n_c)
                     if 0 <= z - d < n_p and needs(z, cc, z - d * t)]
            if not pairs:
                continue
            got = lax.ppermute(last[d], ("patch", "col"), pairs)
            last[d] = got
            bufs[(t, d)] = got
            lines.append(got)
            trade = [((g * n_p + z) * n_c + cc, ((1 - g) * n_p + z) * n_c + cc)
                     for g in range(2) for z in range(n_p) for cc in range(n_c)
                     if 0 <= z - d < n_p and needs(z, cc, z - d * t)]
            bufs[(t, d, "o")] = lax.ppermute(got, ("groups", "patch", "col"), trade)
    names = sorted(bufs, key=str)
    operands = [bufs[n] for n in names]

    def branch(z, cc, g):
        def run(*ops):
            table = dict(zip(names, ops))
            pieces = []
            for r in range(per_core):
                s = cc * per_core + r
                if s == z:
                    mine, other = table["own"], table["own_o"]
                else:
                    d = 1 if s < z else -1
                    t = abs(z - s)
                    mine, other = table[(t, d)], table[(t, d, "o")]
                pieces += [mine, other] if g == 0 else [other, mine]
            return jnp.concatenate(pieces, axis=1)
        return run

    cases = [branch(z, cc, g) for g in range(2) for z in range(n_p) for cc in range(n_c)]
    index = (y * n_p + p) * n_c + c
    return lax.switch(index, cases, *operands), lines


def full_width(block):
    other = swap(block, "col")
    c = lax.axis_index("col")
    left = jnp.where(c == 0, block, other)
    right = jnp.where(c == 0, other, block)
    return jnp.pad(jnp.concatenate([left, right], axis=2), ((0, 0), (0, 0), (1, 1)))


def conv_full(padded, weight):
    kernel = weight.reshape(3, 3, weight.shape[1], weight.shape[2])
    total = lax.conv_general_dilated(
        padded[None],
        kernel,
        window_strides=(1, 1),
        padding="VALID",
        dimension_numbers=("NCHW", "HWOI", "NCHW"),
        preferred_element_type=jnp.float32,
    )[0]
    return total.astype(jnp.bfloat16)


def reduce_cores(part):
    k, c = lax.axis_index("chan"), lax.axis_index("col")
    width = part.shape[2] // 2
    piece = lambda j: lax.dynamic_slice_in_dim(part, j * width, width, axis=2)
    send_a = piece(jnp.where(k == c, 1 - c, c))
    got_a = lax.ppermute(send_a, ("chan", "col"), [(0, 1), (3, 2), (1, 3), (2, 0)])
    got_b = lax.ppermute(piece(1 - c), ("chan", "col"), [(1, 2), (2, 1)])
    first = jnp.where(k == c, piece(c), got_b)
    return first.astype(jnp.float32) + got_a.astype(jnp.float32)


def fast_path():
    return (
        lax.axis_size("chan") == 2
        and lax.axis_size("col") == 2
        and lax.axis_size("groups") == 2
        and lax.axis_size("patch") % 2 == 0
    )


def time_bias(step_index, temb_weight):
    half_width = temb_weight.shape[0] // 2
    freqs = jnp.exp(-math.log(10000.0) * jnp.arange(half_width).astype(jnp.float32) / half_width)
    angles = step_index[0].astype(jnp.float32) * freqs
    embed = jnp.concatenate([jnp.cos(angles), jnp.sin(angles)])
    gated = jax.nn.silu(embed).astype(jnp.bfloat16)
    return jnp.dot(gated[None, :], temb_weight, preferred_element_type=jnp.float32)[0]


def on_device(
    features,
    cache_codes,
    cache_scale,
    step_index,
    gn1_gain,
    gn1_shift,
    conv1_weight,
    conv1_bias,
    temb_weight,
    gn2_gain,
    gn2_shift,
    conv2_weight,
    conv2_bias,
):
    channels, rows_here, cols_here = features.shape
    patches = lax.axis_size("patch")
    group_count = GROUPS // lax.axis_size("chan")
    cell_total = channels // group_count * rows_here * patches * cols_here * lax.axis_size("col")
    fast = fast_path()
    feat32 = features.astype(jnp.float32)
    mean_one, inv_one = group_moments(feat32, group_count, cell_total)
    if fast:
        weight_one, lines_one = line_weights(conv1_weight, after=mean_one)
        weight_two, _ = line_weights(conv2_weight, after=lines_one)
    else:
        slots_one, ids_one = fetch_weights(conv1_weight)
        slots_two, ids_two = fetch_weights(conv2_weight)
    own_act = activate(feat32, mean_one, inv_one, gn1_gain, gn1_shift)
    stale = cache_codes.astype(jnp.float32) * cache_scale[None, :, :]
    rim_act = activate(stale, mean_one, inv_one, gn1_gain, gn1_shift)
    where_patch = lax.axis_index("patch")
    upper_rim = rim_act[:, 0:1, :] * (where_patch > 0).astype(jnp.float32)
    lower_rim = rim_act[:, 1:2, :] * (where_patch < patches - 1).astype(jnp.float32)
    block_one = jnp.concatenate([upper_rim, own_act, lower_rim], axis=1).astype(jnp.bfloat16)
    if fast:
        sum_one = reduce_cores(conv_full(full_width(block_one), weight_one))
    else:
        padded_one = extended(block_one, (("col", 2),), 1)
        sum_one = reduce_chan(conv_slots(padded_one, slots_one), ids_one)
    temb_bias = time_bias(step_index, temb_weight)
    hidden = (sum_one + conv1_bias[:, None, None] + temb_bias[:, None, None]).astype(jnp.bfloat16)
    hidden32 = hidden.astype(jnp.float32)
    mean_two, inv_two = group_moments(hidden32, group_count, cell_total)
    act_two = activate(hidden32, mean_two, inv_two, gn2_gain, gn2_shift).astype(jnp.bfloat16)
    if fast:
        rows_two = extended(act_two, (("patch", 1),), 1)
        sum_two = reduce_cores(conv_full(full_width(rows_two), weight_two))
    else:
        padded_two = extended(act_two, (("patch", 1), ("col", 2)), 1)
        sum_two = reduce_chan(conv_slots(padded_two, slots_two), ids_two)
    return (sum_two + conv2_bias[:, None, None] + feat32).astype(jnp.bfloat16)


def solution(mesh):
    return jax.shard_map(
        on_device,
        mesh=mesh,
        in_specs=(
            P("chan", ("groups", "patch"), "col"),
            P("chan", ("groups", "patch"), "col"),
            P(("groups", "patch"), "col"),
            P("groups"),
            P("chan"),
            P("chan"),
            P(None, None, "patch", "chan"),
            P("chan"),
            P(None, "chan"),
            P("chan"),
            P("chan"),
            P(None, None, "patch", "chan"),
            P("chan"),
        ),
        out_specs=P("chan", ("groups", "patch"), "col"),
        check_vma=False,
    )
```

```python
import math

import jax
import jax.numpy as jnp
from jax import lax
from jax.sharding import PartitionSpec as P

GROUPS = 32


norm_epsilon = 1e-05


def extended(value, sides, width):
    for axis, dim in sides:
        count, length = (lax.axis_size(axis), value.shape[dim])
        up = [(i, (i + 1) % count) for i in range(count - 1)]
        down = [(j, i) for i, j in up]
        last = lax.slice_in_dim(value, length - width, length, axis=dim)
        leading = lax.slice_in_dim(value, 0, width, axis=dim)
        before = lax.ppermute(last, axis, up)
        after = lax.ppermute(leading, axis, down)
        value = jnp.concatenate([before, value, after], axis=dim)
    return value


def group_moments(values, group_count, cell_total):
    grouped = values.reshape(group_count, -1)
    local_sums = (jnp.sum(grouped, axis=1), jnp.sum(grouped * grouped, axis=1))
    totals = lax.psum((local_sums[0], local_sums[1]), ("patch", "col"))
    group_mean = totals[0] / cell_total
    group_var = totals[1] / cell_total - group_mean * group_mean
    return (group_mean, lax.rsqrt(group_var + norm_epsilon))


def activate(values, group_mean, inv_std, gain_vec, shift_vec):
    channels = values.shape[0]
    width = channels // group_mean.shape[0]
    shape_tail = (channels,) + (1,) * (values.ndim - 1)
    mean_chan = jnp.repeat(group_mean, width).reshape(shape_tail)
    inv_chan = jnp.repeat(inv_std, width).reshape(shape_tail)
    normed = (values - mean_chan) * inv_chan * gain_vec.reshape(shape_tail) + shift_vec.reshape(
        shape_tail
    )
    return jax.nn.silu(normed)


def swap(value, axis):
    return lax.ppermute(value, axis, [(0, 1), (1, 0)])


def fetch_weights(weights):
    taps = weights.shape[0] * weights.shape[1]
    out_block, in_block = weights.shape[2], weights.shape[3]
    flat = weights.reshape(taps, out_block, in_block)
    share_y = lax.axis_size("groups") == 2
    n_y = 2 if share_y else 1
    n_c = lax.axis_size("col")
    y_id = lax.axis_index("groups") if share_y else 0
    c_id = lax.axis_index("col")
    piece = out_block // (n_y * n_c)
    own = y_id * n_c + c_id
    mine = lax.dynamic_slice_in_dim(flat, own * piece, piece, axis=1)
    got = lax.all_gather(mine, "patch", axis=0, tiled=False)
    slots, ids = [got], [own]
    if share_y:
        slots.append(swap(got, "groups"))
        ids.append((1 - y_id) * n_c + c_id)
    if n_c == 2:
        for i in range(len(slots)):
            slots.append(swap(slots[i], "col"))
            ids.append(ids[i] - c_id + (1 - c_id))
    return slots, ids


def conv_slots(padded, slots):
    in_chans, height_pad, width_pad = padded.shape
    height = height_pad - 2
    width = width_pad - 2
    windows = [
        [padded[:, a : a + height, b : b + width] for b in range(3)] for a in range(3)
    ]
    outs = []
    for got in slots:
        total = None
        for a in range(3):
            for b in range(3):
                term = jnp.einsum(
                    "poc,chw->pohw",
                    got[:, a * 3 + b],
                    windows[a][b],
                    preferred_element_type=jnp.float32,
                )
                total = term if total is None else total + term
        outs.append(total.astype(jnp.bfloat16))
    return jnp.stack(outs)


def reduce_chan(parts, ids):
    n_slots, blocks, piece, height, width = parts.shape
    n_k = lax.axis_size("chan")
    k = lax.axis_index("chan")
    per = blocks // n_k
    if n_k == 2:
        mine = lax.dynamic_slice_in_dim(parts, k * per, per, axis=1)
        other = lax.dynamic_slice_in_dim(parts, (1 - k) * per, per, axis=1)
        total = mine.astype(jnp.float32) + swap(other, "chan").astype(jnp.float32)
    else:
        split = parts.reshape(n_slots, n_k, per, piece, height, width)
        split = jnp.moveaxis(split, 1, 0)
        got = lax.all_to_all(split, "chan", 0, 0, tiled=False)
        total = jnp.sum(got.astype(jnp.float32), axis=0)
    where = jnp.zeros((n_slots,), jnp.int32)
    for slot, ident in enumerate(ids):
        where = where.at[ident].set(slot)
    ordered = jnp.take(total, where, axis=0)
    ordered = jnp.moveaxis(ordered, 0, 1)
    return ordered.reshape(per * n_slots * piece, height, width)


def line_weights(weights, after=None):
    taps = weights.shape[0] * weights.shape[1]
    out_block, in_block = weights.shape[2], weights.shape[3]
    flat = weights.reshape(taps, out_block, in_block)
    if after is not None:
        flat, _ = lax.optimization_barrier((flat, after))
    n_p, n_c = lax.axis_size("patch"), lax.axis_size("col")
    p, c, y = lax.axis_index("patch"), lax.axis_index("col"), lax.axis_index("groups")
    half = out_block // 2
    own_half = lax.dynamic_slice_in_dim(flat, y * half, half, axis=1)
    own_other = lax.dynamic_slice_in_dim(flat, (1 - y) * half, half, axis=1)
    per_core = n_p // n_c
    needs = lambda z, cc, s: cc * per_core <= s < (cc + 1) * per_core
    bufs = {"own": own_half, "own_o": own_other}
    last = {1: own_half, -1: own_half}
    lines = []
    for t in range(1, n_p):
        for d in (1, -1):
            pairs = [((z - d) * n_c + cc, z * n_c + cc)
                     for z in range(n_p) for cc in range(n_c)
                     if 0 <= z - d < n_p and needs(z, cc, z - d * t)]
            if not pairs:
                continue
            got = lax.ppermute(last[d], ("patch", "col"), pairs)
            last[d] = got
            bufs[(t, d)] = got
            lines.append(got)
            trade = [((g * n_p + z) * n_c + cc, ((1 - g) * n_p + z) * n_c + cc)
                     for g in range(2) for z in range(n_p) for cc in range(n_c)
                     if 0 <= z - d < n_p and needs(z, cc, z - d * t)]
            bufs[(t, d, "o")] = lax.ppermute(got, ("groups", "patch", "col"), trade)
    names = sorted(bufs, key=str)
    operands = [bufs[n] for n in names]

    def branch(z, cc, g):
        def run(*ops):
            table = dict(zip(names, ops))
            pieces = []
            for r in range(per_core):
                s = cc * per_core + r
                if s == z:
                    mine, other = table["own"], table["own_o"]
                else:
                    d = 1 if s < z else -1
                    t = abs(z - s)
                    mine, other = table[(t, d)], table[(t, d, "o")]
                pieces += [mine, other] if g == 0 else [other, mine]
            return jnp.concatenate(pieces, axis=1)
        return run

    cases = [branch(z, cc, g) for g in range(2) for z in range(n_p) for cc in range(n_c)]
    index = (y * n_p + p) * n_c + c
    return lax.switch(index, cases, *operands), lines


def full_width(block):
    other = swap(block, "col")
    c = lax.axis_index("col")
    left = jnp.where(c == 0, block, other)
    right = jnp.where(c == 0, other, block)
    return jnp.pad(jnp.concatenate([left, right], axis=2), ((0, 0), (0, 0), (1, 1)))


def conv_full(padded, weight):
    kernel = weight.reshape(3, 3, weight.shape[1], weight.shape[2])
    total = lax.conv_general_dilated(
        padded[None],
        kernel,
        window_strides=(1, 1),
        padding="VALID",
        dimension_numbers=("NCHW", "HWOI", "NCHW"),
        preferred_element_type=jnp.float32,
    )[0]
    return total.astype(jnp.bfloat16)


def reduce_cores(part):
    k, c = lax.axis_index("chan"), lax.axis_index("col")
    width = part.shape[2] // 2
    piece = lambda j: lax.dynamic_slice_in_dim(part, j * width, width, axis=2)
    send_a = piece(jnp.where(k == c, 1 - c, c))
    got_a = lax.ppermute(send_a, ("chan", "col"), [(0, 1), (3, 2), (1, 3), (2, 0)])
    got_b = lax.ppermute(piece(1 - c), ("chan", "col"), [(1, 2), (2, 1)])
    first = jnp.where(k == c, piece(c), got_b)
    return first.astype(jnp.float32) + got_a.astype(jnp.float32)


def fast_path():
    return (
        lax.axis_size("chan") == 2
        and lax.axis_size("col") == 2
        and lax.axis_size("groups") == 2
        and lax.axis_size("patch") % 2 == 0
    )


def time_bias(step_index, temb_weight):
    half_width = temb_weight.shape[0] // 2
    freqs = jnp.exp(-math.log(10000.0) * jnp.arange(half_width).astype(jnp.float32) / half_width)
    angles = step_index[0].astype(jnp.float32) * freqs
    embed = jnp.concatenate([jnp.cos(angles), jnp.sin(angles)])
    gated = jax.nn.silu(embed).astype(jnp.bfloat16)
    return jnp.dot(gated[None, :], temb_weight, preferred_element_type=jnp.float32)[0]


def on_device(
    features,
    cache_codes,
    cache_scale,
    step_index,
    gn1_gain,
    gn1_shift,
    conv1_weight,
    conv1_bias,
    temb_weight,
    gn2_gain,
    gn2_shift,
    conv2_weight,
    conv2_bias,
):
    channels, rows_here, cols_here = features.shape
    patches = lax.axis_size("patch")
    group_count = GROUPS // lax.axis_size("chan")
    cell_total = channels // group_count * rows_here * patches * cols_here * lax.axis_size("col")
    fast = fast_path()
    feat32 = features.astype(jnp.float32)
    mean_one, inv_one = group_moments(feat32, group_count, cell_total)
    if fast:
        weight_one, lines_one = line_weights(conv1_weight)
        weight_two, _ = line_weights(conv2_weight, after=lines_one)
    else:
        slots_one, ids_one = fetch_weights(conv1_weight)
        slots_two, ids_two = fetch_weights(conv2_weight)
    own_act = activate(feat32, mean_one, inv_one, gn1_gain, gn1_shift)
    stale = cache_codes.astype(jnp.float32) * cache_scale[None, :, :]
    rim_act = activate(stale, mean_one, inv_one, gn1_gain, gn1_shift)
    where_patch = lax.axis_index("patch")
    upper_rim = rim_act[:, 0:1, :] * (where_patch > 0).astype(jnp.float32)
    lower_rim = rim_act[:, 1:2, :] * (where_patch < patches - 1).astype(jnp.float32)
    block_one = jnp.concatenate([upper_rim, own_act, lower_rim], axis=1).astype(jnp.bfloat16)
    if fast:
        sum_one = reduce_cores(conv_full(full_width(block_one), weight_one))
    else:
        padded_one = extended(block_one, (("col", 2),), 1)
        sum_one = reduce_chan(conv_slots(padded_one, slots_one), ids_one)
    temb_bias = time_bias(step_index, temb_weight)
    hidden = (sum_one + conv1_bias[:, None, None] + temb_bias[:, None, None]).astype(jnp.bfloat16)
    hidden32 = hidden.astype(jnp.float32)
    mean_two, inv_two = group_moments(hidden32, group_count, cell_total)
    act_two = activate(hidden32, mean_two, inv_two, gn2_gain, gn2_shift).astype(jnp.bfloat16)
    if fast:
        rows_two = extended(act_two, (("patch", 1),), 1)
        sum_two = reduce_cores(conv_full(full_width(rows_two), weight_two))
    else:
        padded_two = extended(act_two, (("patch", 1), ("col", 2)), 1)
        sum_two = reduce_chan(conv_slots(padded_two, slots_two), ids_two)
    return (sum_two + conv2_bias[:, None, None] + feat32).astype(jnp.bfloat16)


def solution(mesh):
    return jax.shard_map(
        on_device,
        mesh=mesh,
        in_specs=(
            P("chan", ("groups", "patch"), "col"),
            P("chan", ("groups", "patch"), "col"),
            P(("groups", "patch"), "col"),
            P("groups"),
            P("chan"),
            P("chan"),
            P(None, None, "patch", "chan"),
            P("chan"),
            P(None, "chan"),
            P("chan"),
            P("chan"),
            P(None, None, "patch", "chan"),
            P("chan"),
        ),
        out_specs=P("chan", ("groups", "patch"), "col"),
        check_vma=False,
    )
```

```python
import math

import jax
import jax.numpy as jnp
from jax import lax
from jax.sharding import PartitionSpec as P

GROUPS = 32


norm_epsilon = 1e-05


def extended(value, sides, width):
    for axis, dim in sides:
        count, length = (lax.axis_size(axis), value.shape[dim])
        up = [(i, (i + 1) % count) for i in range(count - 1)]
        down = [(j, i) for i, j in up]
        last = lax.slice_in_dim(value, length - width, length, axis=dim)
        leading = lax.slice_in_dim(value, 0, width, axis=dim)
        before = lax.ppermute(last, axis, up)
        after = lax.ppermute(leading, axis, down)
        value = jnp.concatenate([before, value, after], axis=dim)
    return value


def group_moments(values, group_count, cell_total):
    grouped = values.reshape(group_count, -1)
    local_sums = (jnp.sum(grouped, axis=1), jnp.sum(grouped * grouped, axis=1))
    summed = jnp.stack(local_sums)
    if lax.axis_size("col") == 2:
        summed = summed + swap(summed, "col")
    else:
        summed = lax.psum(summed, "col")
    n_p = lax.axis_size("patch")
    if n_p & (n_p - 1) == 0:
        step = 1
        while step < n_p:
            summed = summed + lax.ppermute(summed, "patch", [(i, i ^ step) for i in range(n_p)])
            step *= 2
    else:
        summed = lax.psum(summed, "patch")
    totals = (summed[0], summed[1])
    group_mean = totals[0] / cell_total
    group_var = totals[1] / cell_total - group_mean * group_mean
    return (group_mean, lax.rsqrt(group_var + norm_epsilon))


def activate(values, group_mean, inv_std, gain_vec, shift_vec):
    channels = values.shape[0]
    width = channels // group_mean.shape[0]
    shape_tail = (channels,) + (1,) * (values.ndim - 1)
    mean_chan = jnp.repeat(group_mean, width).reshape(shape_tail)
    inv_chan = jnp.repeat(inv_std, width).reshape(shape_tail)
    normed = (values - mean_chan) * inv_chan * gain_vec.reshape(shape_tail) + shift_vec.reshape(
        shape_tail
    )
    return jax.nn.silu(normed)


def swap(value, axis):
    return lax.ppermute(value, axis, [(0, 1), (1, 0)])


def fetch_weights(weights):
    taps = weights.shape[0] * weights.shape[1]
    out_block, in_block = weights.shape[2], weights.shape[3]
    flat = weights.reshape(taps, out_block, in_block)
    share_y = lax.axis_size("groups") == 2
    n_y = 2 if share_y else 1
    n_c = lax.axis_size("col")
    y_id = lax.axis_index("groups") if share_y else 0
    c_id = lax.axis_index("col")
    piece = out_block // (n_y * n_c)
    own = y_id * n_c + c_id
    mine = lax.dynamic_slice_in_dim(flat, own * piece, piece, axis=1)
    got = lax.all_gather(mine, "patch", axis=0, tiled=False)
    slots, ids = [got], [own]
    if share_y:
        slots.append(swap(got, "groups"))
        ids.append((1 - y_id) * n_c + c_id)
    if n_c == 2:
        for i in range(len(slots)):
            slots.append(swap(slots[i], "col"))
            ids.append(ids[i] - c_id + (1 - c_id))
    return slots, ids


def conv_slots(padded, slots):
    in_chans, height_pad, width_pad = padded.shape
    height = height_pad - 2
    width = width_pad - 2
    windows = [
        [padded[:, a : a + height, b : b + width] for b in range(3)] for a in range(3)
    ]
    outs = []
    for got in slots:
        total = None
        for a in range(3):
            for b in range(3):
                term = jnp.einsum(
                    "poc,chw->pohw",
                    got[:, a * 3 + b],
                    windows[a][b],
                    preferred_element_type=jnp.float32,
                )
                total = term if total is None else total + term
        outs.append(total.astype(jnp.bfloat16))
    return jnp.stack(outs)


def reduce_chan(parts, ids):
    n_slots, blocks, piece, height, width = parts.shape
    n_k = lax.axis_size("chan")
    k = lax.axis_index("chan")
    per = blocks // n_k
    if n_k == 2:
        mine = lax.dynamic_slice_in_dim(parts, k * per, per, axis=1)
        other = lax.dynamic_slice_in_dim(parts, (1 - k) * per, per, axis=1)
        total = mine.astype(jnp.float32) + swap(other, "chan").astype(jnp.float32)
    else:
        split = parts.reshape(n_slots, n_k, per, piece, height, width)
        split = jnp.moveaxis(split, 1, 0)
        got = lax.all_to_all(split, "chan", 0, 0, tiled=False)
        total = jnp.sum(got.astype(jnp.float32), axis=0)
    where = jnp.zeros((n_slots,), jnp.int32)
    for slot, ident in enumerate(ids):
        where = where.at[ident].set(slot)
    ordered = jnp.take(total, where, axis=0)
    ordered = jnp.moveaxis(ordered, 0, 1)
    return ordered.reshape(per * n_slots * piece, height, width)


def line_weights(weights, after=None):
    taps = weights.shape[0] * weights.shape[1]
    out_block, in_block = weights.shape[2], weights.shape[3]
    flat = weights.reshape(taps, out_block, in_block)
    if after is not None:
        flat, _ = lax.optimization_barrier((flat, after))
    n_p, n_c = lax.axis_size("patch"), lax.axis_size("col")
    p, c, y = lax.axis_index("patch"), lax.axis_index("col"), lax.axis_index("groups")
    half = out_block // 2
    own_half = lax.dynamic_slice_in_dim(flat, y * half, half, axis=1)
    own_other = lax.dynamic_slice_in_dim(flat, (1 - y) * half, half, axis=1)
    per_core = n_p // n_c
    needs = lambda z, cc, s: cc * per_core <= s < (cc + 1) * per_core
    bufs = {"own": own_half, "own_o": own_other}
    last = {1: own_half, -1: own_half}
    lines = []
    for t in range(1, n_p):
        for d in (1, -1):
            pairs = [((z - d) * n_c + cc, z * n_c + cc)
                     for z in range(n_p) for cc in range(n_c)
                     if 0 <= z - d < n_p and needs(z, cc, z - d * t)]
            if not pairs:
                continue
            got = lax.ppermute(last[d], ("patch", "col"), pairs)
            last[d] = got
            bufs[(t, d)] = got
            lines.append(got)
            trade = [((g * n_p + z) * n_c + cc, ((1 - g) * n_p + z) * n_c + cc)
                     for g in range(2) for z in range(n_p) for cc in range(n_c)
                     if 0 <= z - d < n_p and needs(z, cc, z - d * t)]
            bufs[(t, d, "o")] = lax.ppermute(got, ("groups", "patch", "col"), trade)
    names = sorted(bufs, key=str)
    operands = [bufs[n] for n in names]

    def branch(z, cc, g):
        def run(*ops):
            table = dict(zip(names, ops))
            pieces = []
            for r in range(per_core):
                s = cc * per_core + r
                if s == z:
                    mine, other = table["own"], table["own_o"]
                else:
                    d = 1 if s < z else -1
                    t = abs(z - s)
                    mine, other = table[(t, d)], table[(t, d, "o")]
                pieces += [mine, other] if g == 0 else [other, mine]
            return jnp.concatenate(pieces, axis=1)
        return run

    cases = [branch(z, cc, g) for g in range(2) for z in range(n_p) for cc in range(n_c)]
    index = (y * n_p + p) * n_c + c
    return lax.switch(index, cases, *operands), lines


def full_width(block):
    other = swap(block, "col")
    c = lax.axis_index("col")
    left = jnp.where(c == 0, block, other)
    right = jnp.where(c == 0, other, block)
    return jnp.pad(jnp.concatenate([left, right], axis=2), ((0, 0), (0, 0), (1, 1)))


def conv_full(padded, weight):
    kernel = weight.reshape(3, 3, weight.shape[1], weight.shape[2])
    total = lax.conv_general_dilated(
        padded[None],
        kernel,
        window_strides=(1, 1),
        padding="VALID",
        dimension_numbers=("NCHW", "HWOI", "NCHW"),
        preferred_element_type=jnp.float32,
    )[0]
    return total.astype(jnp.bfloat16)


def reduce_cores(part):
    k, c = lax.axis_index("chan"), lax.axis_index("col")
    width = part.shape[2] // 2
    piece = lambda j: lax.dynamic_slice_in_dim(part, j * width, width, axis=2)
    send_a = piece(jnp.where(k == c, 1 - c, c))
    got_a = lax.ppermute(send_a, ("chan", "col"), [(0, 1), (3, 2), (1, 3), (2, 0)])
    got_b = lax.ppermute(piece(1 - c), ("chan", "col"), [(1, 2), (2, 1)])
    first = jnp.where(k == c, piece(c), got_b)
    return first.astype(jnp.float32) + got_a.astype(jnp.float32)


def fast_path():
    return (
        lax.axis_size("chan") == 2
        and lax.axis_size("col") == 2
        and lax.axis_size("groups") == 2
        and lax.axis_size("patch") % 2 == 0
    )


def time_bias(step_index, temb_weight):
    half_width = temb_weight.shape[0] // 2
    freqs = jnp.exp(-math.log(10000.0) * jnp.arange(half_width).astype(jnp.float32) / half_width)
    angles = step_index[0].astype(jnp.float32) * freqs
    embed = jnp.concatenate([jnp.cos(angles), jnp.sin(angles)])
    gated = jax.nn.silu(embed).astype(jnp.bfloat16)
    return jnp.dot(gated[None, :], temb_weight, preferred_element_type=jnp.float32)[0]


def on_device(
    features,
    cache_codes,
    cache_scale,
    step_index,
    gn1_gain,
    gn1_shift,
    conv1_weight,
    conv1_bias,
    temb_weight,
    gn2_gain,
    gn2_shift,
    conv2_weight,
    conv2_bias,
):
    channels, rows_here, cols_here = features.shape
    patches = lax.axis_size("patch")
    group_count = GROUPS // lax.axis_size("chan")
    cell_total = channels // group_count * rows_here * patches * cols_here * lax.axis_size("col")
    fast = fast_path()
    feat32 = features.astype(jnp.float32)
    mean_one, inv_one = group_moments(feat32, group_count, cell_total)
    if fast:
        weight_one, lines_one = line_weights(conv1_weight)
        weight_two, _ = line_weights(conv2_weight, after=lines_one)
    else:
        slots_one, ids_one = fetch_weights(conv1_weight)
        slots_two, ids_two = fetch_weights(conv2_weight)
    own_act = activate(feat32, mean_one, inv_one, gn1_gain, gn1_shift)
    stale = cache_codes.astype(jnp.float32) * cache_scale[None, :, :]
    rim_act = activate(stale, mean_one, inv_one, gn1_gain, gn1_shift)
    where_patch = lax.axis_index("patch")
    upper_rim = rim_act[:, 0:1, :] * (where_patch > 0).astype(jnp.float32)
    lower_rim = rim_act[:, 1:2, :] * (where_patch < patches - 1).astype(jnp.float32)
    block_one = jnp.concatenate([upper_rim, own_act, lower_rim], axis=1).astype(jnp.bfloat16)
    if fast:
        sum_one = reduce_cores(conv_full(full_width(block_one), weight_one))
    else:
        padded_one = extended(block_one, (("col", 2),), 1)
        sum_one = reduce_chan(conv_slots(padded_one, slots_one), ids_one)
    temb_bias = time_bias(step_index, temb_weight)
    hidden = (sum_one + conv1_bias[:, None, None] + temb_bias[:, None, None]).astype(jnp.bfloat16)
    hidden32 = hidden.astype(jnp.float32)
    mean_two, inv_two = group_moments(hidden32, group_count, cell_total)
    act_two = activate(hidden32, mean_two, inv_two, gn2_gain, gn2_shift).astype(jnp.bfloat16)
    if fast:
        rows_two = extended(act_two, (("patch", 1),), 1)
        sum_two = reduce_cores(conv_full(full_width(rows_two), weight_two))
    else:
        padded_two = extended(act_two, (("patch", 1), ("col", 2)), 1)
        sum_two = reduce_chan(conv_slots(padded_two, slots_two), ids_two)
    return (sum_two + conv2_bias[:, None, None] + feat32).astype(jnp.bfloat16)


def solution(mesh):
    return jax.shard_map(
        on_device,
        mesh=mesh,
        in_specs=(
            P("chan", ("groups", "patch"), "col"),
            P("chan", ("groups", "patch"), "col"),
            P(("groups", "patch"), "col"),
            P("groups"),
            P("chan"),
            P("chan"),
            P(None, None, "patch", "chan"),
            P("chan"),
            P(None, "chan"),
            P("chan"),
            P("chan"),
            P(None, None, "patch", "chan"),
            P("chan"),
        ),
        out_specs=P("chan", ("groups", "patch"), "col"),
        check_vma=False,
    )
```

```python
import math

import jax
import jax.numpy as jnp
from jax import lax
from jax.sharding import PartitionSpec as P

GROUPS = 32


norm_epsilon = 1e-05


def extended(value, sides, width):
    for axis, dim in sides:
        count, length = (lax.axis_size(axis), value.shape[dim])
        up = [(i, (i + 1) % count) for i in range(count - 1)]
        down = [(j, i) for i, j in up]
        last = lax.slice_in_dim(value, length - width, length, axis=dim)
        leading = lax.slice_in_dim(value, 0, width, axis=dim)
        before = lax.ppermute(last, axis, up)
        after = lax.ppermute(leading, axis, down)
        value = jnp.concatenate([before, value, after], axis=dim)
    return value


def group_moments(values, group_count, cell_total):
    grouped = values.reshape(group_count, -1)
    local_sums = (jnp.sum(grouped, axis=1), jnp.sum(grouped * grouped, axis=1))
    summed = jnp.stack(local_sums)
    if lax.axis_size("col") == 2:
        summed = summed + swap(summed, "col")
    else:
        summed = lax.psum(summed, "col")
    n_p = lax.axis_size("patch")
    if n_p & (n_p - 1) == 0:
        step = 1
        while step < n_p:
            summed = summed + lax.ppermute(summed, "patch", [(i, i ^ step) for i in range(n_p)])
            step *= 2
    else:
        summed = lax.psum(summed, "patch")
    totals = (summed[0], summed[1])
    group_mean = totals[0] / cell_total
    group_var = totals[1] / cell_total - group_mean * group_mean
    return (group_mean, lax.rsqrt(group_var + norm_epsilon))


def activate(values, group_mean, inv_std, gain_vec, shift_vec):
    channels = values.shape[0]
    width = channels // group_mean.shape[0]
    shape_tail = (channels,) + (1,) * (values.ndim - 1)
    mean_chan = jnp.repeat(group_mean, width).reshape(shape_tail)
    inv_chan = jnp.repeat(inv_std, width).reshape(shape_tail)
    normed = (values - mean_chan) * inv_chan * gain_vec.reshape(shape_tail) + shift_vec.reshape(
        shape_tail
    )
    return jax.nn.silu(normed)


def swap(value, axis):
    return lax.ppermute(value, axis, [(0, 1), (1, 0)])


def fetch_weights(weights):
    taps = weights.shape[0] * weights.shape[1]
    out_block, in_block = weights.shape[2], weights.shape[3]
    flat = weights.reshape(taps, out_block, in_block)
    share_y = lax.axis_size("groups") == 2
    n_y = 2 if share_y else 1
    n_c = lax.axis_size("col")
    y_id = lax.axis_index("groups") if share_y else 0
    c_id = lax.axis_index("col")
    piece = out_block // (n_y * n_c)
    own = y_id * n_c + c_id
    mine = lax.dynamic_slice_in_dim(flat, own * piece, piece, axis=1)
    got = lax.all_gather(mine, "patch", axis=0, tiled=False)
    slots, ids = [got], [own]
    if share_y:
        slots.append(swap(got, "groups"))
        ids.append((1 - y_id) * n_c + c_id)
    if n_c == 2:
        for i in range(len(slots)):
            slots.append(swap(slots[i], "col"))
            ids.append(ids[i] - c_id + (1 - c_id))
    return slots, ids


def conv_slots(padded, slots):
    in_chans, height_pad, width_pad = padded.shape
    height = height_pad - 2
    width = width_pad - 2
    windows = [
        [padded[:, a : a + height, b : b + width] for b in range(3)] for a in range(3)
    ]
    outs = []
    for got in slots:
        total = None
        for a in range(3):
            for b in range(3):
                term = jnp.einsum(
                    "poc,chw->pohw",
                    got[:, a * 3 + b],
                    windows[a][b],
                    preferred_element_type=jnp.float32,
                )
                total = term if total is None else total + term
        outs.append(total.astype(jnp.bfloat16))
    return jnp.stack(outs)


def reduce_chan(parts, ids):
    n_slots, blocks, piece, height, width = parts.shape
    n_k = lax.axis_size("chan")
    k = lax.axis_index("chan")
    per = blocks // n_k
    if n_k == 2:
        mine = lax.dynamic_slice_in_dim(parts, k * per, per, axis=1)
        other = lax.dynamic_slice_in_dim(parts, (1 - k) * per, per, axis=1)
        total = mine.astype(jnp.float32) + swap(other, "chan").astype(jnp.float32)
    else:
        split = parts.reshape(n_slots, n_k, per, piece, height, width)
        split = jnp.moveaxis(split, 1, 0)
        got = lax.all_to_all(split, "chan", 0, 0, tiled=False)
        total = jnp.sum(got.astype(jnp.float32), axis=0)
    where = jnp.zeros((n_slots,), jnp.int32)
    for slot, ident in enumerate(ids):
        where = where.at[ident].set(slot)
    ordered = jnp.take(total, where, axis=0)
    ordered = jnp.moveaxis(ordered, 0, 1)
    return ordered.reshape(per * n_slots * piece, height, width)


def line_weights(weights, after=None):
    taps = weights.shape[0] * weights.shape[1]
    out_block, in_block = weights.shape[2], weights.shape[3]
    flat = weights.reshape(taps, out_block, in_block)
    if after is not None:
        flat, _ = lax.optimization_barrier((flat, after))
    n_p, n_c = lax.axis_size("patch"), lax.axis_size("col")
    p, c, y = lax.axis_index("patch"), lax.axis_index("col"), lax.axis_index("groups")
    half = out_block // 2
    own_half = lax.dynamic_slice_in_dim(flat, y * half, half, axis=1)
    own_other = lax.dynamic_slice_in_dim(flat, (1 - y) * half, half, axis=1)
    per_core = n_p // n_c
    needs = lambda z, cc, s: cc * per_core <= s < (cc + 1) * per_core
    bufs = {"own": own_half, "own_o": own_other}
    lines = []
    for t in range(1, n_p):
        for d in (1, -1):
            pairs = [(s * n_c + cc, (s + d * t) * n_c + cc)
                     for cc in range(n_c) for s in range(cc * per_core, (cc + 1) * per_core)
                     if 0 <= s + d * t < n_p]
            if not pairs:
                continue
            got = lax.ppermute(own_half, ("patch", "col"), pairs)
            bufs[(t, d)] = got
            lines.append(got)
            trade = [((g * n_p + z) * n_c + cc, ((1 - g) * n_p + z) * n_c + cc)
                     for g in range(2) for z in range(n_p) for cc in range(n_c)
                     if 0 <= z - d * t < n_p and needs(z, cc, z - d * t)]
            bufs[(t, d, "o")] = lax.ppermute(got, ("groups", "patch", "col"), trade)
    names = sorted(bufs, key=str)
    operands = [bufs[n] for n in names]

    def branch(z, cc, g):
        def run(*ops):
            table = dict(zip(names, ops))
            pieces = []
            for r in range(per_core):
                s = cc * per_core + r
                if s == z:
                    mine, other = table["own"], table["own_o"]
                else:
                    d = 1 if s < z else -1
                    t = abs(z - s)
                    mine, other = table[(t, d)], table[(t, d, "o")]
                pieces += [mine, other] if g == 0 else [other, mine]
            return jnp.concatenate(pieces, axis=1)
        return run

    cases = [branch(z, cc, g) for g in range(2) for z in range(n_p) for cc in range(n_c)]
    index = (y * n_p + p) * n_c + c
    return lax.switch(index, cases, *operands), lines


def full_width(block):
    other = swap(block, "col")
    c = lax.axis_index("col")
    left = jnp.where(c == 0, block, other)
    right = jnp.where(c == 0, other, block)
    return jnp.pad(jnp.concatenate([left, right], axis=2), ((0, 0), (0, 0), (1, 1)))


def conv_full(padded, weight):
    kernel = weight.reshape(3, 3, weight.shape[1], weight.shape[2])
    total = lax.conv_general_dilated(
        padded[None],
        kernel,
        window_strides=(1, 1),
        padding="VALID",
        dimension_numbers=("NCHW", "HWOI", "NCHW"),
        preferred_element_type=jnp.float32,
    )[0]
    return total.astype(jnp.bfloat16)


def reduce_cores(part):
    k, c = lax.axis_index("chan"), lax.axis_index("col")
    width = part.shape[2] // 2
    piece = lambda j: lax.dynamic_slice_in_dim(part, j * width, width, axis=2)
    send_a = piece(jnp.where(k == c, 1 - c, c))
    got_a = lax.ppermute(send_a, ("chan", "col"), [(0, 1), (3, 2), (1, 3), (2, 0)])
    got_b = lax.ppermute(piece(1 - c), ("chan", "col"), [(1, 2), (2, 1)])
    first = jnp.where(k == c, piece(c), got_b)
    return first.astype(jnp.float32) + got_a.astype(jnp.float32)


def fast_path():
    return (
        lax.axis_size("chan") == 2
        and lax.axis_size("col") == 2
        and lax.axis_size("groups") == 2
        and lax.axis_size("patch") % 2 == 0
    )


def time_bias(step_index, temb_weight):
    half_width = temb_weight.shape[0] // 2
    freqs = jnp.exp(-math.log(10000.0) * jnp.arange(half_width).astype(jnp.float32) / half_width)
    angles = step_index[0].astype(jnp.float32) * freqs
    embed = jnp.concatenate([jnp.cos(angles), jnp.sin(angles)])
    gated = jax.nn.silu(embed).astype(jnp.bfloat16)
    return jnp.dot(gated[None, :], temb_weight, preferred_element_type=jnp.float32)[0]


def on_device(
    features,
    cache_codes,
    cache_scale,
    step_index,
    gn1_gain,
    gn1_shift,
    conv1_weight,
    conv1_bias,
    temb_weight,
    gn2_gain,
    gn2_shift,
    conv2_weight,
    conv2_bias,
):
    channels, rows_here, cols_here = features.shape
    patches = lax.axis_size("patch")
    group_count = GROUPS // lax.axis_size("chan")
    cell_total = channels // group_count * rows_here * patches * cols_here * lax.axis_size("col")
    fast = fast_path()
    feat32 = features.astype(jnp.float32)
    mean_one, inv_one = group_moments(feat32, group_count, cell_total)
    if fast:
        weight_one, lines_one = line_weights(conv1_weight)
        weight_two, _ = line_weights(conv2_weight, after=lines_one)
    else:
        slots_one, ids_one = fetch_weights(conv1_weight)
        slots_two, ids_two = fetch_weights(conv2_weight)
    own_act = activate(feat32, mean_one, inv_one, gn1_gain, gn1_shift)
    stale = cache_codes.astype(jnp.float32) * cache_scale[None, :, :]
    rim_act = activate(stale, mean_one, inv_one, gn1_gain, gn1_shift)
    where_patch = lax.axis_index("patch")
    upper_rim = rim_act[:, 0:1, :] * (where_patch > 0).astype(jnp.float32)
    lower_rim = rim_act[:, 1:2, :] * (where_patch < patches - 1).astype(jnp.float32)
    block_one = jnp.concatenate([upper_rim, own_act, lower_rim], axis=1).astype(jnp.bfloat16)
    if fast:
        sum_one = reduce_cores(conv_full(full_width(block_one), weight_one))
    else:
        padded_one = extended(block_one, (("col", 2),), 1)
        sum_one = reduce_chan(conv_slots(padded_one, slots_one), ids_one)
    temb_bias = time_bias(step_index, temb_weight)
    hidden = (sum_one + conv1_bias[:, None, None] + temb_bias[:, None, None]).astype(jnp.bfloat16)
    hidden32 = hidden.astype(jnp.float32)
    mean_two, inv_two = group_moments(hidden32, group_count, cell_total)
    act_two = activate(hidden32, mean_two, inv_two, gn2_gain, gn2_shift).astype(jnp.bfloat16)
    if fast:
        rows_two = extended(act_two, (("patch", 1),), 1)
        sum_two = reduce_cores(conv_full(full_width(rows_two), weight_two))
    else:
        padded_two = extended(act_two, (("patch", 1), ("col", 2)), 1)
        sum_two = reduce_chan(conv_slots(padded_two, slots_two), ids_two)
    return (sum_two + conv2_bias[:, None, None] + feat32).astype(jnp.bfloat16)


def solution(mesh):
    return jax.shard_map(
        on_device,
        mesh=mesh,
        in_specs=(
            P("chan", ("groups", "patch"), "col"),
            P("chan", ("groups", "patch"), "col"),
            P(("groups", "patch"), "col"),
            P("groups"),
            P("chan"),
            P("chan"),
            P(None, None, "patch", "chan"),
            P("chan"),
            P(None, "chan"),
            P("chan"),
            P("chan"),
            P(None, None, "patch", "chan"),
            P("chan"),
        ),
        out_specs=P("chan", ("groups", "patch"), "col"),
        check_vma=False,
    )
```

```python
import math

import jax
import jax.numpy as jnp
from jax import lax
from jax.sharding import PartitionSpec as P

GROUPS = 32


norm_epsilon = 1e-05


def extended(value, sides, width):
    for axis, dim in sides:
        count, length = (lax.axis_size(axis), value.shape[dim])
        up = [(i, (i + 1) % count) for i in range(count - 1)]
        down = [(j, i) for i, j in up]
        last = lax.slice_in_dim(value, length - width, length, axis=dim)
        leading = lax.slice_in_dim(value, 0, width, axis=dim)
        before = lax.ppermute(last, axis, up)
        after = lax.ppermute(leading, axis, down)
        value = jnp.concatenate([before, value, after], axis=dim)
    return value


def group_moments(values, group_count, cell_total):
    grouped = values.reshape(group_count, -1)
    local_sums = (jnp.sum(grouped, axis=1), jnp.sum(grouped * grouped, axis=1))
    summed = jnp.stack(local_sums)
    if lax.axis_size("col") == 2:
        summed = summed + swap(summed, "col")
    else:
        summed = lax.psum(summed, "col")
    n_p = lax.axis_size("patch")
    if n_p & (n_p - 1) == 0:
        step = 1
        while step < n_p:
            summed = summed + lax.ppermute(summed, "patch", [(i, i ^ step) for i in range(n_p)])
            step *= 2
    else:
        summed = lax.psum(summed, "patch")
    totals = (summed[0], summed[1])
    group_mean = totals[0] / cell_total
    group_var = totals[1] / cell_total - group_mean * group_mean
    return (group_mean, lax.rsqrt(group_var + norm_epsilon))


def activate(values, group_mean, inv_std, gain_vec, shift_vec):
    channels = values.shape[0]
    width = channels // group_mean.shape[0]
    shape_tail = (channels,) + (1,) * (values.ndim - 1)
    mean_chan = jnp.repeat(group_mean, width).reshape(shape_tail)
    inv_chan = jnp.repeat(inv_std, width).reshape(shape_tail)
    normed = (values - mean_chan) * inv_chan * gain_vec.reshape(shape_tail) + shift_vec.reshape(
        shape_tail
    )
    return jax.nn.silu(normed)


def swap(value, axis):
    return lax.ppermute(value, axis, [(0, 1), (1, 0)])


def fetch_weights(weights):
    taps = weights.shape[0] * weights.shape[1]
    out_block, in_block = weights.shape[2], weights.shape[3]
    flat = weights.reshape(taps, out_block, in_block)
    share_y = lax.axis_size("groups") == 2
    n_y = 2 if share_y else 1
    n_c = lax.axis_size("col")
    y_id = lax.axis_index("groups") if share_y else 0
    c_id = lax.axis_index("col")
    piece = out_block // (n_y * n_c)
    own = y_id * n_c + c_id
    mine = lax.dynamic_slice_in_dim(flat, own * piece, piece, axis=1)
    got = lax.all_gather(mine, "patch", axis=0, tiled=False)
    slots, ids = [got], [own]
    if share_y:
        slots.append(swap(got, "groups"))
        ids.append((1 - y_id) * n_c + c_id)
    if n_c == 2:
        for i in range(len(slots)):
            slots.append(swap(slots[i], "col"))
            ids.append(ids[i] - c_id + (1 - c_id))
    return slots, ids


def conv_slots(padded, slots):
    in_chans, height_pad, width_pad = padded.shape
    height = height_pad - 2
    width = width_pad - 2
    windows = [
        [padded[:, a : a + height, b : b + width] for b in range(3)] for a in range(3)
    ]
    outs = []
    for got in slots:
        total = None
        for a in range(3):
            for b in range(3):
                term = jnp.einsum(
                    "poc,chw->pohw",
                    got[:, a * 3 + b],
                    windows[a][b],
                    preferred_element_type=jnp.float32,
                )
                total = term if total is None else total + term
        outs.append(total.astype(jnp.bfloat16))
    return jnp.stack(outs)


def reduce_chan(parts, ids):
    n_slots, blocks, piece, height, width = parts.shape
    n_k = lax.axis_size("chan")
    k = lax.axis_index("chan")
    per = blocks // n_k
    if n_k == 2:
        mine = lax.dynamic_slice_in_dim(parts, k * per, per, axis=1)
        other = lax.dynamic_slice_in_dim(parts, (1 - k) * per, per, axis=1)
        total = mine.astype(jnp.float32) + swap(other, "chan").astype(jnp.float32)
    else:
        split = parts.reshape(n_slots, n_k, per, piece, height, width)
        split = jnp.moveaxis(split, 1, 0)
        got = lax.all_to_all(split, "chan", 0, 0, tiled=False)
        total = jnp.sum(got.astype(jnp.float32), axis=0)
    where = jnp.zeros((n_slots,), jnp.int32)
    for slot, ident in enumerate(ids):
        where = where.at[ident].set(slot)
    ordered = jnp.take(total, where, axis=0)
    ordered = jnp.moveaxis(ordered, 0, 1)
    return ordered.reshape(per * n_slots * piece, height, width)


def line_weights(weights, after=None):
    taps = weights.shape[0] * weights.shape[1]
    out_block, in_block = weights.shape[2], weights.shape[3]
    flat = weights.reshape(taps, out_block, in_block)
    if after is not None:
        flat, _ = lax.optimization_barrier((flat, after))
    n_p, n_c = lax.axis_size("patch"), lax.axis_size("col")
    p, c, y = lax.axis_index("patch"), lax.axis_index("col"), lax.axis_index("groups")
    half = out_block // 2
    own_half = lax.dynamic_slice_in_dim(flat, y * half, half, axis=1)
    own_other = lax.dynamic_slice_in_dim(flat, (1 - y) * half, half, axis=1)
    per_core = n_p // n_c
    needs = lambda z, cc, s: cc * per_core <= s < (cc + 1) * per_core
    bufs = {"own": own_half, "own_o": own_other}
    last = {1: own_half, -1: own_half}
    lines = []
    for t in range(1, n_p):
        step_got = []
        for d in (1, -1):
            pairs = [((z - d) * n_c + cc, z * n_c + cc)
                     for z in range(n_p) for cc in range(n_c)
                     if 0 <= z - d < n_p and needs(z, cc, z - d * t)]
            if not pairs:
                continue
            got = lax.ppermute(last[d], ("patch", "col"), pairs)
            last[d] = got
            bufs[(t, d)] = got
            lines.append(got)
            step_got.append(got)
            trade = [((g * n_p + z) * n_c + cc, ((1 - g) * n_p + z) * n_c + cc)
                     for g in range(2) for z in range(n_p) for cc in range(n_c)
                     if 0 <= z - d < n_p and needs(z, cc, z - d * t)]
            bufs[(t, d, "o")] = lax.ppermute(got, ("groups", "patch", "col"), trade)
        if step_got:
            yield step_got
    names = sorted(bufs, key=str)
    operands = [bufs[n] for n in names]

    def branch(z, cc, g):
        def run(*ops):
            table = dict(zip(names, ops))
            pieces = []
            for r in range(per_core):
                s = cc * per_core + r
                if s == z:
                    mine, other = table["own"], table["own_o"]
                else:
                    d = 1 if s < z else -1
                    t = abs(z - s)
                    mine, other = table[(t, d)], table[(t, d, "o")]
                pieces += [mine, other] if g == 0 else [other, mine]
            return jnp.concatenate(pieces, axis=1)
        return run

    cases = [branch(z, cc, g) for g in range(2) for z in range(n_p) for cc in range(n_c)]
    index = (y * n_p + p) * n_c + c
    yield lax.switch(index, cases, *operands), lines


def tie(steps, value):
    got = next(steps)
    if isinstance(got, tuple):
        return got, value
    _, value = lax.optimization_barrier((tuple(got), value))
    return None, value


def finish(steps):
    for got in steps:
        if isinstance(got, tuple):
            return got


def full_width(block):
    other = swap(block, "col")
    c = lax.axis_index("col")
    left = jnp.where(c == 0, block, other)
    right = jnp.where(c == 0, other, block)
    return jnp.pad(jnp.concatenate([left, right], axis=2), ((0, 0), (0, 0), (1, 1)))


def conv_full(padded, weight):
    kernel = weight.reshape(3, 3, weight.shape[1], weight.shape[2])
    total = lax.conv_general_dilated(
        padded[None],
        kernel,
        window_strides=(1, 1),
        padding="VALID",
        dimension_numbers=("NCHW", "HWOI", "NCHW"),
        preferred_element_type=jnp.float32,
    )[0]
    return total.astype(jnp.bfloat16)


def reduce_cores(part):
    k, c = lax.axis_index("chan"), lax.axis_index("col")
    width = part.shape[2] // 2
    piece = lambda j: lax.dynamic_slice_in_dim(part, j * width, width, axis=2)
    send_a = piece(jnp.where(k == c, 1 - c, c))
    got_a = lax.ppermute(send_a, ("chan", "col"), [(0, 1), (3, 2), (1, 3), (2, 0)])
    got_b = lax.ppermute(piece(1 - c), ("chan", "col"), [(1, 2), (2, 1)])
    first = jnp.where(k == c, piece(c), got_b)
    return first.astype(jnp.float32) + got_a.astype(jnp.float32)


def fast_path():
    return (
        lax.axis_size("chan") == 2
        and lax.axis_size("col") == 2
        and lax.axis_size("groups") == 2
        and lax.axis_size("patch") % 2 == 0
    )


def time_bias(step_index, temb_weight):
    half_width = temb_weight.shape[0] // 2
    freqs = jnp.exp(-math.log(10000.0) * jnp.arange(half_width).astype(jnp.float32) / half_width)
    angles = step_index[0].astype(jnp.float32) * freqs
    embed = jnp.concatenate([jnp.cos(angles), jnp.sin(angles)])
    gated = jax.nn.silu(embed).astype(jnp.bfloat16)
    return jnp.dot(gated[None, :], temb_weight, preferred_element_type=jnp.float32)[0]


def on_device(
    features,
    cache_codes,
    cache_scale,
    step_index,
    gn1_gain,
    gn1_shift,
    conv1_weight,
    conv1_bias,
    temb_weight,
    gn2_gain,
    gn2_shift,
    conv2_weight,
    conv2_bias,
):
    channels, rows_here, cols_here = features.shape
    patches = lax.axis_size("patch")
    group_count = GROUPS // lax.axis_size("chan")
    cell_total = channels // group_count * rows_here * patches * cols_here * lax.axis_size("col")
    fast = fast_path()
    feat32 = features.astype(jnp.float32)
    if not fast:
        return slow_path(features, cache_codes, cache_scale, step_index, gn1_gain, gn1_shift,
                         conv1_weight, conv1_bias, temb_weight, gn2_gain, gn2_shift,
                         conv2_weight, conv2_bias)
    steps_one = line_weights(conv1_weight)
    _, feat32 = tie(steps_one, feat32)
    mean_one, inv_one = group_moments(feat32, group_count, cell_total)
    _, (mean_one, inv_one) = tie(steps_one, (mean_one, inv_one))
    own_act = activate(feat32, mean_one, inv_one, gn1_gain, gn1_shift)
    stale = cache_codes.astype(jnp.float32) * cache_scale[None, :, :]
    rim_act = activate(stale, mean_one, inv_one, gn1_gain, gn1_shift)
    where_patch = lax.axis_index("patch")
    upper_rim = rim_act[:, 0:1, :] * (where_patch > 0).astype(jnp.float32)
    lower_rim = rim_act[:, 1:2, :] * (where_patch < patches - 1).astype(jnp.float32)
    block_one = jnp.concatenate([upper_rim, own_act, lower_rim], axis=1).astype(jnp.bfloat16)
    _, block_one = tie(steps_one, block_one)
    weight_one, lines_one = finish(steps_one)
    steps_two = line_weights(conv2_weight, after=lines_one)
    part_one = conv_full(full_width(block_one), weight_one)
    _, part_one = tie(steps_two, part_one)
    sum_one = reduce_cores(part_one)
    _, sum_one = tie(steps_two, sum_one)
    temb_bias = time_bias(step_index, temb_weight)
    hidden = (sum_one + conv1_bias[:, None, None] + temb_bias[:, None, None]).astype(jnp.bfloat16)
    hidden32 = hidden.astype(jnp.float32)
    mean_two, inv_two = group_moments(hidden32, group_count, cell_total)
    _, (mean_two, inv_two) = tie(steps_two, (mean_two, inv_two))
    weight_two, _ = finish(steps_two)
    act_two = activate(hidden32, mean_two, inv_two, gn2_gain, gn2_shift).astype(jnp.bfloat16)
    rows_two = extended(act_two, (("patch", 1),), 1)
    sum_two = reduce_cores(conv_full(full_width(rows_two), weight_two))
    return (sum_two + conv2_bias[:, None, None] + feat32).astype(jnp.bfloat16)


def slow_path(
    features,
    cache_codes,
    cache_scale,
    step_index,
    gn1_gain,
    gn1_shift,
    conv1_weight,
    conv1_bias,
    temb_weight,
    gn2_gain,
    gn2_shift,
    conv2_weight,
    conv2_bias,
):
    channels, rows_here, cols_here = features.shape
    patches = lax.axis_size("patch")
    group_count = GROUPS // lax.axis_size("chan")
    cell_total = channels // group_count * rows_here * patches * cols_here * lax.axis_size("col")
    feat32 = features.astype(jnp.float32)
    mean_one, inv_one = group_moments(feat32, group_count, cell_total)
    slots_one, ids_one = fetch_weights(conv1_weight)
    slots_two, ids_two = fetch_weights(conv2_weight)
    own_act = activate(feat32, mean_one, inv_one, gn1_gain, gn1_shift)
    stale = cache_codes.astype(jnp.float32) * cache_scale[None, :, :]
    rim_act = activate(stale, mean_one, inv_one, gn1_gain, gn1_shift)
    where_patch = lax.axis_index("patch")
    upper_rim = rim_act[:, 0:1, :] * (where_patch > 0).astype(jnp.float32)
    lower_rim = rim_act[:, 1:2, :] * (where_patch < patches - 1).astype(jnp.float32)
    block_one = jnp.concatenate([upper_rim, own_act, lower_rim], axis=1).astype(jnp.bfloat16)
    padded_one = extended(block_one, (("col", 2),), 1)
    sum_one = reduce_chan(conv_slots(padded_one, slots_one), ids_one)
    temb_bias = time_bias(step_index, temb_weight)
    hidden = (sum_one + conv1_bias[:, None, None] + temb_bias[:, None, None]).astype(jnp.bfloat16)
    hidden32 = hidden.astype(jnp.float32)
    mean_two, inv_two = group_moments(hidden32, group_count, cell_total)
    act_two = activate(hidden32, mean_two, inv_two, gn2_gain, gn2_shift).astype(jnp.bfloat16)
    padded_two = extended(act_two, (("patch", 1), ("col", 2)), 1)
    sum_two = reduce_chan(conv_slots(padded_two, slots_two), ids_two)
    return (sum_two + conv2_bias[:, None, None] + feat32).astype(jnp.bfloat16)


def solution(mesh):
    return jax.shard_map(
        on_device,
        mesh=mesh,
        in_specs=(
            P("chan", ("groups", "patch"), "col"),
            P("chan", ("groups", "patch"), "col"),
            P(("groups", "patch"), "col"),
            P("groups"),
            P("chan"),
            P("chan"),
            P(None, None, "patch", "chan"),
            P("chan"),
            P(None, "chan"),
            P("chan"),
            P("chan"),
            P(None, None, "patch", "chan"),
            P("chan"),
        ),
        out_specs=P("chan", ("groups", "patch"), "col"),
        check_vma=False,
    )
```

```python
import math

import jax
import jax.numpy as jnp
from jax import lax
from jax.sharding import PartitionSpec as P

GROUPS = 32


norm_epsilon = 1e-05


def extended(value, sides, width):
    for axis, dim in sides:
        count, length = (lax.axis_size(axis), value.shape[dim])
        up = [(i, (i + 1) % count) for i in range(count - 1)]
        down = [(j, i) for i, j in up]
        last = lax.slice_in_dim(value, length - width, length, axis=dim)
        leading = lax.slice_in_dim(value, 0, width, axis=dim)
        before = lax.ppermute(last, axis, up)
        after = lax.ppermute(leading, axis, down)
        value = jnp.concatenate([before, value, after], axis=dim)
    return value


def group_moments(values, group_count, cell_total):
    grouped = values.reshape(group_count, -1)
    local_sums = (jnp.sum(grouped, axis=1), jnp.sum(grouped * grouped, axis=1))
    summed = jnp.stack(local_sums)
    if lax.axis_size("col") == 2:
        summed = summed + swap(summed, "col")
    else:
        summed = lax.psum(summed, "col")
    n_p = lax.axis_size("patch")
    if n_p & (n_p - 1) == 0:
        step = 1
        while step < n_p:
            summed = summed + lax.ppermute(summed, "patch", [(i, i ^ step) for i in range(n_p)])
            step *= 2
    else:
        summed = lax.psum(summed, "patch")
    totals = (summed[0], summed[1])
    group_mean = totals[0] / cell_total
    group_var = totals[1] / cell_total - group_mean * group_mean
    return (group_mean, lax.rsqrt(group_var + norm_epsilon))


def activate(values, group_mean, inv_std, gain_vec, shift_vec):
    channels = values.shape[0]
    width = channels // group_mean.shape[0]
    shape_tail = (channels,) + (1,) * (values.ndim - 1)
    mean_chan = jnp.repeat(group_mean, width).reshape(shape_tail)
    inv_chan = jnp.repeat(inv_std, width).reshape(shape_tail)
    normed = (values - mean_chan) * inv_chan * gain_vec.reshape(shape_tail) + shift_vec.reshape(
        shape_tail
    )
    return jax.nn.silu(normed)


def swap(value, axis):
    return lax.ppermute(value, axis, [(0, 1), (1, 0)])


def fetch_weights(weights):
    taps = weights.shape[0] * weights.shape[1]
    out_block, in_block = weights.shape[2], weights.shape[3]
    flat = weights.reshape(taps, out_block, in_block)
    share_y = lax.axis_size("groups") == 2
    n_y = 2 if share_y else 1
    n_c = lax.axis_size("col")
    y_id = lax.axis_index("groups") if share_y else 0
    c_id = lax.axis_index("col")
    piece = out_block // (n_y * n_c)
    own = y_id * n_c + c_id
    mine = lax.dynamic_slice_in_dim(flat, own * piece, piece, axis=1)
    got = lax.all_gather(mine, "patch", axis=0, tiled=False)
    slots, ids = [got], [own]
    if share_y:
        slots.append(swap(got, "groups"))
        ids.append((1 - y_id) * n_c + c_id)
    if n_c == 2:
        for i in range(len(slots)):
            slots.append(swap(slots[i], "col"))
            ids.append(ids[i] - c_id + (1 - c_id))
    return slots, ids


def conv_slots(padded, slots):
    in_chans, height_pad, width_pad = padded.shape
    height = height_pad - 2
    width = width_pad - 2
    windows = [
        [padded[:, a : a + height, b : b + width] for b in range(3)] for a in range(3)
    ]
    outs = []
    for got in slots:
        total = None
        for a in range(3):
            for b in range(3):
                term = jnp.einsum(
                    "poc,chw->pohw",
                    got[:, a * 3 + b],
                    windows[a][b],
                    preferred_element_type=jnp.float32,
                )
                total = term if total is None else total + term
        outs.append(total.astype(jnp.bfloat16))
    return jnp.stack(outs)


def reduce_chan(parts, ids):
    n_slots, blocks, piece, height, width = parts.shape
    n_k = lax.axis_size("chan")
    k = lax.axis_index("chan")
    per = blocks // n_k
    if n_k == 2:
        mine = lax.dynamic_slice_in_dim(parts, k * per, per, axis=1)
        other = lax.dynamic_slice_in_dim(parts, (1 - k) * per, per, axis=1)
        total = mine.astype(jnp.float32) + swap(other, "chan").astype(jnp.float32)
    else:
        split = parts.reshape(n_slots, n_k, per, piece, height, width)
        split = jnp.moveaxis(split, 1, 0)
        got = lax.all_to_all(split, "chan", 0, 0, tiled=False)
        total = jnp.sum(got.astype(jnp.float32), axis=0)
    where = jnp.zeros((n_slots,), jnp.int32)
    for slot, ident in enumerate(ids):
        where = where.at[ident].set(slot)
    ordered = jnp.take(total, where, axis=0)
    ordered = jnp.moveaxis(ordered, 0, 1)
    return ordered.reshape(per * n_slots * piece, height, width)


def line_weights(weights, after=None):
    taps = weights.shape[0] * weights.shape[1]
    out_block, in_block = weights.shape[2], weights.shape[3]
    flat = weights.reshape(taps, out_block, in_block)
    if after is not None:
        flat, _ = lax.optimization_barrier((flat, after))
    n_p, n_c = lax.axis_size("patch"), lax.axis_size("col")
    p, c, y = lax.axis_index("patch"), lax.axis_index("col"), lax.axis_index("groups")
    half = out_block // 2
    own_half = lax.dynamic_slice_in_dim(flat, y * half, half, axis=1)
    own_other = lax.dynamic_slice_in_dim(flat, (1 - y) * half, half, axis=1)
    per_core = n_p // n_c
    needs = lambda z, cc, s: cc * per_core <= s < (cc + 1) * per_core
    bufs = {"own": own_half, "own_o": own_other}
    last = {1: own_half, -1: own_half}
    lines = []
    for t in range(1, n_p):
        for d in (1, -1):
            pairs = [((z - d) * n_c + cc, z * n_c + cc)
                     for z in range(n_p) for cc in range(n_c)
                     if 0 <= z - d < n_p and needs(z, cc, z - d * t)]
            if not pairs:
                continue
            got = lax.ppermute(last[d], ("patch", "col"), pairs)
            last[d] = got
            bufs[(t, d)] = got
            lines.append(got)
            trade = [((g * n_p + z) * n_c + cc, ((1 - g) * n_p + z) * n_c + cc)
                     for g in range(2) for z in range(n_p) for cc in range(n_c)
                     if 0 <= z - d < n_p and needs(z, cc, z - d * t)]
            bufs[(t, d, "o")] = lax.ppermute(got, ("groups", "patch", "col"), trade)
    names = sorted(bufs, key=str)
    operands = [bufs[n] for n in names]

    def branch(z, cc, g):
        def run(*ops):
            table = dict(zip(names, ops))
            pieces = []
            for r in range(per_core):
                s = cc * per_core + r
                if s == z:
                    mine, other = table["own"], table["own_o"]
                else:
                    d = 1 if s < z else -1
                    t = abs(z - s)
                    mine, other = table[(t, d)], table[(t, d, "o")]
                pieces += [mine, other] if g == 0 else [other, mine]
            return jnp.concatenate(pieces, axis=1)
        return run

    cases = [branch(z, cc, g) for g in range(2) for z in range(n_p) for cc in range(n_c)]
    index = (y * n_p + p) * n_c + c
    return lax.switch(index, cases, *operands), lines


def full_width(block):
    other = swap(block, "col")
    c = lax.axis_index("col")
    left = jnp.where(c == 0, block, other)
    right = jnp.where(c == 0, other, block)
    return jnp.pad(jnp.concatenate([left, right], axis=2), ((0, 0), (0, 0), (1, 1)))


def conv_full(padded, weight):
    kernel = weight.reshape(3, 3, weight.shape[1], weight.shape[2])
    total = lax.conv_general_dilated(
        padded[None],
        kernel,
        window_strides=(1, 1),
        padding="VALID",
        dimension_numbers=("NCHW", "HWOI", "NCHW"),
        preferred_element_type=jnp.float32,
    )[0]
    return total.astype(jnp.bfloat16)


def reduce_cores(part):
    k, c = lax.axis_index("chan"), lax.axis_index("col")
    width = part.shape[2] // 2
    piece = lambda j: lax.dynamic_slice_in_dim(part, j * width, width, axis=2)
    send_a = piece(jnp.where(k == c, 1 - c, c))
    got_a = lax.ppermute(send_a, ("chan", "col"), [(0, 1), (3, 2), (1, 3), (2, 0)])
    got_b = lax.ppermute(piece(1 - c), ("chan", "col"), [(1, 2), (2, 1)])
    first = jnp.where(k == c, piece(c), got_b)
    return first.astype(jnp.float32) + got_a.astype(jnp.float32)


def group_moments_hwc(values, group_count, cell_total):
    rows, cols, channels = values.shape
    grouped = values.reshape(rows * cols, group_count, channels // group_count)
    local_sums = (jnp.sum(grouped, axis=(0, 2)), jnp.sum(grouped * grouped, axis=(0, 2)))
    summed = jnp.stack(local_sums)
    summed = summed + swap(summed, "col")
    n_p = lax.axis_size("patch")
    if n_p & (n_p - 1) == 0:
        step = 1
        while step < n_p:
            summed = summed + lax.ppermute(summed, "patch", [(i, i ^ step) for i in range(n_p)])
            step *= 2
    else:
        summed = lax.psum(summed, "patch")
    group_mean = summed[0] / cell_total
    group_var = summed[1] / cell_total - group_mean * group_mean
    return (group_mean, lax.rsqrt(group_var + norm_epsilon))


def activate_hwc(values, group_mean, inv_std, gain_vec, shift_vec):
    channels = values.shape[-1]
    width = channels // group_mean.shape[0]
    mean_chan = jnp.repeat(group_mean, width)
    inv_chan = jnp.repeat(inv_std, width)
    normed = (values - mean_chan) * inv_chan * gain_vec + shift_vec
    return jax.nn.silu(normed)


def rows_extended_hwc(value):
    count = lax.axis_size("patch")
    up = [(i, i + 1) for i in range(count - 1)]
    down = [(j, i) for i, j in up]
    before = lax.ppermute(value[-1:], "patch", up)
    after = lax.ppermute(value[:1], "patch", down)
    return jnp.concatenate([before, value, after], axis=0)


def full_width_hwc(block):
    other = swap(block, "col")
    c = lax.axis_index("col")
    left = jnp.where(c == 0, block, other)
    right = jnp.where(c == 0, other, block)
    return jnp.pad(jnp.concatenate([left, right], axis=1), ((0, 0), (1, 1), (0, 0)))


def conv_hwc(padded, weight):
    kernel = weight.reshape(3, 3, weight.shape[1], weight.shape[2])
    total = lax.conv_general_dilated(
        padded[None],
        kernel,
        window_strides=(1, 1),
        padding="VALID",
        dimension_numbers=("NHWC", "HWOI", "NHWC"),
        preferred_element_type=jnp.float32,
    )[0]
    return total.astype(jnp.bfloat16)


def reduce_cores_hwc(part):
    k, c = lax.axis_index("chan"), lax.axis_index("col")
    width = part.shape[1] // 2
    piece = lambda j: lax.dynamic_slice_in_dim(part, j * width, width, axis=1)
    send_a = piece(jnp.where(k == c, 1 - c, c))
    got_a = lax.ppermute(send_a, ("chan", "col"), [(0, 1), (3, 2), (1, 3), (2, 0)])
    got_b = lax.ppermute(piece(1 - c), ("chan", "col"), [(1, 2), (2, 1)])
    first = jnp.where(k == c, piece(c), got_b)
    return first.astype(jnp.float32) + got_a.astype(jnp.float32)


def fast_path():
    return (
        lax.axis_size("chan") == 2
        and lax.axis_size("col") == 2
        and lax.axis_size("groups") == 2
        and lax.axis_size("patch") % 2 == 0
    )


def time_bias(step_index, temb_weight):
    half_width = temb_weight.shape[0] // 2
    freqs = jnp.exp(-math.log(10000.0) * jnp.arange(half_width).astype(jnp.float32) / half_width)
    angles = step_index[0].astype(jnp.float32) * freqs
    embed = jnp.concatenate([jnp.cos(angles), jnp.sin(angles)])
    gated = jax.nn.silu(embed).astype(jnp.bfloat16)
    return jnp.dot(gated[None, :], temb_weight, preferred_element_type=jnp.float32)[0]


def on_device(
    features,
    cache_codes,
    cache_scale,
    step_index,
    gn1_gain,
    gn1_shift,
    conv1_weight,
    conv1_bias,
    temb_weight,
    gn2_gain,
    gn2_shift,
    conv2_weight,
    conv2_bias,
):
    channels, rows_here, cols_here = features.shape
    patches = lax.axis_size("patch")
    group_count = GROUPS // lax.axis_size("chan")
    cell_total = channels // group_count * rows_here * patches * cols_here * lax.axis_size("col")
    fast = fast_path()
    feat32 = features.astype(jnp.float32)
    mean_one, inv_one = group_moments(feat32, group_count, cell_total)
    if fast:
        weight_one, lines_one = line_weights(conv1_weight)
        weight_two, _ = line_weights(conv2_weight, after=lines_one)
    else:
        slots_one, ids_one = fetch_weights(conv1_weight)
        slots_two, ids_two = fetch_weights(conv2_weight)
    own_act = activate(feat32, mean_one, inv_one, gn1_gain, gn1_shift)
    stale = cache_codes.astype(jnp.float32) * cache_scale[None, :, :]
    rim_act = activate(stale, mean_one, inv_one, gn1_gain, gn1_shift)
    where_patch = lax.axis_index("patch")
    upper_rim = rim_act[:, 0:1, :] * (where_patch > 0).astype(jnp.float32)
    lower_rim = rim_act[:, 1:2, :] * (where_patch < patches - 1).astype(jnp.float32)
    block_one = jnp.concatenate([upper_rim, own_act, lower_rim], axis=1).astype(jnp.bfloat16)
    if fast:
        block_hwc = jnp.transpose(block_one, (1, 2, 0))
        sum_one = reduce_cores_hwc(conv_hwc(full_width_hwc(block_hwc), weight_one))
        temb_bias = time_bias(step_index, temb_weight)
        hidden = (sum_one + conv1_bias + temb_bias).astype(jnp.bfloat16)
        hidden32 = hidden.astype(jnp.float32)
        mean_two, inv_two = group_moments_hwc(hidden32, group_count, cell_total)
        act_two = activate_hwc(hidden32, mean_two, inv_two, gn2_gain, gn2_shift).astype(jnp.bfloat16)
        rows_two = rows_extended_hwc(act_two)
        sum_two = reduce_cores_hwc(conv_hwc(full_width_hwc(rows_two), weight_two))
        sum_two = jnp.transpose(sum_two, (2, 0, 1))
        return (sum_two + conv2_bias[:, None, None] + feat32).astype(jnp.bfloat16)
    padded_one = extended(block_one, (("col", 2),), 1)
    sum_one = reduce_chan(conv_slots(padded_one, slots_one), ids_one)
    temb_bias = time_bias(step_index, temb_weight)
    hidden = (sum_one + conv1_bias[:, None, None] + temb_bias[:, None, None]).astype(jnp.bfloat16)
    hidden32 = hidden.astype(jnp.float32)
    mean_two, inv_two = group_moments(hidden32, group_count, cell_total)
    act_two = activate(hidden32, mean_two, inv_two, gn2_gain, gn2_shift).astype(jnp.bfloat16)
    if fast:
        pass
    else:
        padded_two = extended(act_two, (("patch", 1), ("col", 2)), 1)
        sum_two = reduce_chan(conv_slots(padded_two, slots_two), ids_two)
    return (sum_two + conv2_bias[:, None, None] + feat32).astype(jnp.bfloat16)


def solution(mesh):
    return jax.shard_map(
        on_device,
        mesh=mesh,
        in_specs=(
            P("chan", ("groups", "patch"), "col"),
            P("chan", ("groups", "patch"), "col"),
            P(("groups", "patch"), "col"),
            P("groups"),
            P("chan"),
            P("chan"),
            P(None, None, "patch", "chan"),
            P("chan"),
            P(None, "chan"),
            P("chan"),
            P("chan"),
            P(None, None, "patch", "chan"),
            P("chan"),
        ),
        out_specs=P("chan", ("groups", "patch"), "col"),
        check_vma=False,
    )
```

```python
import math

import jax
import jax.numpy as jnp
from jax import lax
from jax.sharding import PartitionSpec as P

GROUPS = 32


norm_epsilon = 1e-05


def extended(value, sides, width):
    for axis, dim in sides:
        count, length = (lax.axis_size(axis), value.shape[dim])
        up = [(i, (i + 1) % count) for i in range(count - 1)]
        down = [(j, i) for i, j in up]
        last = lax.slice_in_dim(value, length - width, length, axis=dim)
        leading = lax.slice_in_dim(value, 0, width, axis=dim)
        before = lax.ppermute(last, axis, up)
        after = lax.ppermute(leading, axis, down)
        value = jnp.concatenate([before, value, after], axis=dim)
    return value


def group_moments(values, group_count, cell_total):
    grouped = values.reshape(group_count, -1)
    local_sums = (jnp.sum(grouped, axis=1), jnp.sum(grouped * grouped, axis=1))
    summed = jnp.stack(local_sums)
    if lax.axis_size("col") == 2:
        summed = summed + swap(summed, "col")
    else:
        summed = lax.psum(summed, "col")
    n_p = lax.axis_size("patch")
    if n_p & (n_p - 1) == 0:
        step = 1
        while step < n_p:
            summed = summed + lax.ppermute(summed, "patch", [(i, i ^ step) for i in range(n_p)])
            step *= 2
    else:
        summed = lax.psum(summed, "patch")
    totals = (summed[0], summed[1])
    group_mean = totals[0] / cell_total
    group_var = totals[1] / cell_total - group_mean * group_mean
    return (group_mean, lax.rsqrt(group_var + norm_epsilon))


def activate(values, group_mean, inv_std, gain_vec, shift_vec):
    channels = values.shape[0]
    width = channels // group_mean.shape[0]
    shape_tail = (channels,) + (1,) * (values.ndim - 1)
    mean_chan = jnp.repeat(group_mean, width).reshape(shape_tail)
    inv_chan = jnp.repeat(inv_std, width).reshape(shape_tail)
    normed = (values - mean_chan) * inv_chan * gain_vec.reshape(shape_tail) + shift_vec.reshape(
        shape_tail
    )
    return jax.nn.silu(normed)


def swap(value, axis):
    return lax.ppermute(value, axis, [(0, 1), (1, 0)])


def fetch_weights(weights):
    taps = weights.shape[0] * weights.shape[1]
    out_block, in_block = weights.shape[2], weights.shape[3]
    flat = weights.reshape(taps, out_block, in_block)
    share_y = lax.axis_size("groups") == 2
    n_y = 2 if share_y else 1
    n_c = lax.axis_size("col")
    y_id = lax.axis_index("groups") if share_y else 0
    c_id = lax.axis_index("col")
    piece = out_block // (n_y * n_c)
    own = y_id * n_c + c_id
    mine = lax.dynamic_slice_in_dim(flat, own * piece, piece, axis=1)
    got = lax.all_gather(mine, "patch", axis=0, tiled=False)
    slots, ids = [got], [own]
    if share_y:
        slots.append(swap(got, "groups"))
        ids.append((1 - y_id) * n_c + c_id)
    if n_c == 2:
        for i in range(len(slots)):
            slots.append(swap(slots[i], "col"))
            ids.append(ids[i] - c_id + (1 - c_id))
    return slots, ids


def conv_slots(padded, slots):
    in_chans, height_pad, width_pad = padded.shape
    height = height_pad - 2
    width = width_pad - 2
    windows = [
        [padded[:, a : a + height, b : b + width] for b in range(3)] for a in range(3)
    ]
    outs = []
    for got in slots:
        total = None
        for a in range(3):
            for b in range(3):
                term = jnp.einsum(
                    "poc,chw->pohw",
                    got[:, a * 3 + b],
                    windows[a][b],
                    preferred_element_type=jnp.float32,
                )
                total = term if total is None else total + term
        outs.append(total.astype(jnp.bfloat16))
    return jnp.stack(outs)


def reduce_chan(parts, ids):
    n_slots, blocks, piece, height, width = parts.shape
    n_k = lax.axis_size("chan")
    k = lax.axis_index("chan")
    per = blocks // n_k
    if n_k == 2:
        mine = lax.dynamic_slice_in_dim(parts, k * per, per, axis=1)
        other = lax.dynamic_slice_in_dim(parts, (1 - k) * per, per, axis=1)
        total = mine.astype(jnp.float32) + swap(other, "chan").astype(jnp.float32)
    else:
        split = parts.reshape(n_slots, n_k, per, piece, height, width)
        split = jnp.moveaxis(split, 1, 0)
        got = lax.all_to_all(split, "chan", 0, 0, tiled=False)
        total = jnp.sum(got.astype(jnp.float32), axis=0)
    where = jnp.zeros((n_slots,), jnp.int32)
    for slot, ident in enumerate(ids):
        where = where.at[ident].set(slot)
    ordered = jnp.take(total, where, axis=0)
    ordered = jnp.moveaxis(ordered, 0, 1)
    return ordered.reshape(per * n_slots * piece, height, width)


def line_weights(weights, after=None):
    taps = weights.shape[0] * weights.shape[1]
    out_block, in_block = weights.shape[2], weights.shape[3]
    flat = weights.reshape(taps, out_block, in_block)
    if after is not None:
        flat, _ = lax.optimization_barrier((flat, after))
    n_p, n_c = lax.axis_size("patch"), lax.axis_size("col")
    p, c, y = lax.axis_index("patch"), lax.axis_index("col"), lax.axis_index("groups")
    half = out_block // 2
    own_half = lax.dynamic_slice_in_dim(flat, y * half, half, axis=1)
    own_other = lax.dynamic_slice_in_dim(flat, (1 - y) * half, half, axis=1)
    per_core = n_p // n_c
    needs = lambda z, cc, s: cc * per_core <= s < (cc + 1) * per_core
    bufs = {"own": own_half, "own_o": own_other}
    last = {1: own_half, -1: own_half}
    lines = []
    for t in range(1, n_p):
        for d in (1, -1):
            pairs = [((z - d) * n_c + cc, z * n_c + cc)
                     for z in range(n_p) for cc in range(n_c)
                     if 0 <= z - d < n_p and needs(z, cc, z - d * t)]
            if not pairs:
                continue
            got = lax.ppermute(last[d], ("patch", "col"), pairs)
            last[d] = got
            bufs[(t, d)] = got
            lines.append(got)
            trade = [((g * n_p + z) * n_c + cc, ((1 - g) * n_p + z) * n_c + cc)
                     for g in range(2) for z in range(n_p) for cc in range(n_c)
                     if 0 <= z - d < n_p and needs(z, cc, z - d * t)]
            bufs[(t, d, "o")] = lax.ppermute(got, ("groups", "patch", "col"), trade)
    names = sorted(bufs, key=str)
    operands = [bufs[n] for n in names]

    def branch(z, cc, g):
        def run(*ops):
            table = dict(zip(names, ops))
            pieces = []
            for r in range(per_core):
                s = cc * per_core + r
                if s == z:
                    mine, other = table["own"], table["own_o"]
                else:
                    d = 1 if s < z else -1
                    t = abs(z - s)
                    mine, other = table[(t, d)], table[(t, d, "o")]
                pieces += [mine, other] if g == 0 else [other, mine]
            return jnp.concatenate(pieces, axis=1)
        return run

    cases = [branch(z, cc, g) for g in range(2) for z in range(n_p) for cc in range(n_c)]
    index = (y * n_p + p) * n_c + c
    return lax.switch(index, cases, *operands), lines


def full_width(block):
    other = swap(block, "col")
    c = lax.axis_index("col")
    left = jnp.where(c == 0, block, other)
    right = jnp.where(c == 0, other, block)
    return jnp.pad(jnp.concatenate([left, right], axis=2), ((0, 0), (0, 0), (1, 1)))


def conv_full(padded, weight):
    kernel = weight.reshape(3, 3, weight.shape[1], weight.shape[2])
    total = lax.conv_general_dilated(
        padded[None],
        kernel,
        window_strides=(1, 1),
        padding="VALID",
        dimension_numbers=("NCHW", "HWOI", "NCHW"),
        preferred_element_type=jnp.float32,
    )[0]
    return total.astype(jnp.bfloat16)


def reduce_cores(part):
    k, c = lax.axis_index("chan"), lax.axis_index("col")
    width = part.shape[2] // 2
    piece = lambda j: lax.dynamic_slice_in_dim(part, j * width, width, axis=2)
    send_a = piece(jnp.where(k == c, 1 - c, c))
    got_a = lax.ppermute(send_a, ("chan", "col"), [(0, 1), (3, 2), (1, 3), (2, 0)])
    got_b = lax.ppermute(piece(1 - c), ("chan", "col"), [(1, 2), (2, 1)])
    first = jnp.where(k == c, piece(c), got_b)
    return first.astype(jnp.float32) + got_a.astype(jnp.float32)


def fast_path():
    return (
        lax.axis_size("chan") == 2
        and lax.axis_size("col") == 2
        and lax.axis_size("groups") == 2
        and lax.axis_size("patch") % 2 == 0
    )


def time_bias(step_index, temb_weight):
    half_width = temb_weight.shape[0] // 2
    freqs = jnp.exp(-math.log(10000.0) * jnp.arange(half_width).astype(jnp.float32) / half_width)
    angles = step_index[0].astype(jnp.float32) * freqs
    embed = jnp.concatenate([jnp.cos(angles), jnp.sin(angles)])
    gated = jax.nn.silu(embed).astype(jnp.bfloat16)
    return jnp.dot(gated[None, :], temb_weight, preferred_element_type=jnp.float32)[0]


def on_device(
    features,
    cache_codes,
    cache_scale,
    step_index,
    gn1_gain,
    gn1_shift,
    conv1_weight,
    conv1_bias,
    temb_weight,
    gn2_gain,
    gn2_shift,
    conv2_weight,
    conv2_bias,
):
    channels, rows_here, cols_here = features.shape
    patches = lax.axis_size("patch")
    group_count = GROUPS // lax.axis_size("chan")
    cell_total = channels // group_count * rows_here * patches * cols_here * lax.axis_size("col")
    fast = fast_path()
    feat32 = features.astype(jnp.float32)
    mean_one, inv_one = group_moments(feat32, group_count, cell_total)
    if fast:
        weight_one, lines_one = line_weights(conv1_weight)
        weight_two, _ = line_weights(conv2_weight)
    else:
        slots_one, ids_one = fetch_weights(conv1_weight)
        slots_two, ids_two = fetch_weights(conv2_weight)
    own_act = activate(feat32, mean_one, inv_one, gn1_gain, gn1_shift)
    stale = cache_codes.astype(jnp.float32) * cache_scale[None, :, :]
    rim_act = activate(stale, mean_one, inv_one, gn1_gain, gn1_shift)
    where_patch = lax.axis_index("patch")
    upper_rim = rim_act[:, 0:1, :] * (where_patch > 0).astype(jnp.float32)
    lower_rim = rim_act[:, 1:2, :] * (where_patch < patches - 1).astype(jnp.float32)
    block_one = jnp.concatenate([upper_rim, own_act, lower_rim], axis=1).astype(jnp.bfloat16)
    if fast:
        sum_one = reduce_cores(conv_full(full_width(block_one), weight_one))
    else:
        padded_one = extended(block_one, (("col", 2),), 1)
        sum_one = reduce_chan(conv_slots(padded_one, slots_one), ids_one)
    temb_bias = time_bias(step_index, temb_weight)
    hidden = (sum_one + conv1_bias[:, None, None] + temb_bias[:, None, None]).astype(jnp.bfloat16)
    hidden32 = hidden.astype(jnp.float32)
    mean_two, inv_two = group_moments(hidden32, group_count, cell_total)
    act_two = activate(hidden32, mean_two, inv_two, gn2_gain, gn2_shift).astype(jnp.bfloat16)
    if fast:
        rows_two = extended(act_two, (("patch", 1),), 1)
        sum_two = reduce_cores(conv_full(full_width(rows_two), weight_two))
    else:
        padded_two = extended(act_two, (("patch", 1), ("col", 2)), 1)
        sum_two = reduce_chan(conv_slots(padded_two, slots_two), ids_two)
    return (sum_two + conv2_bias[:, None, None] + feat32).astype(jnp.bfloat16)


def solution(mesh):
    return jax.shard_map(
        on_device,
        mesh=mesh,
        in_specs=(
            P("chan", ("groups", "patch"), "col"),
            P("chan", ("groups", "patch"), "col"),
            P(("groups", "patch"), "col"),
            P("groups"),
            P("chan"),
            P("chan"),
            P(None, None, "patch", "chan"),
            P("chan"),
            P(None, "chan"),
            P("chan"),
            P("chan"),
            P(None, None, "patch", "chan"),
            P("chan"),
        ),
        out_specs=P("chan", ("groups", "patch"), "col"),
        check_vma=False,
    )
```

```python
import math

import jax
import jax.numpy as jnp
from jax import lax
from jax.sharding import PartitionSpec as P

GROUPS = 32


norm_epsilon = 1e-05


def extended(value, sides, width):
    for axis, dim in sides:
        count, length = (lax.axis_size(axis), value.shape[dim])
        up = [(i, (i + 1) % count) for i in range(count - 1)]
        down = [(j, i) for i, j in up]
        last = lax.slice_in_dim(value, length - width, length, axis=dim)
        leading = lax.slice_in_dim(value, 0, width, axis=dim)
        before = lax.ppermute(last, axis, up)
        after = lax.ppermute(leading, axis, down)
        value = jnp.concatenate([before, value, after], axis=dim)
    return value


def group_moments(values, group_count, cell_total):
    grouped = values.reshape(group_count, -1)
    local_sums = (jnp.sum(grouped, axis=1), jnp.sum(grouped * grouped, axis=1))
    summed = jnp.stack(local_sums)
    if lax.axis_size("col") == 2:
        summed = summed + swap(summed, "col")
    else:
        summed = lax.psum(summed, "col")
    n_p = lax.axis_size("patch")
    if n_p & (n_p - 1) == 0:
        step = 1
        while step < n_p:
            summed = summed + lax.ppermute(summed, "patch", [(i, i ^ step) for i in range(n_p)])
            step *= 2
    else:
        summed = lax.psum(summed, "patch")
    totals = (summed[0], summed[1])
    group_mean = totals[0] / cell_total
    group_var = totals[1] / cell_total - group_mean * group_mean
    return (group_mean, lax.rsqrt(group_var + norm_epsilon))


def activate(values, group_mean, inv_std, gain_vec, shift_vec):
    channels = values.shape[0]
    width = channels // group_mean.shape[0]
    shape_tail = (channels,) + (1,) * (values.ndim - 1)
    mean_chan = jnp.repeat(group_mean, width).reshape(shape_tail)
    inv_chan = jnp.repeat(inv_std, width).reshape(shape_tail)
    normed = (values - mean_chan) * inv_chan * gain_vec.reshape(shape_tail) + shift_vec.reshape(
        shape_tail
    )
    return jax.nn.silu(normed)


def swap(value, axis):
    return lax.ppermute(value, axis, [(0, 1), (1, 0)])


def fetch_weights(weights):
    taps = weights.shape[0] * weights.shape[1]
    out_block, in_block = weights.shape[2], weights.shape[3]
    flat = weights.reshape(taps, out_block, in_block)
    share_y = lax.axis_size("groups") == 2
    n_y = 2 if share_y else 1
    n_c = lax.axis_size("col")
    y_id = lax.axis_index("groups") if share_y else 0
    c_id = lax.axis_index("col")
    piece = out_block // (n_y * n_c)
    own = y_id * n_c + c_id
    mine = lax.dynamic_slice_in_dim(flat, own * piece, piece, axis=1)
    got = lax.all_gather(mine, "patch", axis=0, tiled=False)
    slots, ids = [got], [own]
    if share_y:
        slots.append(swap(got, "groups"))
        ids.append((1 - y_id) * n_c + c_id)
    if n_c == 2:
        for i in range(len(slots)):
            slots.append(swap(slots[i], "col"))
            ids.append(ids[i] - c_id + (1 - c_id))
    return slots, ids


def conv_slots(padded, slots):
    in_chans, height_pad, width_pad = padded.shape
    height = height_pad - 2
    width = width_pad - 2
    windows = [
        [padded[:, a : a + height, b : b + width] for b in range(3)] for a in range(3)
    ]
    outs = []
    for got in slots:
        total = None
        for a in range(3):
            for b in range(3):
                term = jnp.einsum(
                    "poc,chw->pohw",
                    got[:, a * 3 + b],
                    windows[a][b],
                    preferred_element_type=jnp.float32,
                )
                total = term if total is None else total + term
        outs.append(total.astype(jnp.bfloat16))
    return jnp.stack(outs)


def reduce_chan(parts, ids):
    n_slots, blocks, piece, height, width = parts.shape
    n_k = lax.axis_size("chan")
    k = lax.axis_index("chan")
    per = blocks // n_k
    if n_k == 2:
        mine = lax.dynamic_slice_in_dim(parts, k * per, per, axis=1)
        other = lax.dynamic_slice_in_dim(parts, (1 - k) * per, per, axis=1)
        total = mine.astype(jnp.float32) + swap(other, "chan").astype(jnp.float32)
    else:
        split = parts.reshape(n_slots, n_k, per, piece, height, width)
        split = jnp.moveaxis(split, 1, 0)
        got = lax.all_to_all(split, "chan", 0, 0, tiled=False)
        total = jnp.sum(got.astype(jnp.float32), axis=0)
    where = jnp.zeros((n_slots,), jnp.int32)
    for slot, ident in enumerate(ids):
        where = where.at[ident].set(slot)
    ordered = jnp.take(total, where, axis=0)
    ordered = jnp.moveaxis(ordered, 0, 1)
    return ordered.reshape(per * n_slots * piece, height, width)


def line_weights(weights, after=None):
    taps = weights.shape[0] * weights.shape[1]
    out_block, in_block = weights.shape[2], weights.shape[3]
    flat = weights.reshape(taps, out_block, in_block)
    if after is not None:
        flat, _ = lax.optimization_barrier((flat, after))
    n_p, n_c = lax.axis_size("patch"), lax.axis_size("col")
    p, c, y = lax.axis_index("patch"), lax.axis_index("col"), lax.axis_index("groups")
    half = out_block // 2
    own_half = lax.dynamic_slice_in_dim(flat, y * half, half, axis=1)
    own_other = lax.dynamic_slice_in_dim(flat, (1 - y) * half, half, axis=1)
    per_core = n_p // n_c
    needs = lambda z, cc, s: cc * per_core <= s < (cc + 1) * per_core
    bufs = {"own": own_half, "own_o": own_other}
    last = {1: own_half, -1: own_half}
    lines = []
    for t in range(1, n_p):
        step_got = []
        for d in (1, -1):
            pairs = [((z - d) * n_c + cc, z * n_c + cc)
                     for z in range(n_p) for cc in range(n_c)
                     if 0 <= z - d < n_p and needs(z, cc, z - d * t)]
            if not pairs:
                continue
            got = lax.ppermute(last[d], ("patch", "col"), pairs)
            last[d] = got
            bufs[(t, d)] = got
            lines.append(got)
            step_got.append(got)
            trade = [((g * n_p + z) * n_c + cc, ((1 - g) * n_p + z) * n_c + cc)
                     for g in range(2) for z in range(n_p) for cc in range(n_c)
                     if 0 <= z - d < n_p and needs(z, cc, z - d * t)]
            bufs[(t, d, "o")] = lax.ppermute(got, ("groups", "patch", "col"), trade)
        if step_got:
            yield step_got
    names = sorted(bufs, key=str)
    operands = [bufs[n] for n in names]

    def branch(z, cc, g):
        def run(*ops):
            table = dict(zip(names, ops))
            pieces = []
            for r in range(per_core):
                s = cc * per_core + r
                if s == z:
                    mine, other = table["own"], table["own_o"]
                else:
                    d = 1 if s < z else -1
                    t = abs(z - s)
                    mine, other = table[(t, d)], table[(t, d, "o")]
                pieces += [mine, other] if g == 0 else [other, mine]
            return jnp.concatenate(pieces, axis=1)
        return run

    cases = [branch(z, cc, g) for g in range(2) for z in range(n_p) for cc in range(n_c)]
    index = (y * n_p + p) * n_c + c
    yield lax.switch(index, cases, *operands), lines


def tie(steps, value):
    got = next(steps)
    if isinstance(got, tuple):
        return got, value
    _, value = lax.optimization_barrier((tuple(got), value))
    return None, value


def finish(steps):
    for got in steps:
        if isinstance(got, tuple):
            return got


def full_width(block):
    other = swap(block, "col")
    c = lax.axis_index("col")
    left = jnp.where(c == 0, block, other)
    right = jnp.where(c == 0, other, block)
    return jnp.pad(jnp.concatenate([left, right], axis=2), ((0, 0), (0, 0), (1, 1)))


def conv_full(padded, weight):
    kernel = weight.reshape(3, 3, weight.shape[1], weight.shape[2])
    total = lax.conv_general_dilated(
        padded[None],
        kernel,
        window_strides=(1, 1),
        padding="VALID",
        dimension_numbers=("NCHW", "HWOI", "NCHW"),
        preferred_element_type=jnp.float32,
    )[0]
    return total.astype(jnp.bfloat16)


def reduce_cores(part):
    k, c = lax.axis_index("chan"), lax.axis_index("col")
    width = part.shape[2] // 2
    piece = lambda j: lax.dynamic_slice_in_dim(part, j * width, width, axis=2)
    send_a = piece(jnp.where(k == c, 1 - c, c))
    got_a = lax.ppermute(send_a, ("chan", "col"), [(0, 1), (3, 2), (1, 3), (2, 0)])
    got_b = lax.ppermute(piece(1 - c), ("chan", "col"), [(1, 2), (2, 1)])
    first = jnp.where(k == c, piece(c), got_b)
    return first.astype(jnp.float32) + got_a.astype(jnp.float32)


def fast_path():
    return (
        lax.axis_size("chan") == 2
        and lax.axis_size("col") == 2
        and lax.axis_size("groups") == 2
        and lax.axis_size("patch") % 2 == 0
    )


def time_bias(step_index, temb_weight):
    half_width = temb_weight.shape[0] // 2
    freqs = jnp.exp(-math.log(10000.0) * jnp.arange(half_width).astype(jnp.float32) / half_width)
    angles = step_index[0].astype(jnp.float32) * freqs
    embed = jnp.concatenate([jnp.cos(angles), jnp.sin(angles)])
    gated = jax.nn.silu(embed).astype(jnp.bfloat16)
    return jnp.dot(gated[None, :], temb_weight, preferred_element_type=jnp.float32)[0]


def on_device(
    features,
    cache_codes,
    cache_scale,
    step_index,
    gn1_gain,
    gn1_shift,
    conv1_weight,
    conv1_bias,
    temb_weight,
    gn2_gain,
    gn2_shift,
    conv2_weight,
    conv2_bias,
):
    channels, rows_here, cols_here = features.shape
    patches = lax.axis_size("patch")
    group_count = GROUPS // lax.axis_size("chan")
    cell_total = channels // group_count * rows_here * patches * cols_here * lax.axis_size("col")
    fast = fast_path()
    feat32 = features.astype(jnp.float32)
    mean_one, inv_one = group_moments(feat32, group_count, cell_total)
    if fast:
        weight_one, lines_one = finish(line_weights(conv1_weight))
        steps_two = line_weights(conv2_weight)
    else:
        slots_one, ids_one = fetch_weights(conv1_weight)
        slots_two, ids_two = fetch_weights(conv2_weight)
    own_act = activate(feat32, mean_one, inv_one, gn1_gain, gn1_shift)
    stale = cache_codes.astype(jnp.float32) * cache_scale[None, :, :]
    rim_act = activate(stale, mean_one, inv_one, gn1_gain, gn1_shift)
    where_patch = lax.axis_index("patch")
    upper_rim = rim_act[:, 0:1, :] * (where_patch > 0).astype(jnp.float32)
    lower_rim = rim_act[:, 1:2, :] * (where_patch < patches - 1).astype(jnp.float32)
    block_one = jnp.concatenate([upper_rim, own_act, lower_rim], axis=1).astype(jnp.bfloat16)
    if fast:
        _, block_one = tie(steps_two, block_one)
        part_one = conv_full(full_width(block_one), weight_one)
        _, part_one = tie(steps_two, part_one)
        sum_one = reduce_cores(part_one)
        _, sum_one = tie(steps_two, sum_one)
        weight_two, _ = finish(steps_two)
    else:
        padded_one = extended(block_one, (("col", 2),), 1)
        sum_one = reduce_chan(conv_slots(padded_one, slots_one), ids_one)
    temb_bias = time_bias(step_index, temb_weight)
    hidden = (sum_one + conv1_bias[:, None, None] + temb_bias[:, None, None]).astype(jnp.bfloat16)
    hidden32 = hidden.astype(jnp.float32)
    mean_two, inv_two = group_moments(hidden32, group_count, cell_total)
    act_two = activate(hidden32, mean_two, inv_two, gn2_gain, gn2_shift).astype(jnp.bfloat16)
    if fast:
        rows_two = extended(act_two, (("patch", 1),), 1)
        sum_two = reduce_cores(conv_full(full_width(rows_two), weight_two))
    else:
        padded_two = extended(act_two, (("patch", 1), ("col", 2)), 1)
        sum_two = reduce_chan(conv_slots(padded_two, slots_two), ids_two)
    return (sum_two + conv2_bias[:, None, None] + feat32).astype(jnp.bfloat16)


def solution(mesh):
    return jax.shard_map(
        on_device,
        mesh=mesh,
        in_specs=(
            P("chan", ("groups", "patch"), "col"),
            P("chan", ("groups", "patch"), "col"),
            P(("groups", "patch"), "col"),
            P("groups"),
            P("chan"),
            P("chan"),
            P(None, None, "patch", "chan"),
            P("chan"),
            P(None, "chan"),
            P("chan"),
            P("chan"),
            P(None, None, "patch", "chan"),
            P("chan"),
        ),
        out_specs=P("chan", ("groups", "patch"), "col"),
        check_vma=False,
    )
```

```python
import math

import jax
import jax.numpy as jnp
from jax import lax
from jax.sharding import PartitionSpec as P

GROUPS = 32


norm_epsilon = 1e-05


def extended(value, sides, width):
    for axis, dim in sides:
        count, length = (lax.axis_size(axis), value.shape[dim])
        up = [(i, (i + 1) % count) for i in range(count - 1)]
        down = [(j, i) for i, j in up]
        last = lax.slice_in_dim(value, length - width, length, axis=dim)
        leading = lax.slice_in_dim(value, 0, width, axis=dim)
        before = lax.ppermute(last, axis, up)
        after = lax.ppermute(leading, axis, down)
        value = jnp.concatenate([before, value, after], axis=dim)
    return value


def group_moments(values, group_count, cell_total):
    grouped = values.reshape(group_count, -1)
    local_sums = (jnp.sum(grouped, axis=1), jnp.sum(grouped * grouped, axis=1))
    summed = jnp.stack(local_sums)
    if lax.axis_size("col") == 2:
        summed = summed + swap(summed, "col")
    else:
        summed = lax.psum(summed, "col")
    n_p = lax.axis_size("patch")
    if n_p & (n_p - 1) == 0:
        step = 1
        while step < n_p:
            summed = summed + lax.ppermute(summed, "patch", [(i, i ^ step) for i in range(n_p)])
            step *= 2
    else:
        summed = lax.psum(summed, "patch")
    totals = (summed[0], summed[1])
    group_mean = totals[0] / cell_total
    group_var = totals[1] / cell_total - group_mean * group_mean
    return (group_mean, lax.rsqrt(group_var + norm_epsilon))


def activate(values, group_mean, inv_std, gain_vec, shift_vec):
    channels = values.shape[0]
    width = channels // group_mean.shape[0]
    shape_tail = (channels,) + (1,) * (values.ndim - 1)
    mean_chan = jnp.repeat(group_mean, width).reshape(shape_tail)
    inv_chan = jnp.repeat(inv_std, width).reshape(shape_tail)
    normed = (values - mean_chan) * inv_chan * gain_vec.reshape(shape_tail) + shift_vec.reshape(
        shape_tail
    )
    return jax.nn.silu(normed)


def swap(value, axis):
    return lax.ppermute(value, axis, [(0, 1), (1, 0)])


def fetch_weights(weights):
    taps = weights.shape[0] * weights.shape[1]
    out_block, in_block = weights.shape[2], weights.shape[3]
    flat = weights.reshape(taps, out_block, in_block)
    share_y = lax.axis_size("groups") == 2
    n_y = 2 if share_y else 1
    n_c = lax.axis_size("col")
    y_id = lax.axis_index("groups") if share_y else 0
    c_id = lax.axis_index("col")
    piece = out_block // (n_y * n_c)
    own = y_id * n_c + c_id
    mine = lax.dynamic_slice_in_dim(flat, own * piece, piece, axis=1)
    got = lax.all_gather(mine, "patch", axis=0, tiled=False)
    slots, ids = [got], [own]
    if share_y:
        slots.append(swap(got, "groups"))
        ids.append((1 - y_id) * n_c + c_id)
    if n_c == 2:
        for i in range(len(slots)):
            slots.append(swap(slots[i], "col"))
            ids.append(ids[i] - c_id + (1 - c_id))
    return slots, ids


def conv_slots(padded, slots):
    in_chans, height_pad, width_pad = padded.shape
    height = height_pad - 2
    width = width_pad - 2
    windows = [
        [padded[:, a : a + height, b : b + width] for b in range(3)] for a in range(3)
    ]
    outs = []
    for got in slots:
        total = None
        for a in range(3):
            for b in range(3):
                term = jnp.einsum(
                    "poc,chw->pohw",
                    got[:, a * 3 + b],
                    windows[a][b],
                    preferred_element_type=jnp.float32,
                )
                total = term if total is None else total + term
        outs.append(total.astype(jnp.bfloat16))
    return jnp.stack(outs)


def reduce_chan(parts, ids):
    n_slots, blocks, piece, height, width = parts.shape
    n_k = lax.axis_size("chan")
    k = lax.axis_index("chan")
    per = blocks // n_k
    if n_k == 2:
        mine = lax.dynamic_slice_in_dim(parts, k * per, per, axis=1)
        other = lax.dynamic_slice_in_dim(parts, (1 - k) * per, per, axis=1)
        total = mine.astype(jnp.float32) + swap(other, "chan").astype(jnp.float32)
    else:
        split = parts.reshape(n_slots, n_k, per, piece, height, width)
        split = jnp.moveaxis(split, 1, 0)
        got = lax.all_to_all(split, "chan", 0, 0, tiled=False)
        total = jnp.sum(got.astype(jnp.float32), axis=0)
    where = jnp.zeros((n_slots,), jnp.int32)
    for slot, ident in enumerate(ids):
        where = where.at[ident].set(slot)
    ordered = jnp.take(total, where, axis=0)
    ordered = jnp.moveaxis(ordered, 0, 1)
    return ordered.reshape(per * n_slots * piece, height, width)


def line_weights(weights, after=None):
    taps = weights.shape[0] * weights.shape[1]
    out_block, in_block = weights.shape[2], weights.shape[3]
    flat = weights.reshape(taps, out_block, in_block)
    if after is not None:
        flat, _ = lax.optimization_barrier((flat, after))
    n_p, n_c = lax.axis_size("patch"), lax.axis_size("col")
    p, c, y = lax.axis_index("patch"), lax.axis_index("col"), lax.axis_index("groups")
    half = out_block // 2
    own_half = lax.dynamic_slice_in_dim(flat, y * half, half, axis=1)
    own_other = lax.dynamic_slice_in_dim(flat, (1 - y) * half, half, axis=1)
    per_core = n_p // n_c
    needs = lambda z, cc, s: cc * per_core <= s < (cc + 1) * per_core
    bufs = {"own": own_half, "own_o": own_other}
    last = {1: own_half, -1: own_half}
    lines = []
    for t in range(1, n_p):
        for d in (1, -1):
            pairs = [((z - d) * n_c + cc, z * n_c + cc)
                     for z in range(n_p) for cc in range(n_c)
                     if 0 <= z - d < n_p and needs(z, cc, z - d * t)]
            if not pairs:
                continue
            got = lax.ppermute(last[d], ("patch", "col"), pairs)
            last[d] = got
            bufs[(t, d)] = got
            lines.append(got)
            trade = [((g * n_p + z) * n_c + cc, ((1 - g) * n_p + z) * n_c + cc)
                     for g in range(2) for z in range(n_p) for cc in range(n_c)
                     if 0 <= z - d < n_p and needs(z, cc, z - d * t)]
            bufs[(t, d, "o")] = lax.ppermute(got, ("groups", "patch", "col"), trade)
    names = sorted(bufs, key=str)
    operands = [bufs[n] for n in names]

    def branch(z, cc, g):
        def run(*ops):
            table = dict(zip(names, ops))
            pieces = []
            for r in range(per_core):
                s = cc * per_core + r
                if s == z:
                    mine, other = table["own"], table["own_o"]
                else:
                    d = 1 if s < z else -1
                    t = abs(z - s)
                    mine, other = table[(t, d)], table[(t, d, "o")]
                pieces += [mine, other] if g == 0 else [other, mine]
            return jnp.concatenate(pieces, axis=1)
        return run

    cases = [branch(z, cc, g) for g in range(2) for z in range(n_p) for cc in range(n_c)]
    index = (y * n_p + p) * n_c + c
    return lax.switch(index, cases, *operands), lines


def full_width(block):
    other = swap(block, "col")
    c = lax.axis_index("col")
    left = jnp.where(c == 0, block, other)
    right = jnp.where(c == 0, other, block)
    return jnp.pad(jnp.concatenate([left, right], axis=2), ((0, 0), (0, 0), (1, 1)))


def conv_full(padded, weight):
    kernel = weight.reshape(3, 3, weight.shape[1], weight.shape[2])
    total = lax.conv_general_dilated(
        padded[None],
        kernel,
        window_strides=(1, 1),
        padding="VALID",
        dimension_numbers=("NCHW", "HWOI", "NCHW"),
        preferred_element_type=jnp.float32,
    )[0]
    return total.astype(jnp.bfloat16)


def reduce_cores(part):
    k, c = lax.axis_index("chan"), lax.axis_index("col")
    width = part.shape[2] // 2
    piece = lambda j: lax.dynamic_slice_in_dim(part, j * width, width, axis=2)
    send_a = piece(jnp.where(k == c, 1 - c, c))
    got_a = lax.ppermute(send_a, ("chan", "col"), [(0, 1), (3, 2), (1, 3), (2, 0)])
    got_b = lax.ppermute(piece(1 - c), ("chan", "col"), [(1, 2), (2, 1)])
    first = jnp.where(k == c, piece(c), got_b)
    return first.astype(jnp.float32) + got_a.astype(jnp.float32)


def conv_reduce_split(padded, weight):
    half = weight.shape[1] // 2
    first = reduce_cores(conv_full(padded, weight[:, :half]))
    second = reduce_cores(conv_full(padded, weight[:, half:]))
    return jnp.concatenate([first, second], axis=0)


def fast_path():
    return (
        lax.axis_size("chan") == 2
        and lax.axis_size("col") == 2
        and lax.axis_size("groups") == 2
        and lax.axis_size("patch") % 2 == 0
    )


def time_bias(step_index, temb_weight):
    half_width = temb_weight.shape[0] // 2
    freqs = jnp.exp(-math.log(10000.0) * jnp.arange(half_width).astype(jnp.float32) / half_width)
    angles = step_index[0].astype(jnp.float32) * freqs
    embed = jnp.concatenate([jnp.cos(angles), jnp.sin(angles)])
    gated = jax.nn.silu(embed).astype(jnp.bfloat16)
    return jnp.dot(gated[None, :], temb_weight, preferred_element_type=jnp.float32)[0]


def on_device(
    features,
    cache_codes,
    cache_scale,
    step_index,
    gn1_gain,
    gn1_shift,
    conv1_weight,
    conv1_bias,
    temb_weight,
    gn2_gain,
    gn2_shift,
    conv2_weight,
    conv2_bias,
):
    channels, rows_here, cols_here = features.shape
    patches = lax.axis_size("patch")
    group_count = GROUPS // lax.axis_size("chan")
    cell_total = channels // group_count * rows_here * patches * cols_here * lax.axis_size("col")
    fast = fast_path()
    feat32 = features.astype(jnp.float32)
    mean_one, inv_one = group_moments(feat32, group_count, cell_total)
    if fast:
        weight_one, lines_one = line_weights(conv1_weight)
        weight_two, _ = line_weights(conv2_weight)
    else:
        slots_one, ids_one = fetch_weights(conv1_weight)
        slots_two, ids_two = fetch_weights(conv2_weight)
    own_act = activate(feat32, mean_one, inv_one, gn1_gain, gn1_shift)
    stale = cache_codes.astype(jnp.float32) * cache_scale[None, :, :]
    rim_act = activate(stale, mean_one, inv_one, gn1_gain, gn1_shift)
    where_patch = lax.axis_index("patch")
    upper_rim = rim_act[:, 0:1, :] * (where_patch > 0).astype(jnp.float32)
    lower_rim = rim_act[:, 1:2, :] * (where_patch < patches - 1).astype(jnp.float32)
    block_one = jnp.concatenate([upper_rim, own_act, lower_rim], axis=1).astype(jnp.bfloat16)
    if fast:
        sum_one = conv_reduce_split(full_width(block_one), weight_one)
    else:
        padded_one = extended(block_one, (("col", 2),), 1)
        sum_one = reduce_chan(conv_slots(padded_one, slots_one), ids_one)
    temb_bias = time_bias(step_index, temb_weight)
    hidden = (sum_one + conv1_bias[:, None, None] + temb_bias[:, None, None]).astype(jnp.bfloat16)
    hidden32 = hidden.astype(jnp.float32)
    mean_two, inv_two = group_moments(hidden32, group_count, cell_total)
    act_two = activate(hidden32, mean_two, inv_two, gn2_gain, gn2_shift).astype(jnp.bfloat16)
    if fast:
        rows_two = extended(act_two, (("patch", 1),), 1)
        sum_two = conv_reduce_split(full_width(rows_two), weight_two)
    else:
        padded_two = extended(act_two, (("patch", 1), ("col", 2)), 1)
        sum_two = reduce_chan(conv_slots(padded_two, slots_two), ids_two)
    return (sum_two + conv2_bias[:, None, None] + feat32).astype(jnp.bfloat16)


def solution(mesh):
    return jax.shard_map(
        on_device,
        mesh=mesh,
        in_specs=(
            P("chan", ("groups", "patch"), "col"),
            P("chan", ("groups", "patch"), "col"),
            P(("groups", "patch"), "col"),
            P("groups"),
            P("chan"),
            P("chan"),
            P(None, None, "patch", "chan"),
            P("chan"),
            P(None, "chan"),
            P("chan"),
            P("chan"),
            P(None, None, "patch", "chan"),
            P("chan"),
        ),
        out_specs=P("chan", ("groups", "patch"), "col"),
        check_vma=False,
    )
```

```python
import math

import jax
import jax.numpy as jnp
from jax import lax
from jax.sharding import PartitionSpec as P

GROUPS = 32


norm_epsilon = 1e-05


def extended(value, sides, width):
    for axis, dim in sides:
        count, length = (lax.axis_size(axis), value.shape[dim])
        up = [(i, (i + 1) % count) for i in range(count - 1)]
        down = [(j, i) for i, j in up]
        last = lax.slice_in_dim(value, length - width, length, axis=dim)
        leading = lax.slice_in_dim(value, 0, width, axis=dim)
        before = lax.ppermute(last, axis, up)
        after = lax.ppermute(leading, axis, down)
        value = jnp.concatenate([before, value, after], axis=dim)
    return value


def group_moments(values, group_count, cell_total):
    grouped = values.reshape(group_count, -1)
    local_sums = (jnp.sum(grouped, axis=1), jnp.sum(grouped * grouped, axis=1))
    summed = jnp.stack(local_sums)
    if lax.axis_size("col") == 2:
        summed = summed + swap(summed, "col")
    else:
        summed = lax.psum(summed, "col")
    n_p = lax.axis_size("patch")
    if n_p & (n_p - 1) == 0:
        step = 1
        while step < n_p:
            summed = summed + lax.ppermute(summed, "patch", [(i, i ^ step) for i in range(n_p)])
            step *= 2
    else:
        summed = lax.psum(summed, "patch")
    totals = (summed[0], summed[1])
    group_mean = totals[0] / cell_total
    group_var = totals[1] / cell_total - group_mean * group_mean
    return (group_mean, lax.rsqrt(group_var + norm_epsilon))


def activate(values, group_mean, inv_std, gain_vec, shift_vec):
    channels = values.shape[0]
    width = channels // group_mean.shape[0]
    shape_tail = (channels,) + (1,) * (values.ndim - 1)
    mean_chan = jnp.repeat(group_mean, width).reshape(shape_tail)
    inv_chan = jnp.repeat(inv_std, width).reshape(shape_tail)
    normed = (values - mean_chan) * inv_chan * gain_vec.reshape(shape_tail) + shift_vec.reshape(
        shape_tail
    )
    return jax.nn.silu(normed)


def swap(value, axis):
    return lax.ppermute(value, axis, [(0, 1), (1, 0)])


def fetch_weights(weights):
    taps = weights.shape[0] * weights.shape[1]
    out_block, in_block = weights.shape[2], weights.shape[3]
    flat = weights.reshape(taps, out_block, in_block)
    share_y = lax.axis_size("groups") == 2
    n_y = 2 if share_y else 1
    n_c = lax.axis_size("col")
    y_id = lax.axis_index("groups") if share_y else 0
    c_id = lax.axis_index("col")
    piece = out_block // (n_y * n_c)
    own = y_id * n_c + c_id
    mine = lax.dynamic_slice_in_dim(flat, own * piece, piece, axis=1)
    got = lax.all_gather(mine, "patch", axis=0, tiled=False)
    slots, ids = [got], [own]
    if share_y:
        slots.append(swap(got, "groups"))
        ids.append((1 - y_id) * n_c + c_id)
    if n_c == 2:
        for i in range(len(slots)):
            slots.append(swap(slots[i], "col"))
            ids.append(ids[i] - c_id + (1 - c_id))
    return slots, ids


def conv_slots(padded, slots):
    in_chans, height_pad, width_pad = padded.shape
    height = height_pad - 2
    width = width_pad - 2
    windows = [
        [padded[:, a : a + height, b : b + width] for b in range(3)] for a in range(3)
    ]
    outs = []
    for got in slots:
        total = None
        for a in range(3):
            for b in range(3):
                term = jnp.einsum(
                    "poc,chw->pohw",
                    got[:, a * 3 + b],
                    windows[a][b],
                    preferred_element_type=jnp.float32,
                )
                total = term if total is None else total + term
        outs.append(total.astype(jnp.bfloat16))
    return jnp.stack(outs)


def reduce_chan(parts, ids):
    n_slots, blocks, piece, height, width = parts.shape
    n_k = lax.axis_size("chan")
    k = lax.axis_index("chan")
    per = blocks // n_k
    if n_k == 2:
        mine = lax.dynamic_slice_in_dim(parts, k * per, per, axis=1)
        other = lax.dynamic_slice_in_dim(parts, (1 - k) * per, per, axis=1)
        total = mine.astype(jnp.float32) + swap(other, "chan").astype(jnp.float32)
    else:
        split = parts.reshape(n_slots, n_k, per, piece, height, width)
        split = jnp.moveaxis(split, 1, 0)
        got = lax.all_to_all(split, "chan", 0, 0, tiled=False)
        total = jnp.sum(got.astype(jnp.float32), axis=0)
    where = jnp.zeros((n_slots,), jnp.int32)
    for slot, ident in enumerate(ids):
        where = where.at[ident].set(slot)
    ordered = jnp.take(total, where, axis=0)
    ordered = jnp.moveaxis(ordered, 0, 1)
    return ordered.reshape(per * n_slots * piece, height, width)


def line_weights(weights, after=None):
    taps = weights.shape[0] * weights.shape[1]
    out_block, in_block = weights.shape[2], weights.shape[3]
    flat = weights.reshape(taps, out_block, in_block)
    if after is not None:
        flat, _ = lax.optimization_barrier((flat, after))
    n_p, n_c = lax.axis_size("patch"), lax.axis_size("col")
    p, c, y = lax.axis_index("patch"), lax.axis_index("col"), lax.axis_index("groups")
    half = out_block // 2
    own_half = lax.dynamic_slice_in_dim(flat, y * half, half, axis=1)
    own_other = lax.dynamic_slice_in_dim(flat, (1 - y) * half, half, axis=1)
    per_core = n_p // n_c
    needs = lambda z, cc, s: cc * per_core <= s < (cc + 1) * per_core
    bufs = {"own": own_half, "own_o": own_other}
    last = {1: own_half, -1: own_half}
    lines = []
    for t in range(1, n_p):
        for d in (1, -1):
            pairs = [((z - d) * n_c + cc, z * n_c + cc)
                     for z in range(n_p) for cc in range(n_c)
                     if 0 <= z - d < n_p and needs(z, cc, z - d * t)]
            if not pairs:
                continue
            got = lax.ppermute(last[d], ("patch", "col"), pairs)
            last[d] = got
            bufs[(t, d)] = got
            lines.append(got)
            trade = [((g * n_p + z) * n_c + cc, ((1 - g) * n_p + z) * n_c + cc)
                     for g in range(2) for z in range(n_p) for cc in range(n_c)
                     if 0 <= z - d < n_p and needs(z, cc, z - d * t)]
            bufs[(t, d, "o")] = lax.ppermute(got, ("groups", "patch", "col"), trade)
    names = sorted(bufs, key=str)
    operands = [bufs[n] for n in names]

    def branch(z, cc, g):
        def run(*ops):
            table = dict(zip(names, ops))
            pieces = []
            for r in range(per_core):
                s = cc * per_core + r
                if s == z:
                    mine, other = table["own"], table["own_o"]
                else:
                    d = 1 if s < z else -1
                    t = abs(z - s)
                    mine, other = table[(t, d)], table[(t, d, "o")]
                pieces += [mine, other] if g == 0 else [other, mine]
            return jnp.concatenate(pieces, axis=1)
        return run

    cases = [branch(z, cc, g) for g in range(2) for z in range(n_p) for cc in range(n_c)]
    index = (y * n_p + p) * n_c + c
    return lax.switch(index, cases, *operands), lines


def full_width(block):
    other = swap(block, "col")
    c = lax.axis_index("col")
    left = jnp.where(c == 0, block, other)
    right = jnp.where(c == 0, other, block)
    return jnp.pad(jnp.concatenate([left, right], axis=2), ((0, 0), (0, 0), (1, 1)))


def conv_full(padded, weight):
    kernel = weight.reshape(3, 3, weight.shape[1], weight.shape[2])
    total = lax.conv_general_dilated(
        padded[None],
        kernel,
        window_strides=(1, 1),
        padding="VALID",
        dimension_numbers=("NCHW", "HWOI", "NCHW"),
        preferred_element_type=jnp.float32,
    )[0]
    return total.astype(jnp.bfloat16)


def reduce_cores(part):
    k, c = lax.axis_index("chan"), lax.axis_index("col")
    width = part.shape[2] // 2
    piece = lambda j: lax.dynamic_slice_in_dim(part, j * width, width, axis=2)
    send_a = piece(jnp.where(k == c, 1 - c, c))
    got_a = lax.ppermute(send_a, ("chan", "col"), [(0, 1), (3, 2), (1, 3), (2, 0)])
    got_b = lax.ppermute(piece(1 - c), ("chan", "col"), [(1, 2), (2, 1)])
    first = jnp.where(k == c, piece(c), got_b)
    return first.astype(jnp.float32) + got_a.astype(jnp.float32)


def fast_path():
    return (
        lax.axis_size("chan") == 2
        and lax.axis_size("col") == 2
        and lax.axis_size("groups") == 2
        and lax.axis_size("patch") % 2 == 0
    )


def time_bias(step_index, temb_weight):
    half_width = temb_weight.shape[0] // 2
    freqs = jnp.exp(-math.log(10000.0) * jnp.arange(half_width).astype(jnp.float32) / half_width)
    angles = step_index[0].astype(jnp.float32) * freqs
    embed = jnp.concatenate([jnp.cos(angles), jnp.sin(angles)])
    gated = jax.nn.silu(embed).astype(jnp.bfloat16)
    return jnp.dot(gated[None, :], temb_weight, preferred_element_type=jnp.float32)[0]


def on_device(
    features,
    cache_codes,
    cache_scale,
    step_index,
    gn1_gain,
    gn1_shift,
    conv1_weight,
    conv1_bias,
    temb_weight,
    gn2_gain,
    gn2_shift,
    conv2_weight,
    conv2_bias,
):
    channels, rows_here, cols_here = features.shape
    patches = lax.axis_size("patch")
    group_count = GROUPS // lax.axis_size("chan")
    cell_total = channels // group_count * rows_here * patches * cols_here * lax.axis_size("col")
    fast = fast_path()
    feat32 = features.astype(jnp.float32)
    mean_one, inv_one = group_moments(feat32, group_count, cell_total)
    if fast:
        weight_one, lines_one = line_weights(conv1_weight)
        weight_two, _ = line_weights(conv2_weight, after=lines_one[:2])
    else:
        slots_one, ids_one = fetch_weights(conv1_weight)
        slots_two, ids_two = fetch_weights(conv2_weight)
    own_act = activate(feat32, mean_one, inv_one, gn1_gain, gn1_shift)
    stale = cache_codes.astype(jnp.float32) * cache_scale[None, :, :]
    rim_act = activate(stale, mean_one, inv_one, gn1_gain, gn1_shift)
    where_patch = lax.axis_index("patch")
    upper_rim = rim_act[:, 0:1, :] * (where_patch > 0).astype(jnp.float32)
    lower_rim = rim_act[:, 1:2, :] * (where_patch < patches - 1).astype(jnp.float32)
    block_one = jnp.concatenate([upper_rim, own_act, lower_rim], axis=1).astype(jnp.bfloat16)
    if fast:
        sum_one = reduce_cores(conv_full(full_width(block_one), weight_one))
    else:
        padded_one = extended(block_one, (("col", 2),), 1)
        sum_one = reduce_chan(conv_slots(padded_one, slots_one), ids_one)
    temb_bias = time_bias(step_index, temb_weight)
    hidden = (sum_one + conv1_bias[:, None, None] + temb_bias[:, None, None]).astype(jnp.bfloat16)
    hidden32 = hidden.astype(jnp.float32)
    mean_two, inv_two = group_moments(hidden32, group_count, cell_total)
    act_two = activate(hidden32, mean_two, inv_two, gn2_gain, gn2_shift).astype(jnp.bfloat16)
    if fast:
        rows_two = extended(act_two, (("patch", 1),), 1)
        sum_two = reduce_cores(conv_full(full_width(rows_two), weight_two))
    else:
        padded_two = extended(act_two, (("patch", 1), ("col", 2)), 1)
        sum_two = reduce_chan(conv_slots(padded_two, slots_two), ids_two)
    return (sum_two + conv2_bias[:, None, None] + feat32).astype(jnp.bfloat16)


def solution(mesh):
    return jax.shard_map(
        on_device,
        mesh=mesh,
        in_specs=(
            P("chan", ("groups", "patch"), "col"),
            P("chan", ("groups", "patch"), "col"),
            P(("groups", "patch"), "col"),
            P("groups"),
            P("chan"),
            P("chan"),
            P(None, None, "patch", "chan"),
            P("chan"),
            P(None, "chan"),
            P("chan"),
            P("chan"),
            P(None, None, "patch", "chan"),
            P("chan"),
        ),
        out_specs=P("chan", ("groups", "patch"), "col"),
        check_vma=False,
    )
```

```python
import math

import jax
import jax.numpy as jnp
from jax import lax
from jax.sharding import PartitionSpec as P

GROUPS = 32


norm_epsilon = 1e-05


def extended(value, sides, width):
    for axis, dim in sides:
        count, length = (lax.axis_size(axis), value.shape[dim])
        up = [(i, (i + 1) % count) for i in range(count - 1)]
        down = [(j, i) for i, j in up]
        last = lax.slice_in_dim(value, length - width, length, axis=dim)
        leading = lax.slice_in_dim(value, 0, width, axis=dim)
        before = lax.ppermute(last, axis, up)
        after = lax.ppermute(leading, axis, down)
        value = jnp.concatenate([before, value, after], axis=dim)
    return value


def group_moments(values, group_count, cell_total):
    grouped = values.reshape(group_count, -1)
    local_sums = (jnp.sum(grouped, axis=1), jnp.sum(grouped * grouped, axis=1))
    summed = jnp.stack(local_sums)
    if lax.axis_size("col") == 2:
        summed = summed + swap(summed, "col")
    else:
        summed = lax.psum(summed, "col")
    n_p = lax.axis_size("patch")
    if n_p & (n_p - 1) == 0:
        step = 1
        while step < n_p:
            summed = summed + lax.ppermute(summed, "patch", [(i, i ^ step) for i in range(n_p)])
            step *= 2
    else:
        summed = lax.psum(summed, "patch")
    totals = (summed[0], summed[1])
    group_mean = totals[0] / cell_total
    group_var = totals[1] / cell_total - group_mean * group_mean
    return (group_mean, lax.rsqrt(group_var + norm_epsilon))


def activate(values, group_mean, inv_std, gain_vec, shift_vec):
    channels = values.shape[0]
    width = channels // group_mean.shape[0]
    shape_tail = (channels,) + (1,) * (values.ndim - 1)
    mean_chan = jnp.repeat(group_mean, width).reshape(shape_tail)
    inv_chan = jnp.repeat(inv_std, width).reshape(shape_tail)
    normed = (values - mean_chan) * inv_chan * gain_vec.reshape(shape_tail) + shift_vec.reshape(
        shape_tail
    )
    return jax.nn.silu(normed)


def swap(value, axis):
    return lax.ppermute(value, axis, [(0, 1), (1, 0)])


def fetch_weights(weights):
    taps = weights.shape[0] * weights.shape[1]
    out_block, in_block = weights.shape[2], weights.shape[3]
    flat = weights.reshape(taps, out_block, in_block)
    share_y = lax.axis_size("groups") == 2
    n_y = 2 if share_y else 1
    n_c = lax.axis_size("col")
    y_id = lax.axis_index("groups") if share_y else 0
    c_id = lax.axis_index("col")
    piece = out_block // (n_y * n_c)
    own = y_id * n_c + c_id
    mine = lax.dynamic_slice_in_dim(flat, own * piece, piece, axis=1)
    got = lax.all_gather(mine, "patch", axis=0, tiled=False)
    slots, ids = [got], [own]
    if share_y:
        slots.append(swap(got, "groups"))
        ids.append((1 - y_id) * n_c + c_id)
    if n_c == 2:
        for i in range(len(slots)):
            slots.append(swap(slots[i], "col"))
            ids.append(ids[i] - c_id + (1 - c_id))
    return slots, ids


def conv_slots(padded, slots):
    in_chans, height_pad, width_pad = padded.shape
    height = height_pad - 2
    width = width_pad - 2
    windows = [
        [padded[:, a : a + height, b : b + width] for b in range(3)] for a in range(3)
    ]
    outs = []
    for got in slots:
        total = None
        for a in range(3):
            for b in range(3):
                term = jnp.einsum(
                    "poc,chw->pohw",
                    got[:, a * 3 + b],
                    windows[a][b],
                    preferred_element_type=jnp.float32,
                )
                total = term if total is None else total + term
        outs.append(total.astype(jnp.bfloat16))
    return jnp.stack(outs)


def reduce_chan(parts, ids):
    n_slots, blocks, piece, height, width = parts.shape
    n_k = lax.axis_size("chan")
    k = lax.axis_index("chan")
    per = blocks // n_k
    if n_k == 2:
        mine = lax.dynamic_slice_in_dim(parts, k * per, per, axis=1)
        other = lax.dynamic_slice_in_dim(parts, (1 - k) * per, per, axis=1)
        total = mine.astype(jnp.float32) + swap(other, "chan").astype(jnp.float32)
    else:
        split = parts.reshape(n_slots, n_k, per, piece, height, width)
        split = jnp.moveaxis(split, 1, 0)
        got = lax.all_to_all(split, "chan", 0, 0, tiled=False)
        total = jnp.sum(got.astype(jnp.float32), axis=0)
    where = jnp.zeros((n_slots,), jnp.int32)
    for slot, ident in enumerate(ids):
        where = where.at[ident].set(slot)
    ordered = jnp.take(total, where, axis=0)
    ordered = jnp.moveaxis(ordered, 0, 1)
    return ordered.reshape(per * n_slots * piece, height, width)


def line_weights(weights, after=None):
    taps = weights.shape[0] * weights.shape[1]
    out_block, in_block = weights.shape[2], weights.shape[3]
    flat = weights.reshape(taps, out_block, in_block)
    if after is not None:
        flat, _ = lax.optimization_barrier((flat, after))
    n_p, n_c = lax.axis_size("patch"), lax.axis_size("col")
    p, c, y = lax.axis_index("patch"), lax.axis_index("col"), lax.axis_index("groups")
    half = out_block // 2
    own_half = lax.dynamic_slice_in_dim(flat, y * half, half, axis=1)
    own_other = lax.dynamic_slice_in_dim(flat, (1 - y) * half, half, axis=1)
    per_core = n_p // n_c
    needs = lambda z, cc, s: cc * per_core <= s < (cc + 1) * per_core
    bufs = {"own": own_half, "own_o": own_other}
    last = {1: own_half, -1: own_half}
    lines = []
    for t in range(1, n_p):
        for d in (1, -1):
            pairs = [((z - d) * n_c + cc, z * n_c + cc)
                     for z in range(n_p) for cc in range(n_c)
                     if 0 <= z - d < n_p and needs(z, cc, z - d * t)]
            if not pairs:
                continue
            got = lax.ppermute(last[d], ("patch", "col"), pairs)
            last[d] = got
            bufs[(t, d)] = got
            lines.append(got)
            trade = [((g * n_p + z) * n_c + cc, ((1 - g) * n_p + z) * n_c + cc)
                     for g in range(2) for z in range(n_p) for cc in range(n_c)
                     if 0 <= z - d < n_p and needs(z, cc, z - d * t)]
            bufs[(t, d, "o")] = lax.ppermute(got, ("groups", "patch", "col"), trade)
    names = sorted(bufs, key=str)
    operands = [bufs[n] for n in names]

    def branch(z, cc, g):
        def run(*ops):
            table = dict(zip(names, ops))
            pieces = []
            for r in range(per_core):
                s = cc * per_core + r
                if s == z:
                    mine, other = table["own"], table["own_o"]
                else:
                    d = 1 if s < z else -1
                    t = abs(z - s)
                    mine, other = table[(t, d)], table[(t, d, "o")]
                pieces += [mine, other]
            return jnp.concatenate(pieces, axis=1)
        return run

    cases = [branch(z, cc, 0) for z in range(n_p) for cc in range(n_c)]
    index = p * n_c + c
    return lax.switch(index, cases, *operands), lines


def full_width(block):
    other = swap(block, "col")
    c = lax.axis_index("col")
    left = jnp.where(c == 0, block, other)
    right = jnp.where(c == 0, other, block)
    return jnp.pad(jnp.concatenate([left, right], axis=2), ((0, 0), (0, 0), (1, 1)))


def conv_full(padded, weight):
    kernel = weight.reshape(3, 3, weight.shape[1], weight.shape[2])
    total = lax.conv_general_dilated(
        padded[None],
        kernel,
        window_strides=(1, 1),
        padding="VALID",
        dimension_numbers=("NCHW", "HWOI", "NCHW"),
        preferred_element_type=jnp.float32,
    )[0]
    return total.astype(jnp.bfloat16)


def reduce_cores(part):
    k, c = lax.axis_index("chan"), lax.axis_index("col")
    width = part.shape[2] // 2
    piece = lambda j: lax.dynamic_slice_in_dim(part, j * width, width, axis=2)
    send_a = piece(jnp.where(k == c, 1 - c, c))
    got_a = lax.ppermute(send_a, ("chan", "col"), [(0, 1), (3, 2), (1, 3), (2, 0)])
    got_b = lax.ppermute(piece(1 - c), ("chan", "col"), [(1, 2), (2, 1)])
    first = jnp.where(k == c, piece(c), got_b)
    return first.astype(jnp.float32) + got_a.astype(jnp.float32)


def unswap_halves(total):
    roles = lax.axis_size("patch") // lax.axis_size("col")
    blocks = total.reshape(roles, 2, -1, *total.shape[1:])
    swapped = blocks[:, ::-1]
    y = lax.axis_index("groups")
    return jnp.where(y == 0, blocks, swapped).reshape(total.shape)


def fast_path():
    return (
        lax.axis_size("chan") == 2
        and lax.axis_size("col") == 2
        and lax.axis_size("groups") == 2
        and lax.axis_size("patch") % 2 == 0
    )


def time_bias(step_index, temb_weight):
    half_width = temb_weight.shape[0] // 2
    freqs = jnp.exp(-math.log(10000.0) * jnp.arange(half_width).astype(jnp.float32) / half_width)
    angles = step_index[0].astype(jnp.float32) * freqs
    embed = jnp.concatenate([jnp.cos(angles), jnp.sin(angles)])
    gated = jax.nn.silu(embed).astype(jnp.bfloat16)
    return jnp.dot(gated[None, :], temb_weight, preferred_element_type=jnp.float32)[0]


def on_device(
    features,
    cache_codes,
    cache_scale,
    step_index,
    gn1_gain,
    gn1_shift,
    conv1_weight,
    conv1_bias,
    temb_weight,
    gn2_gain,
    gn2_shift,
    conv2_weight,
    conv2_bias,
):
    channels, rows_here, cols_here = features.shape
    patches = lax.axis_size("patch")
    group_count = GROUPS // lax.axis_size("chan")
    cell_total = channels // group_count * rows_here * patches * cols_here * lax.axis_size("col")
    fast = fast_path()
    feat32 = features.astype(jnp.float32)
    mean_one, inv_one = group_moments(feat32, group_count, cell_total)
    if fast:
        weight_one, lines_one = line_weights(conv1_weight)
        weight_two, _ = line_weights(conv2_weight)
    else:
        slots_one, ids_one = fetch_weights(conv1_weight)
        slots_two, ids_two = fetch_weights(conv2_weight)
    own_act = activate(feat32, mean_one, inv_one, gn1_gain, gn1_shift)
    stale = cache_codes.astype(jnp.float32) * cache_scale[None, :, :]
    rim_act = activate(stale, mean_one, inv_one, gn1_gain, gn1_shift)
    where_patch = lax.axis_index("patch")
    upper_rim = rim_act[:, 0:1, :] * (where_patch > 0).astype(jnp.float32)
    lower_rim = rim_act[:, 1:2, :] * (where_patch < patches - 1).astype(jnp.float32)
    block_one = jnp.concatenate([upper_rim, own_act, lower_rim], axis=1).astype(jnp.bfloat16)
    if fast:
        sum_one = unswap_halves(reduce_cores(conv_full(full_width(block_one), weight_one)))
    else:
        padded_one = extended(block_one, (("col", 2),), 1)
        sum_one = reduce_chan(conv_slots(padded_one, slots_one), ids_one)
    temb_bias = time_bias(step_index, temb_weight)
    hidden = (sum_one + conv1_bias[:, None, None] + temb_bias[:, None, None]).astype(jnp.bfloat16)
    hidden32 = hidden.astype(jnp.float32)
    mean_two, inv_two = group_moments(hidden32, group_count, cell_total)
    act_two = activate(hidden32, mean_two, inv_two, gn2_gain, gn2_shift).astype(jnp.bfloat16)
    if fast:
        rows_two = extended(act_two, (("patch", 1),), 1)
        sum_two = unswap_halves(reduce_cores(conv_full(full_width(rows_two), weight_two)))
    else:
        padded_two = extended(act_two, (("patch", 1), ("col", 2)), 1)
        sum_two = reduce_chan(conv_slots(padded_two, slots_two), ids_two)
    return (sum_two + conv2_bias[:, None, None] + feat32).astype(jnp.bfloat16)


def solution(mesh):
    return jax.shard_map(
        on_device,
        mesh=mesh,
        in_specs=(
            P("chan", ("groups", "patch"), "col"),
            P("chan", ("groups", "patch"), "col"),
            P(("groups", "patch"), "col"),
            P("groups"),
            P("chan"),
            P("chan"),
            P(None, None, "patch", "chan"),
            P("chan"),
            P(None, "chan"),
            P("chan"),
            P("chan"),
            P(None, None, "patch", "chan"),
            P("chan"),
        ),
        out_specs=P("chan", ("groups", "patch"), "col"),
        check_vma=False,
    )
```

```python
import math

import jax
import jax.numpy as jnp
from jax import lax
from jax.sharding import PartitionSpec as P

GROUPS = 32


norm_epsilon = 1e-05


def extended(value, sides, width):
    for axis, dim in sides:
        count, length = (lax.axis_size(axis), value.shape[dim])
        up = [(i, (i + 1) % count) for i in range(count - 1)]
        down = [(j, i) for i, j in up]
        last = lax.slice_in_dim(value, length - width, length, axis=dim)
        leading = lax.slice_in_dim(value, 0, width, axis=dim)
        before = lax.ppermute(last, axis, up)
        after = lax.ppermute(leading, axis, down)
        value = jnp.concatenate([before, value, after], axis=dim)
    return value


def group_moments(values, group_count, cell_total):
    grouped = values.reshape(group_count, -1)
    local_sums = (jnp.sum(grouped, axis=1), jnp.sum(grouped * grouped, axis=1))
    summed = jnp.stack(local_sums)
    if lax.axis_size("col") == 2:
        summed = summed + swap(summed, "col")
    else:
        summed = lax.psum(summed, "col")
    n_p = lax.axis_size("patch")
    if n_p & (n_p - 1) == 0:
        step = 1
        while step < n_p:
            summed = summed + lax.ppermute(summed, "patch", [(i, i ^ step) for i in range(n_p)])
            step *= 2
    else:
        summed = lax.psum(summed, "patch")
    totals = (summed[0], summed[1])
    group_mean = totals[0] / cell_total
    group_var = totals[1] / cell_total - group_mean * group_mean
    return (group_mean, lax.rsqrt(group_var + norm_epsilon))


def activate(values, group_mean, inv_std, gain_vec, shift_vec):
    channels = values.shape[0]
    width = channels // group_mean.shape[0]
    shape_tail = (channels,) + (1,) * (values.ndim - 1)
    mean_chan = jnp.repeat(group_mean, width).reshape(shape_tail)
    inv_chan = jnp.repeat(inv_std, width).reshape(shape_tail)
    normed = (values - mean_chan) * inv_chan * gain_vec.reshape(shape_tail) + shift_vec.reshape(
        shape_tail
    )
    return jax.nn.silu(normed)


def swap(value, axis):
    return lax.ppermute(value, axis, [(0, 1), (1, 0)])


def fetch_weights(weights):
    taps = weights.shape[0] * weights.shape[1]
    out_block, in_block = weights.shape[2], weights.shape[3]
    flat = weights.reshape(taps, out_block, in_block)
    share_y = lax.axis_size("groups") == 2
    n_y = 2 if share_y else 1
    n_c = lax.axis_size("col")
    y_id = lax.axis_index("groups") if share_y else 0
    c_id = lax.axis_index("col")
    piece = out_block // (n_y * n_c)
    own = y_id * n_c + c_id
    mine = lax.dynamic_slice_in_dim(flat, own * piece, piece, axis=1)
    got = lax.all_gather(mine, "patch", axis=0, tiled=False)
    slots, ids = [got], [own]
    if share_y:
        slots.append(swap(got, "groups"))
        ids.append((1 - y_id) * n_c + c_id)
    if n_c == 2:
        for i in range(len(slots)):
            slots.append(swap(slots[i], "col"))
            ids.append(ids[i] - c_id + (1 - c_id))
    return slots, ids


def conv_slots(padded, slots):
    in_chans, height_pad, width_pad = padded.shape
    height = height_pad - 2
    width = width_pad - 2
    windows = [
        [padded[:, a : a + height, b : b + width] for b in range(3)] for a in range(3)
    ]
    outs = []
    for got in slots:
        total = None
        for a in range(3):
            for b in range(3):
                term = jnp.einsum(
                    "poc,chw->pohw",
                    got[:, a * 3 + b],
                    windows[a][b],
                    preferred_element_type=jnp.float32,
                )
                total = term if total is None else total + term
        outs.append(total.astype(jnp.bfloat16))
    return jnp.stack(outs)


def reduce_chan(parts, ids):
    n_slots, blocks, piece, height, width = parts.shape
    n_k = lax.axis_size("chan")
    k = lax.axis_index("chan")
    per = blocks // n_k
    if n_k == 2:
        mine = lax.dynamic_slice_in_dim(parts, k * per, per, axis=1)
        other = lax.dynamic_slice_in_dim(parts, (1 - k) * per, per, axis=1)
        total = mine.astype(jnp.float32) + swap(other, "chan").astype(jnp.float32)
    else:
        split = parts.reshape(n_slots, n_k, per, piece, height, width)
        split = jnp.moveaxis(split, 1, 0)
        got = lax.all_to_all(split, "chan", 0, 0, tiled=False)
        total = jnp.sum(got.astype(jnp.float32), axis=0)
    where = jnp.zeros((n_slots,), jnp.int32)
    for slot, ident in enumerate(ids):
        where = where.at[ident].set(slot)
    ordered = jnp.take(total, where, axis=0)
    ordered = jnp.moveaxis(ordered, 0, 1)
    return ordered.reshape(per * n_slots * piece, height, width)


def line_weights(weights, after=None):
    taps = weights.shape[0] * weights.shape[1]
    out_block, in_block = weights.shape[2], weights.shape[3]
    flat = weights.reshape(taps, out_block, in_block)
    if after is not None:
        flat, _ = lax.optimization_barrier((flat, after))
    n_p, n_c = lax.axis_size("patch"), lax.axis_size("col")
    p, c, y = lax.axis_index("patch"), lax.axis_index("col"), lax.axis_index("groups")
    half = out_block // 2
    own_half = lax.dynamic_slice_in_dim(flat, y * half, half, axis=1)
    own_other = lax.dynamic_slice_in_dim(flat, (1 - y) * half, half, axis=1)
    per_core = n_p // n_c
    needs = lambda z, cc, s: cc * per_core <= s < (cc + 1) * per_core
    bufs = {"own": own_half, "own_o": own_other}
    last = {1: own_half, -1: own_half}
    lines = []
    for t in range(1, n_p):
        for d in (1, -1):
            pairs = [((z - d) * n_c + cc, z * n_c + cc)
                     for z in range(n_p) for cc in range(n_c)
                     if 0 <= z - d < n_p and needs(z, cc, z - d * t)]
            if not pairs:
                continue
            got = lax.ppermute(last[d], ("patch", "col"), pairs)
            last[d] = got
            bufs[(t, d)] = got
            lines.append(got)
            trade = [((g * n_p + z) * n_c + cc, ((1 - g) * n_p + z) * n_c + cc)
                     for g in range(2) for z in range(n_p) for cc in range(n_c)
                     if 0 <= z - d < n_p and needs(z, cc, z - d * t)]
            bufs[(t, d, "o")] = lax.ppermute(got, ("groups", "patch", "col"), trade)
    names = sorted(bufs, key=str)
    operands = [bufs[n] for n in names]

    def branch(z, cc, g):
        def run(*ops):
            table = dict(zip(names, ops))
            pieces = []
            for r in range(per_core):
                s = cc * per_core + r
                if s == z:
                    mine, other = table["own"], table["own_o"]
                else:
                    d = 1 if s < z else -1
                    t = abs(z - s)
                    mine, other = table[(t, d)], table[(t, d, "o")]
                pieces += [mine, other]
            return jnp.concatenate(pieces, axis=1)
        return run

    cases = [branch(z, cc, 0) for z in range(n_p) for cc in range(n_c)]
    index = p * n_c + c
    return lax.switch(index, cases, *operands), lines


def full_width(block):
    other = swap(block, "col")
    c = lax.axis_index("col")
    left = jnp.where(c == 0, block, other)
    right = jnp.where(c == 0, other, block)
    return jnp.pad(jnp.concatenate([left, right], axis=2), ((0, 0), (0, 0), (1, 1)))


def conv_full(padded, weight, unswap=False):
    kernel = weight.reshape(3, 3, weight.shape[1], weight.shape[2])
    total = lax.conv_general_dilated(
        padded[None],
        kernel,
        window_strides=(1, 1),
        padding="VALID",
        dimension_numbers=("NCHW", "HWOI", "NCHW"),
        preferred_element_type=jnp.float32,
    )[0]
    if unswap:
        total = unswap_halves(total)
    return total.astype(jnp.bfloat16)


def reduce_cores(part):
    k, c = lax.axis_index("chan"), lax.axis_index("col")
    width = part.shape[2] // 2
    piece = lambda j: lax.dynamic_slice_in_dim(part, j * width, width, axis=2)
    send_a = piece(jnp.where(k == c, 1 - c, c))
    got_a = lax.ppermute(send_a, ("chan", "col"), [(0, 1), (3, 2), (1, 3), (2, 0)])
    got_b = lax.ppermute(piece(1 - c), ("chan", "col"), [(1, 2), (2, 1)])
    first = jnp.where(k == c, piece(c), got_b)
    return first.astype(jnp.float32) + got_a.astype(jnp.float32)


def unswap_halves(total):
    roles = lax.axis_size("patch") // lax.axis_size("col")
    blocks = total.reshape(roles, 2, -1, *total.shape[1:])
    swapped = blocks[:, ::-1]
    y = lax.axis_index("groups")
    return jnp.where(y == 0, blocks, swapped).reshape(total.shape)


def fast_path():
    return (
        lax.axis_size("chan") == 2
        and lax.axis_size("col") == 2
        and lax.axis_size("groups") == 2
        and lax.axis_size("patch") % 2 == 0
    )


def time_bias(step_index, temb_weight):
    half_width = temb_weight.shape[0] // 2
    freqs = jnp.exp(-math.log(10000.0) * jnp.arange(half_width).astype(jnp.float32) / half_width)
    angles = step_index[0].astype(jnp.float32) * freqs
    embed = jnp.concatenate([jnp.cos(angles), jnp.sin(angles)])
    gated = jax.nn.silu(embed).astype(jnp.bfloat16)
    return jnp.dot(gated[None, :], temb_weight, preferred_element_type=jnp.float32)[0]


def on_device(
    features,
    cache_codes,
    cache_scale,
    step_index,
    gn1_gain,
    gn1_shift,
    conv1_weight,
    conv1_bias,
    temb_weight,
    gn2_gain,
    gn2_shift,
    conv2_weight,
    conv2_bias,
):
    channels, rows_here, cols_here = features.shape
    patches = lax.axis_size("patch")
    group_count = GROUPS // lax.axis_size("chan")
    cell_total = channels // group_count * rows_here * patches * cols_here * lax.axis_size("col")
    fast = fast_path()
    feat32 = features.astype(jnp.float32)
    mean_one, inv_one = group_moments(feat32, group_count, cell_total)
    if fast:
        weight_one, lines_one = line_weights(conv1_weight)
        weight_two, _ = line_weights(conv2_weight)
    else:
        slots_one, ids_one = fetch_weights(conv1_weight)
        slots_two, ids_two = fetch_weights(conv2_weight)
    own_act = activate(feat32, mean_one, inv_one, gn1_gain, gn1_shift)
    stale = cache_codes.astype(jnp.float32) * cache_scale[None, :, :]
    rim_act = activate(stale, mean_one, inv_one, gn1_gain, gn1_shift)
    where_patch = lax.axis_index("patch")
    upper_rim = rim_act[:, 0:1, :] * (where_patch > 0).astype(jnp.float32)
    lower_rim = rim_act[:, 1:2, :] * (where_patch < patches - 1).astype(jnp.float32)
    block_one = jnp.concatenate([upper_rim, own_act, lower_rim], axis=1).astype(jnp.bfloat16)
    if fast:
        sum_one = reduce_cores(conv_full(full_width(block_one), weight_one, unswap=True))
    else:
        padded_one = extended(block_one, (("col", 2),), 1)
        sum_one = reduce_chan(conv_slots(padded_one, slots_one), ids_one)
    temb_bias = time_bias(step_index, temb_weight)
    hidden = (sum_one + conv1_bias[:, None, None] + temb_bias[:, None, None]).astype(jnp.bfloat16)
    hidden32 = hidden.astype(jnp.float32)
    mean_two, inv_two = group_moments(hidden32, group_count, cell_total)
    act_two = activate(hidden32, mean_two, inv_two, gn2_gain, gn2_shift).astype(jnp.bfloat16)
    if fast:
        rows_two = extended(act_two, (("patch", 1),), 1)
        sum_two = reduce_cores(conv_full(full_width(rows_two), weight_two, unswap=True))
    else:
        padded_two = extended(act_two, (("patch", 1), ("col", 2)), 1)
        sum_two = reduce_chan(conv_slots(padded_two, slots_two), ids_two)
    return (sum_two + conv2_bias[:, None, None] + feat32).astype(jnp.bfloat16)


def solution(mesh):
    return jax.shard_map(
        on_device,
        mesh=mesh,
        in_specs=(
            P("chan", ("groups", "patch"), "col"),
            P("chan", ("groups", "patch"), "col"),
            P(("groups", "patch"), "col"),
            P("groups"),
            P("chan"),
            P("chan"),
            P(None, None, "patch", "chan"),
            P("chan"),
            P(None, "chan"),
            P("chan"),
            P("chan"),
            P(None, None, "patch", "chan"),
            P("chan"),
        ),
        out_specs=P("chan", ("groups", "patch"), "col"),
        check_vma=False,
    )
```

```python
import math

import jax
import jax.numpy as jnp
from jax import lax
from jax.sharding import PartitionSpec as P

GROUPS = 32


norm_epsilon = 1e-05


def extended(value, sides, width):
    for axis, dim in sides:
        count, length = (lax.axis_size(axis), value.shape[dim])
        up = [(i, (i + 1) % count) for i in range(count - 1)]
        down = [(j, i) for i, j in up]
        last = lax.slice_in_dim(value, length - width, length, axis=dim)
        leading = lax.slice_in_dim(value, 0, width, axis=dim)
        before = lax.ppermute(last, axis, up)
        after = lax.ppermute(leading, axis, down)
        value = jnp.concatenate([before, value, after], axis=dim)
    return value


def group_moments(values, group_count, cell_total):
    grouped = values.reshape(group_count, -1)
    local_sums = (jnp.sum(grouped, axis=1), jnp.sum(grouped * grouped, axis=1))
    summed = jnp.stack(local_sums)
    if lax.axis_size("col") == 2:
        summed = summed + swap(summed, "col")
    else:
        summed = lax.psum(summed, "col")
    n_p = lax.axis_size("patch")
    if n_p & (n_p - 1) == 0:
        step = 1
        while step < n_p:
            summed = summed + lax.ppermute(summed, "patch", [(i, i ^ step) for i in range(n_p)])
            step *= 2
    else:
        summed = lax.psum(summed, "patch")
    totals = (summed[0], summed[1])
    group_mean = totals[0] / cell_total
    group_var = totals[1] / cell_total - group_mean * group_mean
    return (group_mean, lax.rsqrt(group_var + norm_epsilon))


def activate(values, group_mean, inv_std, gain_vec, shift_vec):
    channels = values.shape[0]
    width = channels // group_mean.shape[0]
    shape_tail = (channels,) + (1,) * (values.ndim - 1)
    mean_chan = jnp.repeat(group_mean, width).reshape(shape_tail)
    inv_chan = jnp.repeat(inv_std, width).reshape(shape_tail)
    normed = (values - mean_chan) * inv_chan * gain_vec.reshape(shape_tail) + shift_vec.reshape(
        shape_tail
    )
    return jax.nn.silu(normed)


def swap(value, axis):
    return lax.ppermute(value, axis, [(0, 1), (1, 0)])


def fetch_weights(weights):
    taps = weights.shape[0] * weights.shape[1]
    out_block, in_block = weights.shape[2], weights.shape[3]
    flat = weights.reshape(taps, out_block, in_block)
    share_y = lax.axis_size("groups") == 2
    n_y = 2 if share_y else 1
    n_c = lax.axis_size("col")
    y_id = lax.axis_index("groups") if share_y else 0
    c_id = lax.axis_index("col")
    piece = out_block // (n_y * n_c)
    own = y_id * n_c + c_id
    mine = lax.dynamic_slice_in_dim(flat, own * piece, piece, axis=1)
    got = lax.all_gather(mine, "patch", axis=0, tiled=False)
    slots, ids = [got], [own]
    if share_y:
        slots.append(swap(got, "groups"))
        ids.append((1 - y_id) * n_c + c_id)
    if n_c == 2:
        for i in range(len(slots)):
            slots.append(swap(slots[i], "col"))
            ids.append(ids[i] - c_id + (1 - c_id))
    return slots, ids


def conv_slots(padded, slots):
    in_chans, height_pad, width_pad = padded.shape
    height = height_pad - 2
    width = width_pad - 2
    windows = [
        [padded[:, a : a + height, b : b + width] for b in range(3)] for a in range(3)
    ]
    outs = []
    for got in slots:
        total = None
        for a in range(3):
            for b in range(3):
                term = jnp.einsum(
                    "poc,chw->pohw",
                    got[:, a * 3 + b],
                    windows[a][b],
                    preferred_element_type=jnp.float32,
                )
                total = term if total is None else total + term
        outs.append(total.astype(jnp.bfloat16))
    return jnp.stack(outs)


def reduce_chan(parts, ids):
    n_slots, blocks, piece, height, width = parts.shape
    n_k = lax.axis_size("chan")
    k = lax.axis_index("chan")
    per = blocks // n_k
    if n_k == 2:
        mine = lax.dynamic_slice_in_dim(parts, k * per, per, axis=1)
        other = lax.dynamic_slice_in_dim(parts, (1 - k) * per, per, axis=1)
        total = mine.astype(jnp.float32) + swap(other, "chan").astype(jnp.float32)
    else:
        split = parts.reshape(n_slots, n_k, per, piece, height, width)
        split = jnp.moveaxis(split, 1, 0)
        got = lax.all_to_all(split, "chan", 0, 0, tiled=False)
        total = jnp.sum(got.astype(jnp.float32), axis=0)
    where = jnp.zeros((n_slots,), jnp.int32)
    for slot, ident in enumerate(ids):
        where = where.at[ident].set(slot)
    ordered = jnp.take(total, where, axis=0)
    ordered = jnp.moveaxis(ordered, 0, 1)
    return ordered.reshape(per * n_slots * piece, height, width)


def line_weights(weights, after=None):
    taps = weights.shape[0] * weights.shape[1]
    out_block, in_block = weights.shape[2], weights.shape[3]
    flat = weights.reshape(taps, out_block, in_block)
    if after is not None:
        flat, _ = lax.optimization_barrier((flat, after))
    n_p, n_c = lax.axis_size("patch"), lax.axis_size("col")
    p, c, y = lax.axis_index("patch"), lax.axis_index("col"), lax.axis_index("groups")
    half = out_block // 2
    own_half = lax.dynamic_slice_in_dim(flat, y * half, half, axis=1)
    own_other = lax.dynamic_slice_in_dim(flat, (1 - y) * half, half, axis=1)
    per_core = n_p // n_c
    needs = lambda z, cc, s: cc * per_core <= s < (cc + 1) * per_core
    bufs = {"own": own_half, "own_o": own_other}
    last = {1: own_half, -1: own_half}
    lines = []
    for t in range(1, n_p):
        for d in (1, -1):
            pairs = [((z - d) * n_c + cc, z * n_c + cc)
                     for z in range(n_p) for cc in range(n_c)
                     if 0 <= z - d < n_p and needs(z, cc, z - d * t)]
            if not pairs:
                continue
            got = lax.ppermute(last[d], ("patch", "col"), pairs)
            last[d] = got
            bufs[(t, d)] = got
            lines.append(got)
            trade = [((g * n_p + z) * n_c + cc, ((1 - g) * n_p + z) * n_c + cc)
                     for g in range(2) for z in range(n_p) for cc in range(n_c)
                     if 0 <= z - d < n_p and needs(z, cc, z - d * t)]
            bufs[(t, d, "o")] = lax.ppermute(got, ("groups", "patch", "col"), trade)
    names = sorted(bufs, key=str)
    operands = [bufs[n] for n in names]

    def branch(z, cc, g):
        def run(*ops):
            table = dict(zip(names, ops))
            pieces = []
            for r in range(per_core):
                s = cc * per_core + r
                if s == z:
                    mine, other = table["own"], table["own_o"]
                else:
                    d = 1 if s < z else -1
                    t = abs(z - s)
                    mine, other = table[(t, d)], table[(t, d, "o")]
                pieces += [mine, other] if g == 0 else [other, mine]
            return jnp.concatenate(pieces, axis=1)
        return run

    cases = [branch(z, cc, g) for g in range(2) for z in range(n_p) for cc in range(n_c)]
    index = (y * n_p + p) * n_c + c
    return lax.switch(index, cases, *operands), lines


def full_width(block):
    other = swap(block, "col")
    c = lax.axis_index("col")
    left = jnp.where(c == 0, block, other)
    right = jnp.where(c == 0, other, block)
    return jnp.concatenate([left, right], axis=2)


def conv_full(padded, weight):
    kernel = weight.reshape(3, 3, weight.shape[1], weight.shape[2])
    total = lax.conv_general_dilated(
        padded[None],
        kernel,
        window_strides=(1, 1),
        padding=((0, 0), (1, 1)),
        dimension_numbers=("NCHW", "HWOI", "NCHW"),
        preferred_element_type=jnp.float32,
    )[0]
    return total.astype(jnp.bfloat16)


def reduce_cores(part):
    k, c = lax.axis_index("chan"), lax.axis_index("col")
    width = part.shape[2] // 2
    piece = lambda j: lax.dynamic_slice_in_dim(part, j * width, width, axis=2)
    send_a = piece(jnp.where(k == c, 1 - c, c))
    got_a = lax.ppermute(send_a, ("chan", "col"), [(0, 1), (3, 2), (1, 3), (2, 0)])
    got_b = lax.ppermute(piece(1 - c), ("chan", "col"), [(1, 2), (2, 1)])
    first = jnp.where(k == c, piece(c), got_b)
    return first.astype(jnp.float32) + got_a.astype(jnp.float32)


def fast_path():
    return (
        lax.axis_size("chan") == 2
        and lax.axis_size("col") == 2
        and lax.axis_size("groups") == 2
        and lax.axis_size("patch") % 2 == 0
    )


def time_bias(step_index, temb_weight):
    half_width = temb_weight.shape[0] // 2
    freqs = jnp.exp(-math.log(10000.0) * jnp.arange(half_width).astype(jnp.float32) / half_width)
    angles = step_index[0].astype(jnp.float32) * freqs
    embed = jnp.concatenate([jnp.cos(angles), jnp.sin(angles)])
    gated = jax.nn.silu(embed).astype(jnp.bfloat16)
    return jnp.dot(gated[None, :], temb_weight, preferred_element_type=jnp.float32)[0]


def on_device(
    features,
    cache_codes,
    cache_scale,
    step_index,
    gn1_gain,
    gn1_shift,
    conv1_weight,
    conv1_bias,
    temb_weight,
    gn2_gain,
    gn2_shift,
    conv2_weight,
    conv2_bias,
):
    channels, rows_here, cols_here = features.shape
    patches = lax.axis_size("patch")
    group_count = GROUPS // lax.axis_size("chan")
    cell_total = channels // group_count * rows_here * patches * cols_here * lax.axis_size("col")
    fast = fast_path()
    feat32 = features.astype(jnp.float32)
    mean_one, inv_one = group_moments(feat32, group_count, cell_total)
    if fast:
        weight_one, lines_one = line_weights(conv1_weight)
        weight_two, _ = line_weights(conv2_weight)
    else:
        slots_one, ids_one = fetch_weights(conv1_weight)
        slots_two, ids_two = fetch_weights(conv2_weight)
    own_act = activate(feat32, mean_one, inv_one, gn1_gain, gn1_shift)
    stale = cache_codes.astype(jnp.float32) * cache_scale[None, :, :]
    rim_act = activate(stale, mean_one, inv_one, gn1_gain, gn1_shift)
    where_patch = lax.axis_index("patch")
    upper_rim = rim_act[:, 0:1, :] * (where_patch > 0).astype(jnp.float32)
    lower_rim = rim_act[:, 1:2, :] * (where_patch < patches - 1).astype(jnp.float32)
    block_one = jnp.concatenate([upper_rim, own_act, lower_rim], axis=1).astype(jnp.bfloat16)
    if fast:
        sum_one = reduce_cores(conv_full(full_width(block_one), weight_one))
    else:
        padded_one = extended(block_one, (("col", 2),), 1)
        sum_one = reduce_chan(conv_slots(padded_one, slots_one), ids_one)
    temb_bias = time_bias(step_index, temb_weight)
    hidden = (sum_one + conv1_bias[:, None, None] + temb_bias[:, None, None]).astype(jnp.bfloat16)
    hidden32 = hidden.astype(jnp.float32)
    mean_two, inv_two = group_moments(hidden32, group_count, cell_total)
    act_two = activate(hidden32, mean_two, inv_two, gn2_gain, gn2_shift).astype(jnp.bfloat16)
    if fast:
        rows_two = extended(act_two, (("patch", 1),), 1)
        sum_two = reduce_cores(conv_full(full_width(rows_two), weight_two))
    else:
        padded_two = extended(act_two, (("patch", 1), ("col", 2)), 1)
        sum_two = reduce_chan(conv_slots(padded_two, slots_two), ids_two)
    return (sum_two + conv2_bias[:, None, None] + feat32).astype(jnp.bfloat16)


def solution(mesh):
    return jax.shard_map(
        on_device,
        mesh=mesh,
        in_specs=(
            P("chan", ("groups", "patch"), "col"),
            P("chan", ("groups", "patch"), "col"),
            P(("groups", "patch"), "col"),
            P("groups"),
            P("chan"),
            P("chan"),
            P(None, None, "patch", "chan"),
            P("chan"),
            P(None, "chan"),
            P("chan"),
            P("chan"),
            P(None, None, "patch", "chan"),
            P("chan"),
        ),
        out_specs=P("chan", ("groups", "patch"), "col"),
        check_vma=False,
    )
```

```python
import math

import jax
import jax.numpy as jnp
from jax import lax
from jax.sharding import PartitionSpec as P

GROUPS = 32


norm_epsilon = 1e-05


def extended(value, sides, width):
    for axis, dim in sides:
        count, length = (lax.axis_size(axis), value.shape[dim])
        up = [(i, (i + 1) % count) for i in range(count - 1)]
        down = [(j, i) for i, j in up]
        last = lax.slice_in_dim(value, length - width, length, axis=dim)
        leading = lax.slice_in_dim(value, 0, width, axis=dim)
        before = lax.ppermute(last, axis, up)
        after = lax.ppermute(leading, axis, down)
        value = jnp.concatenate([before, value, after], axis=dim)
    return value


def group_moments(values, group_count, cell_total):
    grouped = values.reshape(group_count, -1)
    local_sums = (jnp.sum(grouped, axis=1), jnp.sum(grouped * grouped, axis=1))
    summed = jnp.stack(local_sums)
    if lax.axis_size("col") == 2:
        summed = summed + swap(summed, "col")
    else:
        summed = lax.psum(summed, "col")
    n_p = lax.axis_size("patch")
    if n_p & (n_p - 1) == 0:
        step = 1
        while step < n_p:
            summed = summed + lax.ppermute(summed, "patch", [(i, i ^ step) for i in range(n_p)])
            step *= 2
    else:
        summed = lax.psum(summed, "patch")
    totals = (summed[0], summed[1])
    group_mean = totals[0] / cell_total
    group_var = totals[1] / cell_total - group_mean * group_mean
    return (group_mean, lax.rsqrt(group_var + norm_epsilon))


def activate(values, group_mean, inv_std, gain_vec, shift_vec):
    channels = values.shape[0]
    width = channels // group_mean.shape[0]
    shape_tail = (channels,) + (1,) * (values.ndim - 1)
    mean_chan = jnp.repeat(group_mean, width).reshape(shape_tail)
    inv_chan = jnp.repeat(inv_std, width).reshape(shape_tail)
    normed = (values - mean_chan) * inv_chan * gain_vec.reshape(shape_tail) + shift_vec.reshape(
        shape_tail
    )
    return jax.nn.silu(normed)


def swap(value, axis):
    return lax.ppermute(value, axis, [(0, 1), (1, 0)])


def fetch_weights(weights):
    taps = weights.shape[0] * weights.shape[1]
    out_block, in_block = weights.shape[2], weights.shape[3]
    flat = weights.reshape(taps, out_block, in_block)
    share_y = lax.axis_size("groups") == 2
    n_y = 2 if share_y else 1
    n_c = lax.axis_size("col")
    y_id = lax.axis_index("groups") if share_y else 0
    c_id = lax.axis_index("col")
    piece = out_block // (n_y * n_c)
    own = y_id * n_c + c_id
    mine = lax.dynamic_slice_in_dim(flat, own * piece, piece, axis=1)
    got = lax.all_gather(mine, "patch", axis=0, tiled=False)
    slots, ids = [got], [own]
    if share_y:
        slots.append(swap(got, "groups"))
        ids.append((1 - y_id) * n_c + c_id)
    if n_c == 2:
        for i in range(len(slots)):
            slots.append(swap(slots[i], "col"))
            ids.append(ids[i] - c_id + (1 - c_id))
    return slots, ids


def conv_slots(padded, slots):
    in_chans, height_pad, width_pad = padded.shape
    height = height_pad - 2
    width = width_pad - 2
    windows = [
        [padded[:, a : a + height, b : b + width] for b in range(3)] for a in range(3)
    ]
    outs = []
    for got in slots:
        total = None
        for a in range(3):
            for b in range(3):
                term = jnp.einsum(
                    "poc,chw->pohw",
                    got[:, a * 3 + b],
                    windows[a][b],
                    preferred_element_type=jnp.float32,
                )
                total = term if total is None else total + term
        outs.append(total.astype(jnp.bfloat16))
    return jnp.stack(outs)


def reduce_chan(parts, ids):
    n_slots, blocks, piece, height, width = parts.shape
    n_k = lax.axis_size("chan")
    k = lax.axis_index("chan")
    per = blocks // n_k
    if n_k == 2:
        mine = lax.dynamic_slice_in_dim(parts, k * per, per, axis=1)
        other = lax.dynamic_slice_in_dim(parts, (1 - k) * per, per, axis=1)
        total = mine.astype(jnp.float32) + swap(other, "chan").astype(jnp.float32)
    else:
        split = parts.reshape(n_slots, n_k, per, piece, height, width)
        split = jnp.moveaxis(split, 1, 0)
        got = lax.all_to_all(split, "chan", 0, 0, tiled=False)
        total = jnp.sum(got.astype(jnp.float32), axis=0)
    where = jnp.zeros((n_slots,), jnp.int32)
    for slot, ident in enumerate(ids):
        where = where.at[ident].set(slot)
    ordered = jnp.take(total, where, axis=0)
    ordered = jnp.moveaxis(ordered, 0, 1)
    return ordered.reshape(per * n_slots * piece, height, width)


def line_weights(weights, after=None):
    taps = weights.shape[0] * weights.shape[1]
    out_block, in_block = weights.shape[2], weights.shape[3]
    flat = weights.reshape(taps, out_block, in_block)
    if after is not None:
        flat, _ = lax.optimization_barrier((flat, after))
    n_p, n_c = lax.axis_size("patch"), lax.axis_size("col")
    p, c, y = lax.axis_index("patch"), lax.axis_index("col"), lax.axis_index("groups")
    half = out_block // 2
    own_half = lax.dynamic_slice_in_dim(flat, y * half, half, axis=1)
    own_other = lax.dynamic_slice_in_dim(flat, (1 - y) * half, half, axis=1)
    per_core = n_p // n_c
    needs = lambda z, cc, s: cc * per_core <= s < (cc + 1) * per_core
    bufs = {"own": own_half, "own_o": own_other}
    last = {1: own_half, -1: own_half}
    lines = []
    for t in range(1, n_p):
        for d in (1, -1):
            pairs = [((z - d) * n_c + cc, z * n_c + cc)
                     for z in range(n_p) for cc in range(n_c)
                     if 0 <= z - d < n_p and needs(z, cc, z - d * t)]
            if not pairs:
                continue
            got = lax.ppermute(last[d], ("patch", "col"), pairs)
            last[d] = got
            bufs[(t, d)] = got
            lines.append(got)
            trade = [((g * n_p + z) * n_c + cc, ((1 - g) * n_p + z) * n_c + cc)
                     for g in range(2) for z in range(n_p) for cc in range(n_c)
                     if 0 <= z - d < n_p and needs(z, cc, z - d * t)]
            bufs[(t, d, "o")] = lax.ppermute(got, ("groups", "patch", "col"), trade)
    names = sorted(bufs, key=str)
    operands = [bufs[n] for n in names]

    def branch(z, cc, g):
        def run(*ops):
            table = dict(zip(names, ops))
            pieces = []
            for r in range(per_core):
                s = cc * per_core + r
                if s == z:
                    mine, other = table["own"], table["own_o"]
                else:
                    d = 1 if s < z else -1
                    t = abs(z - s)
                    mine, other = table[(t, d)], table[(t, d, "o")]
                pieces += [mine, other] if g == 0 else [other, mine]
            return jnp.concatenate(pieces, axis=1)
        return run

    cases = [branch(z, cc, g) for g in range(2) for z in range(n_p) for cc in range(n_c)]
    index = (y * n_p + p) * n_c + c
    return lax.switch(index, cases, *operands), lines


def full_width(block):
    other = swap(block, "col")
    c = lax.axis_index("col")
    pair = jnp.stack([block, other])
    left = lax.dynamic_index_in_dim(pair, c, axis=0, keepdims=False)
    right = lax.dynamic_index_in_dim(pair, 1 - c, axis=0, keepdims=False)
    return jnp.concatenate([left, right], axis=2)


def conv_full(padded, weight):
    kernel = weight.reshape(3, 3, weight.shape[1], weight.shape[2])
    total = lax.conv_general_dilated(
        padded[None],
        kernel,
        window_strides=(1, 1),
        padding=((0, 0), (1, 1)),
        dimension_numbers=("NCHW", "HWOI", "NCHW"),
        preferred_element_type=jnp.float32,
    )[0]
    return total.astype(jnp.bfloat16)


def reduce_cores(part):
    k, c = lax.axis_index("chan"), lax.axis_index("col")
    width = part.shape[2] // 2
    piece = lambda j: lax.dynamic_slice_in_dim(part, j * width, width, axis=2)
    send_a = piece(jnp.where(k == c, 1 - c, c))
    got_a = lax.ppermute(send_a, ("chan", "col"), [(0, 1), (3, 2), (1, 3), (2, 0)])
    got_b = lax.ppermute(piece(1 - c), ("chan", "col"), [(1, 2), (2, 1)])
    first = jnp.where(k == c, piece(c), got_b)
    return first.astype(jnp.float32) + got_a.astype(jnp.float32)


def fast_path():
    return (
        lax.axis_size("chan") == 2
        and lax.axis_size("col") == 2
        and lax.axis_size("groups") == 2
        and lax.axis_size("patch") % 2 == 0
    )


def time_bias(step_index, temb_weight):
    half_width = temb_weight.shape[0] // 2
    freqs = jnp.exp(-math.log(10000.0) * jnp.arange(half_width).astype(jnp.float32) / half_width)
    angles = step_index[0].astype(jnp.float32) * freqs
    embed = jnp.concatenate([jnp.cos(angles), jnp.sin(angles)])
    gated = jax.nn.silu(embed).astype(jnp.bfloat16)
    return jnp.dot(gated[None, :], temb_weight, preferred_element_type=jnp.float32)[0]


def on_device(
    features,
    cache_codes,
    cache_scale,
    step_index,
    gn1_gain,
    gn1_shift,
    conv1_weight,
    conv1_bias,
    temb_weight,
    gn2_gain,
    gn2_shift,
    conv2_weight,
    conv2_bias,
):
    channels, rows_here, cols_here = features.shape
    patches = lax.axis_size("patch")
    group_count = GROUPS // lax.axis_size("chan")
    cell_total = channels // group_count * rows_here * patches * cols_here * lax.axis_size("col")
    fast = fast_path()
    feat32 = features.astype(jnp.float32)
    mean_one, inv_one = group_moments(feat32, group_count, cell_total)
    if fast:
        weight_one, lines_one = line_weights(conv1_weight)
        weight_two, _ = line_weights(conv2_weight)
    else:
        slots_one, ids_one = fetch_weights(conv1_weight)
        slots_two, ids_two = fetch_weights(conv2_weight)
    own_act = activate(feat32, mean_one, inv_one, gn1_gain, gn1_shift)
    stale = cache_codes.astype(jnp.float32) * cache_scale[None, :, :]
    rim_act = activate(stale, mean_one, inv_one, gn1_gain, gn1_shift)
    where_patch = lax.axis_index("patch")
    upper_rim = rim_act[:, 0:1, :] * (where_patch > 0).astype(jnp.float32)
    lower_rim = rim_act[:, 1:2, :] * (where_patch < patches - 1).astype(jnp.float32)
    block_one = jnp.concatenate([upper_rim, own_act, lower_rim], axis=1).astype(jnp.bfloat16)
    if fast:
        sum_one = reduce_cores(conv_full(full_width(block_one), weight_one))
    else:
        padded_one = extended(block_one, (("col", 2),), 1)
        sum_one = reduce_chan(conv_slots(padded_one, slots_one), ids_one)
    temb_bias = time_bias(step_index, temb_weight)
    hidden = (sum_one + conv1_bias[:, None, None] + temb_bias[:, None, None]).astype(jnp.bfloat16)
    hidden32 = hidden.astype(jnp.float32)
    mean_two, inv_two = group_moments(hidden32, group_count, cell_total)
    act_two = activate(hidden32, mean_two, inv_two, gn2_gain, gn2_shift).astype(jnp.bfloat16)
    if fast:
        rows_two = extended(act_two, (("patch", 1),), 1)
        sum_two = reduce_cores(conv_full(full_width(rows_two), weight_two))
    else:
        padded_two = extended(act_two, (("patch", 1), ("col", 2)), 1)
        sum_two = reduce_chan(conv_slots(padded_two, slots_two), ids_two)
    return (sum_two + conv2_bias[:, None, None] + feat32).astype(jnp.bfloat16)


def solution(mesh):
    return jax.shard_map(
        on_device,
        mesh=mesh,
        in_specs=(
            P("chan", ("groups", "patch"), "col"),
            P("chan", ("groups", "patch"), "col"),
            P(("groups", "patch"), "col"),
            P("groups"),
            P("chan"),
            P("chan"),
            P(None, None, "patch", "chan"),
            P("chan"),
            P(None, "chan"),
            P("chan"),
            P("chan"),
            P(None, None, "patch", "chan"),
            P("chan"),
        ),
        out_specs=P("chan", ("groups", "patch"), "col"),
        check_vma=False,
    )
```
